32 devices in a mesh: slab: 4 (over y, x), gx: 8 (over z, core).
Axes of the slice: x: 2, y: 2, z: 4, core: 2. Of those that a mesh axis runs over, the one named last changes fastest.
Arguments:
- wavefield: bfloat16 [4, 2, 2048, 2048], P('slab', None, 'gx'), may hold values from -6 to 6
- boundary: bfloat16 [4, 2, 2048, 2048], P('slab', None, 'gx'), may hold values from -6 to 6
- source: bfloat16 [4, 2, 2048, 2048], P('slab', None, 'gx'), may hold values from -6 to 6
- slowness: float32 [4, 2048, 2048], P('slab', 'gx'), may hold values from 0.6 to 1.4
- reflectivity: float32 [4, 2048, 2048], P('slab', 'gx'), may hold values from -0.6 to 0.6
- ref_slowness: float32 [4], P('slab'), may hold values from 0.8 to 1.2
Outputs:
- extrapolated: bfloat16 [4, 2, 2048, 2048], P('slab', None, 'gx')
- image: float32 [4, 2048, 2048], P('slab', 'gx')
The draws below stay inside these ranges and needn't reach their ends.
All inputs are finite; a program needn't handle non-finite values.
Results may differ from the reference program's by a relative error of at most 0.001.
Values may be sent and summed in bfloat16 or wider, within the bound.
No kernel may reach another device: no remote copies, remote signals or barrier semaphores. Data moves between devices by JAX's collectives and lax.ppermute only.
A program may use at most 64 MiB of HBM per device.

```python
import math
import jax
import jax.numpy as jnp
from jax import lax

NX = 2048
NY = 2048
SLABS = 4


def level_of(stream_key, shape, pieces, least, top_value):
    gain = 1.0
    for dim, parts in pieces:
        draws = jax.random.uniform(jax.random.fold_in(jax.random.fold_in(stream_key, 6), dim), (parts,), jnp.float32, least / len(pieces), top_value / len(pieces))
        gain = gain * jnp.repeat(jnp.exp(draws), shape[dim] // parts).reshape((-1,) + (1,) * (len(shape) - 1 - dim))
    return gain


def scatter_about(rng, dims, spread, reach, split=(), kind=jnp.bfloat16):
    gain = level_of(rng, dims, split, -0.22, 0.18) if split else 1.0
    values = jax.random.normal(rng, dims, jnp.float32) * spread * gain
    return jnp.minimum(jnp.maximum(values, -reach), reach).astype(kind)


def setup_inputs(seed: int = 0) -> dict:
    seeds = jax.random.split(jax.random.key(seed), 7)
    return {
        "wavefield": scatter_about(seeds[0], (SLABS, 2, NX, NY), 1.0, 6.0, ((0, 4), (2, 8))),
        "boundary": scatter_about(seeds[1], (SLABS, 2, NX, NY), 1.0, 6.0, ((0, 4), (2, 8))),
        "source": scatter_about(seeds[2], (SLABS, 2, NX, NY), 1.0, 6.0, ((0, 4), (2, 8))),
        "slowness": jnp.clip(0.6 + 0.79999995 * jax.random.uniform(seeds[3], (SLABS, NX, NY), jnp.float32) ** level_of(seeds[3], (SLABS, NX, NY), ((0, 4), (1, 8)), -0.2, 0.2), 0.6, 1.4),
        "reflectivity": scatter_about(seeds[4], (SLABS, NX, NY), 0.12, 0.6, ((0, 4), (1, 8)), jnp.float32),
        "ref_slowness": jnp.clip(0.8 + 0.40000004 * jax.random.uniform(seeds[5], (SLABS,), jnp.float32) ** level_of(seeds[5], (SLABS,), ((0, 4),), -0.2, 0.2), 0.8, 1.2),
    }


OMEGA = 2.5
DEPTH_STEP = 1.0

def angular(length):
    position = jnp.arange(length, dtype=jnp.int32)
    signed = jnp.where(position < length // 2, position, position - length)
    return signed.astype(jnp.float32) * (2.0 * math.pi / length)

def propagator(freq_row, freq_col, base):
    kz_square = (OMEGA * base) ** 2 - freq_row * freq_row - freq_col * freq_col
    root = jnp.sqrt(jnp.abs(kz_square))
    upward = kz_square >= 0.0
    real_part = jnp.where(upward, jnp.cos(root * DEPTH_STEP), jnp.exp(-root * DEPTH_STEP))
    imag_part = jnp.where(upward, -jnp.sin(root * DEPTH_STEP), jnp.zeros_like(root))
    return (real_part, imag_part)

def one_slab(operands):
    wave, handed, src, slow, refl, base = operands
    wave = wave.astype(jnp.float32)
    handed = handed.astype(jnp.float32)
    src = src.astype(jnp.float32)
    real_in = wave[0] + handed[0] + OMEGA * OMEGA * refl * src[0]
    imag_in = wave[1] + handed[1] + OMEGA * OMEGA * refl * src[1]
    angle = -OMEGA * (slow - base) * DEPTH_STEP
    cosine = jnp.cos(angle)
    sine = jnp.sin(angle)
    lensed_real = real_in * cosine - imag_in * sine
    lensed_imag = real_in * sine + imag_in * cosine
    spectrum = jnp.fft.fft2(lax.complex(lensed_real, lensed_imag))
    prop_real, prop_imag = propagator(angular(NX)[:, None], angular(NY)[None, :], base)
    spectrum = spectrum * lax.complex(prop_real, prop_imag)
    field = jnp.fft.ifft2(spectrum)
    out_real = jnp.real(field)
    out_imag = jnp.imag(field)
    image = src[0] * out_real + src[1] * out_imag
    return (jnp.stack([out_real, out_imag]).astype(jnp.bfloat16), image)

def reference(wavefield, boundary, source, slowness, reflectivity, ref_slowness):
    handed = jnp.concatenate([boundary[1:], jnp.zeros_like(boundary[:1])], axis=0)
    extrapolated, image = lax.map(one_slab, (wavefield, handed, source, slowness, reflectivity, ref_slowness))
    return (extrapolated, image)
```

```python
from functools import partial
import math

import jax
import jax.numpy as jnp
from jax import lax
from jax.sharding import PartitionSpec as P
from jax.experimental import pallas as pl
from jax.experimental.pallas import tpu as pltpu

OMEGA = 2.5
DEPTH_STEP = 1.0
precise = lax.Precision.HIGHEST


def shifted(block, axis, distance):
    devices = range(lax.axis_size(axis))
    route = [(i - distance, i) for i in devices if i - distance in devices]
    return lax.ppermute(block, axis, route)


def factor_pair(length):
    outer = math.gcd(length, 16)
    return (outer, length // outer)


def dft_table(length, orient):
    position = jnp.arange(length, dtype=jnp.int32)
    product = position[:, None] * position[None, :] % length
    angle = orient * 2.0 * math.pi * product.astype(jnp.float32) / length
    return (jnp.cos(angle), jnp.sin(angle))


def twiddle_table(first, second, length, orient):
    product = (
        jnp.arange(first, dtype=jnp.int32)[:, None]
        * jnp.arange(second, dtype=jnp.int32)[None, :]
        % length
    )
    angle = orient * 2.0 * math.pi * product.astype(jnp.float32) / length
    return (jnp.cos(angle), jnp.sin(angle))


def complex_einsum(form, table, field):
    mixing = partial(jnp.einsum, form, precision=precise)
    return (
        mixing(table[0], field[0]) - mixing(table[1], field[1]),
        mixing(table[0], field[1]) + mixing(table[1], field[0]),
    )


def times_complex(field, factor):
    return (
        field[0] * factor[0] - field[1] * factor[1],
        field[0] * factor[1] + field[1] * factor[0],
    )


def columns_forward(field):
    count, length = field[0].shape
    outer, inner = factor_pair(length)
    shaped = tuple((part.reshape(count, outer, inner) for part in field))
    section = complex_einsum("ka,rab->rkb", dft_table(outer, -1.0), shaped)
    section = times_complex(section, twiddle_table(outer, inner, length, -1.0))
    section = complex_einsum("mb,rkb->rkm", dft_table(inner, -1.0), section)
    return tuple((part.reshape(count, length) for part in section))


def columns_inverse(field):
    count, length = field[0].shape
    outer, inner = factor_pair(length)
    shaped = tuple((part.reshape(count, outer, inner) for part in field))
    section = complex_einsum("mb,rkm->rkb", dft_table(inner, 1.0), shaped)
    section = times_complex(section, twiddle_table(outer, inner, length, 1.0))
    section = complex_einsum("ka,rkb->rab", dft_table(outer, 1.0), section)
    return tuple((part.reshape(count, length) for part in section))


def rows_forward(field):
    length, count = field[0].shape
    outer, inner = factor_pair(length)
    shaped = tuple((part.reshape(outer, inner, count) for part in field))
    section = complex_einsum("ka,abc->kbc", dft_table(outer, -1.0), shaped)
    turned = twiddle_table(outer, inner, length, -1.0)
    section = times_complex(section, (turned[0][:, :, None], turned[1][:, :, None]))
    section = complex_einsum("mb,kbc->kmc", dft_table(inner, -1.0), section)
    return tuple((part.reshape(length, count) for part in section))


def rows_inverse(field):
    length, count = field[0].shape
    outer, inner = factor_pair(length)
    shaped = tuple((part.reshape(outer, inner, count) for part in field))
    section = complex_einsum("mb,kmc->kbc", dft_table(inner, 1.0), shaped)
    turned = twiddle_table(outer, inner, length, 1.0)
    section = times_complex(section, (turned[0][:, :, None], turned[1][:, :, None]))
    section = complex_einsum("ka,kbc->abc", dft_table(outer, 1.0), section)
    return tuple((part.reshape(length, count) for part in section))


def rotate(part, step, count):
    step %= count
    if step == 0:
        return part
    if 4 * step == count:
        return (-part[1], part[0])
    if 2 * step == count:
        return (-part[0], -part[1])
    if 4 * step == 3 * count:
        return (part[1], -part[0])
    cosine = math.cos(2.0 * math.pi * step / count)
    sine = math.sin(2.0 * math.pi * step / count)
    return (part[0] * cosine - part[1] * sine, part[0] * sine + part[1] * cosine)


def fft_slabs(parts, orient):
    count = len(parts)
    if count == 1:
        return list(parts)
    even = fft_slabs(parts[0::2], orient)
    odd = fft_slabs(parts[1::2], orient)
    half = count // 2
    out = [None] * count
    for k in range(half):
        turned = rotate(odd[k], orient * k, count)
        out[k] = (even[k][0] + turned[0], even[k][1] + turned[1])
        out[k + half] = (even[k][0] - turned[0], even[k][1] - turned[1])
    return out


def stacked_matmul(stacked, real, imag):
    size = real.shape[1]
    rows = stacked.shape[0] // 2
    both = jnp.concatenate([real, imag], axis=1)
    prod = jnp.dot(stacked, both, precision=lax.Precision.HIGH, preferred_element_type=jnp.float32)
    return (
        prod[:rows, :size] - prod[rows:, size:],
        prod[:rows, size:] + prod[rows:, :size],
    )


def rows_kernel(x_ref, p_ref, w_ref, tw_ref, o_ref):
    outer = tw_ref.shape[1]
    inner = tw_ref.shape[2]
    slabs = [
        (x_ref[0, a * inner:(a + 1) * inner, :], x_ref[1, a * inner:(a + 1) * inner, :])
        for a in range(outer)
    ]
    spec = fft_slabs(slabs, -1)
    wr = w_ref[0]
    wi = w_ref[1]
    forward = jnp.concatenate([wr, wi], axis=0)
    backward = jnp.concatenate([wr, -wi], axis=0)
    outs = []
    for k in range(outer):
        zr, zi = spec[k]
        tr = tw_ref[0, k]
        ti = tw_ref[1, k]
        zr, zi = zr * tr - zi * ti, zr * ti + zi * tr
        yr, yi = stacked_matmul(forward, zr, zi)
        pr = p_ref[0, k * inner:(k + 1) * inner, :]
        pi = p_ref[1, k * inner:(k + 1) * inner, :]
        yr, yi = yr * pr - yi * pi, yr * pi + yi * pr
        sr, si = stacked_matmul(backward, yr, yi)
        outs.append((sr * tr + si * ti, si * tr - sr * ti))
    res = fft_slabs(outs, 1)
    for a in range(outer):
        o_ref[0, a * inner:(a + 1) * inner, :] = res[a][0]
        o_ref[1, a * inner:(a + 1) * inner, :] = res[a][1]


def rows_shift(turned, factor):
    _, length, width = turned.shape
    outer, inner = factor_pair(length)
    block = min(width, 128)
    table = dft_table(inner, -1.0)
    turn = twiddle_table(outer, inner, length, -1.0)
    table = jnp.stack(table)
    turn = jnp.stack(turn)[..., None]
    field_spec = pl.BlockSpec((2, length, block), lambda j: (0, 0, j))
    return pl.pallas_call(
        rows_kernel,
        grid=(width // block,),
        in_specs=[
            field_spec,
            field_spec,
            pl.BlockSpec((2, inner, inner), lambda j: (0, 0, 0)),
            pl.BlockSpec((2, outer, inner, 1), lambda j: (0, 0, 0, 0)),
        ],
        out_specs=field_spec,
        out_shape=jax.ShapeDtypeStruct(turned.shape, jnp.float32),
    )(turned, factor, table, turn)


def signed_freq(index, length):
    signed = jnp.where(index < length // 2, index, index - length)
    return signed.astype(jnp.float32) * (2.0 * math.pi / length)


def permuted_freq(position, length):
    outer, inner = factor_pair(length)
    index = position // inner + outer * (position % inner)
    return signed_freq(index, length)


def propagator(freq_row, freq_col, base, scale):
    kz_square = (OMEGA * base) ** 2 - freq_row * freq_row - freq_col * freq_col
    root = jnp.sqrt(jnp.abs(kz_square))
    upward = kz_square >= 0.0
    real_part = jnp.where(upward, jnp.cos(root * DEPTH_STEP), jnp.exp(-root * DEPTH_STEP))
    imag_part = jnp.where(upward, -jnp.sin(root * DEPTH_STEP), jnp.zeros_like(root))
    return (real_part * scale, imag_part * scale)


def body(wavefield, boundary, source, slowness, reflectivity, ref_slowness):
    handed = shifted(boundary, "slab", -1)
    wave = wavefield[0].astype(jnp.float32)
    handed_field = handed[0].astype(jnp.float32)
    source_field = source[0].astype(jnp.float32)
    slow = slowness[0]
    refl = reflectivity[0]
    base = ref_slowness[0]
    real_in = wave[0] + handed_field[0] + OMEGA * OMEGA * refl * source_field[0]
    imag_in = wave[1] + handed_field[1] + OMEGA * OMEGA * refl * source_field[1]
    angle = -OMEGA * (slow - base) * DEPTH_STEP
    cosine = jnp.cos(angle)
    sine = jnp.sin(angle)
    field = columns_forward((real_in * cosine - imag_in * sine, real_in * sine + imag_in * cosine))
    count, columns = field[0].shape
    groups = lax.axis_size("gx")
    device = lax.axis_index("gx")
    total_rows = count * groups
    scale = 1.0 / (total_rows * columns)
    turned = lax.all_to_all(jnp.stack(field), "gx", split_axis=2, concat_axis=1, tiled=True)
    width = turned.shape[2]
    freq_row = permuted_freq(jnp.arange(total_rows, dtype=jnp.int32), total_rows)
    freq_col = permuted_freq(device * width + jnp.arange(width, dtype=jnp.int32), columns)
    factor = propagator(freq_row[:, None], freq_col[None, :], base, scale)
    spatial = rows_shift(turned, jnp.stack(factor))
    back = lax.all_to_all(spatial, "gx", split_axis=1, concat_axis=2, tiled=True)
    field = (back[0], back[1])
    out_real, out_imag = columns_inverse(field)
    image = source_field[0] * out_real + source_field[1] * out_imag
    return (jnp.stack([out_real, out_imag])[None].astype(jnp.bfloat16), image[None])


def solution(mesh):
    return jax.shard_map(
        body,
        mesh=mesh,
        in_specs=(
            P("slab", None, "gx", None),
            P("slab", None, "gx", None),
            P("slab", None, "gx", None),
            P("slab", "gx", None),
            P("slab", "gx", None),
            P("slab"),
        ),
        out_specs=(P("slab", None, "gx", None), P("slab", "gx", None)),
        check_vma=False,
    )
```

```python
from functools import partial
import math

import jax
import jax.numpy as jnp
from jax import lax
from jax.sharding import PartitionSpec as P
from jax.experimental import pallas as pl
from jax.experimental.pallas import tpu as pltpu

OMEGA = 2.5
DEPTH_STEP = 1.0
precise = lax.Precision.HIGHEST


def shifted(block, axis, distance):
    devices = range(lax.axis_size(axis))
    route = [(i - distance, i) for i in devices if i - distance in devices]
    return lax.ppermute(block, axis, route)


def factor_pair(length):
    outer = math.gcd(length, 16)
    return (outer, length // outer)


def dft_table(length, orient):
    position = jnp.arange(length, dtype=jnp.int32)
    product = position[:, None] * position[None, :] % length
    angle = orient * 2.0 * math.pi * product.astype(jnp.float32) / length
    return (jnp.cos(angle), jnp.sin(angle))


def twiddle_table(first, second, length, orient):
    product = (
        jnp.arange(first, dtype=jnp.int32)[:, None]
        * jnp.arange(second, dtype=jnp.int32)[None, :]
        % length
    )
    angle = orient * 2.0 * math.pi * product.astype(jnp.float32) / length
    return (jnp.cos(angle), jnp.sin(angle))


def complex_einsum(form, table, field):
    mixing = partial(jnp.einsum, form, precision=precise)
    return (
        mixing(table[0], field[0]) - mixing(table[1], field[1]),
        mixing(table[0], field[1]) + mixing(table[1], field[0]),
    )


def times_complex(field, factor):
    return (
        field[0] * factor[0] - field[1] * factor[1],
        field[0] * factor[1] + field[1] * factor[0],
    )


def columns_forward(field):
    count, length = field[0].shape
    outer, inner = factor_pair(length)
    shaped = tuple((part.reshape(count, outer, inner) for part in field))
    section = complex_einsum("ka,rab->rkb", dft_table(outer, -1.0), shaped)
    section = times_complex(section, twiddle_table(outer, inner, length, -1.0))
    section = complex_einsum("mb,rkb->rkm", dft_table(inner, -1.0), section)
    return tuple((part.reshape(count, length) for part in section))


def columns_inverse(field):
    count, length = field[0].shape
    outer, inner = factor_pair(length)
    shaped = tuple((part.reshape(count, outer, inner) for part in field))
    section = complex_einsum("mb,rkm->rkb", dft_table(inner, 1.0), shaped)
    section = times_complex(section, twiddle_table(outer, inner, length, 1.0))
    section = complex_einsum("ka,rkb->rab", dft_table(outer, 1.0), section)
    return tuple((part.reshape(count, length) for part in section))


def rows_forward(field):
    length, count = field[0].shape
    outer, inner = factor_pair(length)
    shaped = tuple((part.reshape(outer, inner, count) for part in field))
    section = complex_einsum("ka,abc->kbc", dft_table(outer, -1.0), shaped)
    turned = twiddle_table(outer, inner, length, -1.0)
    section = times_complex(section, (turned[0][:, :, None], turned[1][:, :, None]))
    section = complex_einsum("mb,kbc->kmc", dft_table(inner, -1.0), section)
    return tuple((part.reshape(length, count) for part in section))


def rows_inverse(field):
    length, count = field[0].shape
    outer, inner = factor_pair(length)
    shaped = tuple((part.reshape(outer, inner, count) for part in field))
    section = complex_einsum("mb,kmc->kbc", dft_table(inner, 1.0), shaped)
    turned = twiddle_table(outer, inner, length, 1.0)
    section = times_complex(section, (turned[0][:, :, None], turned[1][:, :, None]))
    section = complex_einsum("ka,kbc->abc", dft_table(outer, 1.0), section)
    return tuple((part.reshape(length, count) for part in section))


def rotate(part, step, count):
    step %= count
    if step == 0:
        return part
    if 4 * step == count:
        return (-part[1], part[0])
    if 2 * step == count:
        return (-part[0], -part[1])
    if 4 * step == 3 * count:
        return (part[1], -part[0])
    cosine = math.cos(2.0 * math.pi * step / count)
    sine = math.sin(2.0 * math.pi * step / count)
    return (part[0] * cosine - part[1] * sine, part[0] * sine + part[1] * cosine)


def fft_slabs(parts, orient):
    count = len(parts)
    if count == 1:
        return list(parts)
    even = fft_slabs(parts[0::2], orient)
    odd = fft_slabs(parts[1::2], orient)
    half = count // 2
    out = [None] * count
    for k in range(half):
        turned = rotate(odd[k], orient * k, count)
        out[k] = (even[k][0] + turned[0], even[k][1] + turned[1])
        out[k + half] = (even[k][0] - turned[0], even[k][1] - turned[1])
    return out


def stacked_matmul(stacked, real, imag):
    size = real.shape[1]
    rows = stacked.shape[0] // 2
    both = jnp.concatenate([real, imag], axis=1)
    prod = jnp.dot(stacked, both, precision=lax.Precision.HIGH, preferred_element_type=jnp.float32)
    return (
        prod[:rows, :size] - prod[rows:, size:],
        prod[:rows, size:] + prod[rows:, :size],
    )


def rows_kernel(x_ref, p_ref, w_ref, tw_ref, o_ref):
    outer = tw_ref.shape[1]
    inner = tw_ref.shape[2]
    slabs = [
        (x_ref[0, a * inner:(a + 1) * inner, :], x_ref[1, a * inner:(a + 1) * inner, :])
        for a in range(outer)
    ]
    spec = fft_slabs(slabs, -1)
    wr = w_ref[0]
    wi = w_ref[1]
    forward = jnp.concatenate([wr, wi], axis=0)
    backward = jnp.concatenate([wr, -wi], axis=0)
    outs = []
    for k in range(outer):
        zr, zi = spec[k]
        tr = tw_ref[0, k]
        ti = tw_ref[1, k]
        zr, zi = zr * tr - zi * ti, zr * ti + zi * tr
        yr, yi = stacked_matmul(forward, zr, zi)
        pr = p_ref[0, k * inner:(k + 1) * inner, :]
        pi = p_ref[1, k * inner:(k + 1) * inner, :]
        yr, yi = yr * pr - yi * pi, yr * pi + yi * pr
        sr, si = stacked_matmul(backward, yr, yi)
        outs.append((sr * tr + si * ti, si * tr - sr * ti))
    res = fft_slabs(outs, 1)
    for a in range(outer):
        o_ref[0, a * inner:(a + 1) * inner, :] = res[a][0]
        o_ref[1, a * inner:(a + 1) * inner, :] = res[a][1]


def rows_shift(turned, factor):
    _, length, width = turned.shape
    outer, inner = factor_pair(length)
    block = min(width, 128)
    table = dft_table(inner, -1.0)
    turn = twiddle_table(outer, inner, length, -1.0)
    table = jnp.stack(table)
    turn = jnp.stack(turn)[..., None]
    field_spec = pl.BlockSpec((2, length, block), lambda j: (0, 0, j))
    return pl.pallas_call(
        rows_kernel,
        grid=(width // block,),
        in_specs=[
            field_spec,
            field_spec,
            pl.BlockSpec((2, inner, inner), lambda j: (0, 0, 0)),
            pl.BlockSpec((2, outer, inner, 1), lambda j: (0, 0, 0, 0)),
        ],
        out_specs=field_spec,
        out_shape=jax.ShapeDtypeStruct(turned.shape, jnp.float32),
    )(turned, factor, table, turn)


def signed_freq(index, length):
    signed = jnp.where(index < length // 2, index, index - length)
    return signed.astype(jnp.float32) * (2.0 * math.pi / length)


def permuted_freq(position, length):
    outer, inner = factor_pair(length)
    index = position // inner + outer * (position % inner)
    return signed_freq(index, length)


def propagator(freq_row, freq_col, base, scale):
    kz_square = (OMEGA * base) ** 2 - freq_row * freq_row - freq_col * freq_col
    root = jnp.sqrt(jnp.abs(kz_square))
    upward = kz_square >= 0.0
    real_part = jnp.where(upward, jnp.cos(root * DEPTH_STEP), jnp.exp(-root * DEPTH_STEP))
    imag_part = jnp.where(upward, -jnp.sin(root * DEPTH_STEP), jnp.zeros_like(root))
    return (real_part * scale, imag_part * scale)


CHUNKS = 4


def lens_rows(wave, handed, source, slow, refl, base):
    wave = wave.astype(jnp.float32)
    handed = handed.astype(jnp.float32)
    source = source.astype(jnp.float32)
    real_in = wave[0] + handed[0] + OMEGA * OMEGA * refl * source[0]
    imag_in = wave[1] + handed[1] + OMEGA * OMEGA * refl * source[1]
    angle = -OMEGA * (slow - base) * DEPTH_STEP
    cosine = jnp.cos(angle)
    sine = jnp.sin(angle)
    return (real_in * cosine - imag_in * sine, real_in * sine + imag_in * cosine)


def body(wavefield, boundary, source, slowness, reflectivity, ref_slowness):
    count = wavefield.shape[2]
    columns = wavefield.shape[3]
    chunks = CHUNKS if count % CHUNKS == 0 else 1
    step = count // chunks
    groups = lax.axis_size("gx")
    device = lax.axis_index("gx")
    total_rows = count * groups
    width = columns // groups
    scale = 1.0 / (total_rows * columns)
    base = ref_slowness[0]
    pieces = []
    for c in range(chunks):
        rows = slice(c * step, (c + 1) * step)
        handed = shifted(boundary[0, :, rows], "slab", -1)
        field = columns_forward(
            lens_rows(wavefield[0, :, rows], handed, source[0, :, rows], slowness[0, rows], reflectivity[0, rows], base)
        )
        sent = lax.all_to_all(jnp.stack(field), "gx", split_axis=2, concat_axis=1, tiled=True)
        pieces.append(sent.reshape(2, groups, step, width))
    turned = jnp.stack(pieces, axis=2).reshape(2, total_rows, width)
    freq_row = permuted_freq(jnp.arange(total_rows, dtype=jnp.int32), total_rows)
    freq_col = permuted_freq(device * width + jnp.arange(width, dtype=jnp.int32), columns)
    factor = propagator(freq_row[:, None], freq_col[None, :], base, scale)
    spatial = rows_shift(turned, jnp.stack(factor)).reshape(2, groups, chunks, step, width)
    extrapolated = []
    images = []
    for c in range(chunks):
        part = spatial[:, :, c].reshape(2, groups * step, width)
        back = lax.all_to_all(part, "gx", split_axis=1, concat_axis=2, tiled=True)
        out_real, out_imag = columns_inverse((back[0], back[1]))
        src = source[0, :, c * step:(c + 1) * step].astype(jnp.float32)
        images.append(src[0] * out_real + src[1] * out_imag)
        extrapolated.append(jnp.stack([out_real, out_imag]).astype(jnp.bfloat16))
    return (jnp.concatenate(extrapolated, axis=1)[None], jnp.concatenate(images, axis=0)[None])


def solution(mesh):
    return jax.shard_map(
        body,
        mesh=mesh,
        in_specs=(
            P("slab", None, "gx", None),
            P("slab", None, "gx", None),
            P("slab", None, "gx", None),
            P("slab", "gx", None),
            P("slab", "gx", None),
            P("slab"),
        ),
        out_specs=(P("slab", None, "gx", None), P("slab", "gx", None)),
        check_vma=False,
    )
```

```python
from functools import partial
import math

import jax
import jax.numpy as jnp
from jax import lax
from jax.sharding import PartitionSpec as P
from jax.experimental import pallas as pl
from jax.experimental.pallas import tpu as pltpu

OMEGA = 2.5
DEPTH_STEP = 1.0
precise = lax.Precision.HIGHEST


def shifted(block, axis, distance):
    devices = range(lax.axis_size(axis))
    route = [(i - distance, i) for i in devices if i - distance in devices]
    return lax.ppermute(block, axis, route)


def factor_pair(length):
    outer = math.gcd(length, 16)
    return (outer, length // outer)


def dft_table(length, orient):
    position = jnp.arange(length, dtype=jnp.int32)
    product = position[:, None] * position[None, :] % length
    angle = orient * 2.0 * math.pi * product.astype(jnp.float32) / length
    return (jnp.cos(angle), jnp.sin(angle))


def twiddle_table(first, second, length, orient):
    product = (
        jnp.arange(first, dtype=jnp.int32)[:, None]
        * jnp.arange(second, dtype=jnp.int32)[None, :]
        % length
    )
    angle = orient * 2.0 * math.pi * product.astype(jnp.float32) / length
    return (jnp.cos(angle), jnp.sin(angle))


def complex_einsum(form, table, field):
    mixing = partial(jnp.einsum, form, precision=precise)
    return (
        mixing(table[0], field[0]) - mixing(table[1], field[1]),
        mixing(table[0], field[1]) + mixing(table[1], field[0]),
    )


def times_complex(field, factor):
    return (
        field[0] * factor[0] - field[1] * factor[1],
        field[0] * factor[1] + field[1] * factor[0],
    )


def columns_forward(field):
    count, length = field[0].shape
    outer, inner = factor_pair(length)
    shaped = tuple((part.reshape(count, outer, inner) for part in field))
    section = complex_einsum("ka,rab->rkb", dft_table(outer, -1.0), shaped)
    section = times_complex(section, twiddle_table(outer, inner, length, -1.0))
    section = complex_einsum("mb,rkb->rkm", dft_table(inner, -1.0), section)
    return tuple((part.reshape(count, length) for part in section))


def columns_inverse(field):
    count, length = field[0].shape
    outer, inner = factor_pair(length)
    shaped = tuple((part.reshape(count, outer, inner) for part in field))
    section = complex_einsum("mb,rkm->rkb", dft_table(inner, 1.0), shaped)
    section = times_complex(section, twiddle_table(outer, inner, length, 1.0))
    section = complex_einsum("ka,rkb->rab", dft_table(outer, 1.0), section)
    return tuple((part.reshape(count, length) for part in section))


def rows_forward(field):
    length, count = field[0].shape
    outer, inner = factor_pair(length)
    shaped = tuple((part.reshape(outer, inner, count) for part in field))
    section = complex_einsum("ka,abc->kbc", dft_table(outer, -1.0), shaped)
    turned = twiddle_table(outer, inner, length, -1.0)
    section = times_complex(section, (turned[0][:, :, None], turned[1][:, :, None]))
    section = complex_einsum("mb,kbc->kmc", dft_table(inner, -1.0), section)
    return tuple((part.reshape(length, count) for part in section))


def rows_inverse(field):
    length, count = field[0].shape
    outer, inner = factor_pair(length)
    shaped = tuple((part.reshape(outer, inner, count) for part in field))
    section = complex_einsum("mb,kmc->kbc", dft_table(inner, 1.0), shaped)
    turned = twiddle_table(outer, inner, length, 1.0)
    section = times_complex(section, (turned[0][:, :, None], turned[1][:, :, None]))
    section = complex_einsum("ka,kbc->abc", dft_table(outer, 1.0), section)
    return tuple((part.reshape(length, count) for part in section))


def rotate(part, step, count):
    step %= count
    if step == 0:
        return part
    if 4 * step == count:
        return (-part[1], part[0])
    if 2 * step == count:
        return (-part[0], -part[1])
    if 4 * step == 3 * count:
        return (part[1], -part[0])
    cosine = math.cos(2.0 * math.pi * step / count)
    sine = math.sin(2.0 * math.pi * step / count)
    return (part[0] * cosine - part[1] * sine, part[0] * sine + part[1] * cosine)


def fft_slabs(parts, orient):
    count = len(parts)
    if count == 1:
        return list(parts)
    even = fft_slabs(parts[0::2], orient)
    odd = fft_slabs(parts[1::2], orient)
    half = count // 2
    out = [None] * count
    for k in range(half):
        turned = rotate(odd[k], orient * k, count)
        out[k] = (even[k][0] + turned[0], even[k][1] + turned[1])
        out[k + half] = (even[k][0] - turned[0], even[k][1] - turned[1])
    return out


def stacked_matmul(stacked, real, imag):
    size = real.shape[1]
    rows = stacked.shape[0] // 2
    both = jnp.concatenate([real, imag], axis=1)
    prod = jnp.dot(stacked, both, precision=lax.Precision.HIGH, preferred_element_type=jnp.float32)
    return (
        prod[:rows, :size] - prod[rows:, size:],
        prod[:rows, size:] + prod[rows:, :size],
    )


def rows_kernel(x_ref, p_ref, w_ref, tw_ref, o_ref):
    outer = tw_ref.shape[1]
    inner = tw_ref.shape[2]
    slabs = [
        (x_ref[0, a * inner:(a + 1) * inner, :], x_ref[1, a * inner:(a + 1) * inner, :])
        for a in range(outer)
    ]
    spec = fft_slabs(slabs, -1)
    wr = w_ref[0]
    wi = w_ref[1]
    forward = jnp.concatenate([wr, wi], axis=0)
    backward = jnp.concatenate([wr, -wi], axis=0)
    outs = []
    for k in range(outer):
        zr, zi = spec[k]
        tr = tw_ref[0, k]
        ti = tw_ref[1, k]
        zr, zi = zr * tr - zi * ti, zr * ti + zi * tr
        yr, yi = stacked_matmul(forward, zr, zi)
        pr = p_ref[0, k * inner:(k + 1) * inner, :]
        pi = p_ref[1, k * inner:(k + 1) * inner, :]
        yr, yi = yr * pr - yi * pi, yr * pi + yi * pr
        sr, si = stacked_matmul(backward, yr, yi)
        outs.append((sr * tr + si * ti, si * tr - sr * ti))
    res = fft_slabs(outs, 1)
    for a in range(outer):
        o_ref[0, a * inner:(a + 1) * inner, :] = res[a][0]
        o_ref[1, a * inner:(a + 1) * inner, :] = res[a][1]


def rows_shift(turned, factor):
    _, length, width = turned.shape
    outer, inner = factor_pair(length)
    block = min(width, 128)
    table = dft_table(inner, -1.0)
    turn = twiddle_table(outer, inner, length, -1.0)
    table = jnp.stack(table)
    turn = jnp.stack(turn)[..., None]
    field_spec = pl.BlockSpec((2, length, block), lambda j: (0, 0, j))
    return pl.pallas_call(
        rows_kernel,
        grid=(width // block,),
        in_specs=[
            field_spec,
            field_spec,
            pl.BlockSpec((2, inner, inner), lambda j: (0, 0, 0)),
            pl.BlockSpec((2, outer, inner, 1), lambda j: (0, 0, 0, 0)),
        ],
        out_specs=field_spec,
        out_shape=jax.ShapeDtypeStruct(turned.shape, jnp.float32),
    )(turned, factor, table, turn)


def lanes_forward_kernel(base_ref, wave_ref, hand_ref, src_ref, slow_ref, refl_ref, w_ref, tw_ref, o_ref):
    outer = tw_ref.shape[1]
    inner = tw_ref.shape[2]
    base = base_ref[0, 0]
    gain = OMEGA * OMEGA * refl_ref[0]
    real_in = (
        wave_ref[0, 0].astype(jnp.float32)
        + hand_ref[0].astype(jnp.float32)
        + gain * src_ref[0, 0].astype(jnp.float32)
    )
    imag_in = (
        wave_ref[0, 1].astype(jnp.float32)
        + hand_ref[1].astype(jnp.float32)
        + gain * src_ref[0, 1].astype(jnp.float32)
    )
    angle = -OMEGA * (slow_ref[0] - base) * DEPTH_STEP
    cosine = jnp.cos(angle)
    sine = jnp.sin(angle)
    lensed_real = real_in * cosine - imag_in * sine
    lensed_imag = real_in * sine + imag_in * cosine
    slabs = [
        (lensed_real[:, a * inner:(a + 1) * inner], lensed_imag[:, a * inner:(a + 1) * inner])
        for a in range(outer)
    ]
    spec = fft_slabs(slabs, -1)
    both = jnp.concatenate([w_ref[0], w_ref[1]], axis=1)
    count = lensed_real.shape[0]
    for k in range(outer):
        zr, zi = spec[k]
        tr = tw_ref[0, k:k + 1, :]
        ti = tw_ref[1, k:k + 1, :]
        zr, zi = zr * tr - zi * ti, zr * ti + zi * tr
        prod = jnp.dot(
            jnp.concatenate([zr, zi], axis=0), both,
            precision=lax.Precision.HIGH, preferred_element_type=jnp.float32,
        )
        o_ref[0, :, k * inner:(k + 1) * inner] = prod[:count, :inner] - prod[count:, inner:]
        o_ref[1, :, k * inner:(k + 1) * inner] = prod[:count, inner:] + prod[count:, :inner]


def lanes_inverse_kernel(x_ref, src_ref, w_ref, tw_ref, ext_ref, img_ref):
    outer = tw_ref.shape[1]
    inner = tw_ref.shape[2]
    count = x_ref.shape[1]
    both = jnp.concatenate([w_ref[0], -w_ref[1]], axis=1)
    outs = []
    for k in range(outer):
        yr = x_ref[0, :, k * inner:(k + 1) * inner]
        yi = x_ref[1, :, k * inner:(k + 1) * inner]
        prod = jnp.dot(
            jnp.concatenate([yr, yi], axis=0), both,
            precision=lax.Precision.HIGH, preferred_element_type=jnp.float32,
        )
        sr = prod[:count, :inner] - prod[count:, inner:]
        si = prod[:count, inner:] + prod[count:, :inner]
        tr = tw_ref[0, k:k + 1, :]
        ti = tw_ref[1, k:k + 1, :]
        outs.append((sr * tr + si * ti, si * tr - sr * ti))
    res = fft_slabs(outs, 1)
    for a in range(outer):
        out_real, out_imag = res[a]
        lanes = slice(a * inner, (a + 1) * inner)
        ext_ref[0, 0, :, lanes] = out_real.astype(ext_ref.dtype)
        ext_ref[0, 1, :, lanes] = out_imag.astype(ext_ref.dtype)
        img_ref[0, :, lanes] = (
            src_ref[0, 0, :, lanes].astype(jnp.float32) * out_real
            + src_ref[0, 1, :, lanes].astype(jnp.float32) * out_imag
        )


def lane_tables(length):
    outer, inner = factor_pair(length)
    table = jnp.stack(dft_table(inner, -1.0))
    turn = jnp.stack(twiddle_table(outer, inner, length, -1.0))
    return outer, inner, table, turn


def lanes_forward(wavefield, handed, source, slowness, reflectivity, base, first, step):
    length = wavefield.shape[3]
    outer, inner, table, turn = lane_tables(length)
    block = min(step, 32)
    offset = first // block
    quad = lambda i: (0, 0, offset + i, 0)
    flat = lambda i: (0, offset + i, 0)
    return pl.pallas_call(
        lanes_forward_kernel,
        grid=(step // block,),
        in_specs=[
            pl.BlockSpec(memory_space=pltpu.SMEM),
            pl.BlockSpec((1, 2, block, length), quad),
            pl.BlockSpec((2, block, length), lambda i: (0, i, 0)),
            pl.BlockSpec((1, 2, block, length), quad),
            pl.BlockSpec((1, block, length), flat),
            pl.BlockSpec((1, block, length), flat),
            pl.BlockSpec((2, inner, inner), lambda i: (0, 0, 0)),
            pl.BlockSpec((2, outer, inner), lambda i: (0, 0, 0)),
        ],
        out_specs=pl.BlockSpec((2, block, length), lambda i: (0, i, 0)),
        out_shape=jax.ShapeDtypeStruct((2, step, length), jnp.float32),
    )(base.reshape(1, 1), wavefield, handed, source, slowness, reflectivity, table, turn)


def lanes_inverse(back, source):
    _, step, length = back.shape
    outer, inner, table, turn = lane_tables(length)
    block = min(step, 32)
    return pl.pallas_call(
        lanes_inverse_kernel,
        grid=(step // block,),
        in_specs=[
            pl.BlockSpec((2, block, length), lambda i: (0, i, 0)),
            pl.BlockSpec((1, 2, block, length), lambda i: (0, 0, i, 0)),
            pl.BlockSpec((2, inner, inner), lambda i: (0, 0, 0)),
            pl.BlockSpec((2, outer, inner), lambda i: (0, 0, 0)),
        ],
        out_specs=[
            pl.BlockSpec((1, 2, block, length), lambda i: (0, 0, i, 0)),
            pl.BlockSpec((1, block, length), lambda i: (0, i, 0)),
        ],
        out_shape=[
            jax.ShapeDtypeStruct((1, 2, step, length), jnp.bfloat16),
            jax.ShapeDtypeStruct((1, step, length), jnp.float32),
        ],
    )(back, source, table, turn)


def signed_freq(index, length):
    signed = jnp.where(index < length // 2, index, index - length)
    return signed.astype(jnp.float32) * (2.0 * math.pi / length)


def permuted_freq(position, length):
    outer, inner = factor_pair(length)
    index = position // inner + outer * (position % inner)
    return signed_freq(index, length)


def propagator(freq_row, freq_col, base, scale):
    kz_square = (OMEGA * base) ** 2 - freq_row * freq_row - freq_col * freq_col
    root = jnp.sqrt(jnp.abs(kz_square))
    upward = kz_square >= 0.0
    real_part = jnp.where(upward, jnp.cos(root * DEPTH_STEP), jnp.exp(-root * DEPTH_STEP))
    imag_part = jnp.where(upward, -jnp.sin(root * DEPTH_STEP), jnp.zeros_like(root))
    return (real_part * scale, imag_part * scale)


CHUNKS = 4


def lens_rows(wave, handed, source, slow, refl, base):
    wave = wave.astype(jnp.float32)
    handed = handed.astype(jnp.float32)
    source = source.astype(jnp.float32)
    real_in = wave[0] + handed[0] + OMEGA * OMEGA * refl * source[0]
    imag_in = wave[1] + handed[1] + OMEGA * OMEGA * refl * source[1]
    angle = -OMEGA * (slow - base) * DEPTH_STEP
    cosine = jnp.cos(angle)
    sine = jnp.sin(angle)
    return (real_in * cosine - imag_in * sine, real_in * sine + imag_in * cosine)


def body(wavefield, boundary, source, slowness, reflectivity, ref_slowness):
    count = wavefield.shape[2]
    columns = wavefield.shape[3]
    chunks = CHUNKS if count % CHUNKS == 0 else 1
    step = count // chunks
    groups = lax.axis_size("gx")
    device = lax.axis_index("gx")
    total_rows = count * groups
    width = columns // groups
    scale = 1.0 / (total_rows * columns)
    base = ref_slowness[0]
    pieces = []
    for c in range(chunks):
        rows = slice(c * step, (c + 1) * step)
        handed = shifted(boundary[0, :, rows], "slab", -1)
        field = lanes_forward(wavefield, handed, source, slowness, reflectivity, base, c * step, step)
        sent = lax.all_to_all(field, "gx", split_axis=2, concat_axis=1, tiled=True)
        pieces.append(sent.reshape(2, groups, step, width))
    turned = jnp.stack(pieces, axis=2).reshape(2, total_rows, width)
    freq_row = permuted_freq(jnp.arange(total_rows, dtype=jnp.int32), total_rows)
    freq_col = permuted_freq(device * width + jnp.arange(width, dtype=jnp.int32), columns)
    factor = propagator(freq_row[:, None], freq_col[None, :], base, scale)
    spatial = rows_shift(turned, jnp.stack(factor)).reshape(2, groups, chunks, step, width)
    extrapolated = []
    images = []
    for c in range(chunks):
        part = spatial[:, :, c].reshape(2, groups * step, width)
        back = lax.all_to_all(part, "gx", split_axis=1, concat_axis=2, tiled=True)
        ext, img = lanes_inverse(back, source[:, :, c * step:(c + 1) * step])
        extrapolated.append(ext)
        images.append(img)
    return (jnp.concatenate(extrapolated, axis=2), jnp.concatenate(images, axis=1))


def solution(mesh):
    return jax.shard_map(
        body,
        mesh=mesh,
        in_specs=(
            P("slab", None, "gx", None),
            P("slab", None, "gx", None),
            P("slab", None, "gx", None),
            P("slab", "gx", None),
            P("slab", "gx", None),
            P("slab"),
        ),
        out_specs=(P("slab", None, "gx", None), P("slab", "gx", None)),
        check_vma=False,
    )
```

```python
from functools import partial
import math

import jax
import jax.numpy as jnp
from jax import lax
from jax.sharding import PartitionSpec as P
from jax.experimental import pallas as pl
from jax.experimental.pallas import tpu as pltpu

OMEGA = 2.5
DEPTH_STEP = 1.0
precise = lax.Precision.HIGHEST


def shifted(block, axis, distance):
    devices = range(lax.axis_size(axis))
    route = [(i - distance, i) for i in devices if i - distance in devices]
    return lax.ppermute(block, axis, route)


def factor_pair(length):
    outer = math.gcd(length, 16)
    return (outer, length // outer)


def dft_table(length, orient):
    position = jnp.arange(length, dtype=jnp.int32)
    product = position[:, None] * position[None, :] % length
    angle = orient * 2.0 * math.pi * product.astype(jnp.float32) / length
    return (jnp.cos(angle), jnp.sin(angle))


def twiddle_table(first, second, length, orient):
    product = (
        jnp.arange(first, dtype=jnp.int32)[:, None]
        * jnp.arange(second, dtype=jnp.int32)[None, :]
        % length
    )
    angle = orient * 2.0 * math.pi * product.astype(jnp.float32) / length
    return (jnp.cos(angle), jnp.sin(angle))


def complex_einsum(form, table, field):
    mixing = partial(jnp.einsum, form, precision=precise)
    return (
        mixing(table[0], field[0]) - mixing(table[1], field[1]),
        mixing(table[0], field[1]) + mixing(table[1], field[0]),
    )


def times_complex(field, factor):
    return (
        field[0] * factor[0] - field[1] * factor[1],
        field[0] * factor[1] + field[1] * factor[0],
    )


def columns_forward(field):
    count, length = field[0].shape
    outer, inner = factor_pair(length)
    shaped = tuple((part.reshape(count, outer, inner) for part in field))
    section = complex_einsum("ka,rab->rkb", dft_table(outer, -1.0), shaped)
    section = times_complex(section, twiddle_table(outer, inner, length, -1.0))
    section = complex_einsum("mb,rkb->rkm", dft_table(inner, -1.0), section)
    return tuple((part.reshape(count, length) for part in section))


def columns_inverse(field):
    count, length = field[0].shape
    outer, inner = factor_pair(length)
    shaped = tuple((part.reshape(count, outer, inner) for part in field))
    section = complex_einsum("mb,rkm->rkb", dft_table(inner, 1.0), shaped)
    section = times_complex(section, twiddle_table(outer, inner, length, 1.0))
    section = complex_einsum("ka,rkb->rab", dft_table(outer, 1.0), section)
    return tuple((part.reshape(count, length) for part in section))


def rows_forward(field):
    length, count = field[0].shape
    outer, inner = factor_pair(length)
    shaped = tuple((part.reshape(outer, inner, count) for part in field))
    section = complex_einsum("ka,abc->kbc", dft_table(outer, -1.0), shaped)
    turned = twiddle_table(outer, inner, length, -1.0)
    section = times_complex(section, (turned[0][:, :, None], turned[1][:, :, None]))
    section = complex_einsum("mb,kbc->kmc", dft_table(inner, -1.0), section)
    return tuple((part.reshape(length, count) for part in section))


def rows_inverse(field):
    length, count = field[0].shape
    outer, inner = factor_pair(length)
    shaped = tuple((part.reshape(outer, inner, count) for part in field))
    section = complex_einsum("mb,kmc->kbc", dft_table(inner, 1.0), shaped)
    turned = twiddle_table(outer, inner, length, 1.0)
    section = times_complex(section, (turned[0][:, :, None], turned[1][:, :, None]))
    section = complex_einsum("ka,kbc->abc", dft_table(outer, 1.0), section)
    return tuple((part.reshape(length, count) for part in section))


def rotate(part, step, count):
    step %= count
    if step == 0:
        return part
    if 4 * step == count:
        return (-part[1], part[0])
    if 2 * step == count:
        return (-part[0], -part[1])
    if 4 * step == 3 * count:
        return (part[1], -part[0])
    cosine = math.cos(2.0 * math.pi * step / count)
    sine = math.sin(2.0 * math.pi * step / count)
    return (part[0] * cosine - part[1] * sine, part[0] * sine + part[1] * cosine)


def fft_slabs(parts, orient):
    count = len(parts)
    if count == 1:
        return list(parts)
    even = fft_slabs(parts[0::2], orient)
    odd = fft_slabs(parts[1::2], orient)
    half = count // 2
    out = [None] * count
    for k in range(half):
        turned = rotate(odd[k], orient * k, count)
        out[k] = (even[k][0] + turned[0], even[k][1] + turned[1])
        out[k + half] = (even[k][0] - turned[0], even[k][1] - turned[1])
    return out


def stacked_matmul(stacked, real, imag):
    size = real.shape[1]
    rows = stacked.shape[0] // 2
    both = jnp.concatenate([real, imag], axis=1)
    prod = jnp.dot(stacked, both, precision=lax.Precision.HIGH, preferred_element_type=jnp.float32)
    return (
        prod[:rows, :size] - prod[rows:, size:],
        prod[:rows, size:] + prod[rows:, :size],
    )


def rows_kernel(x_ref, p_ref, w_ref, tw_ref, o_ref):
    outer = tw_ref.shape[1]
    inner = tw_ref.shape[2]
    slabs = [
        (x_ref[0, a * inner:(a + 1) * inner, :], x_ref[1, a * inner:(a + 1) * inner, :])
        for a in range(outer)
    ]
    spec = fft_slabs(slabs, -1)
    wr = w_ref[0]
    wi = w_ref[1]
    forward = jnp.concatenate([wr, wi], axis=0)
    backward = jnp.concatenate([wr, -wi], axis=0)
    outs = []
    for k in range(outer):
        zr, zi = spec[k]
        tr = tw_ref[0, k]
        ti = tw_ref[1, k]
        zr, zi = zr * tr - zi * ti, zr * ti + zi * tr
        yr, yi = stacked_matmul(forward, zr, zi)
        pr = p_ref[0, k * inner:(k + 1) * inner, :]
        pi = p_ref[1, k * inner:(k + 1) * inner, :]
        yr, yi = yr * pr - yi * pi, yr * pi + yi * pr
        sr, si = stacked_matmul(backward, yr, yi)
        outs.append((sr * tr + si * ti, si * tr - sr * ti))
    res = fft_slabs(outs, 1)
    for a in range(outer):
        o_ref[0, a * inner:(a + 1) * inner, :] = res[a][0]
        o_ref[1, a * inner:(a + 1) * inner, :] = res[a][1]


def rows_shift(turned, factor):
    _, length, width = turned.shape
    outer, inner = factor_pair(length)
    block = min(width, 128)
    table = dft_table(inner, -1.0)
    turn = twiddle_table(outer, inner, length, -1.0)
    table = jnp.stack(table)
    turn = jnp.stack(turn)[..., None]
    field_spec = pl.BlockSpec((2, length, block), lambda j: (0, 0, j))
    return pl.pallas_call(
        rows_kernel,
        grid=(width // block,),
        in_specs=[
            field_spec,
            field_spec,
            pl.BlockSpec((2, inner, inner), lambda j: (0, 0, 0)),
            pl.BlockSpec((2, outer, inner, 1), lambda j: (0, 0, 0, 0)),
        ],
        out_specs=field_spec,
        out_shape=jax.ShapeDtypeStruct(turned.shape, jnp.float32),
    )(turned, factor, table, turn)


def lanes_forward_kernel(base_ref, wave_ref, hand_ref, src_ref, slow_ref, refl_ref, w_ref, tw_ref, o_ref):
    outer = tw_ref.shape[1]
    inner = tw_ref.shape[2]
    base = base_ref[0, 0]
    gain = OMEGA * OMEGA * refl_ref[0]
    real_in = (
        wave_ref[0, 0].astype(jnp.float32)
        + hand_ref[0].astype(jnp.float32)
        + gain * src_ref[0, 0].astype(jnp.float32)
    )
    imag_in = (
        wave_ref[0, 1].astype(jnp.float32)
        + hand_ref[1].astype(jnp.float32)
        + gain * src_ref[0, 1].astype(jnp.float32)
    )
    angle = -OMEGA * (slow_ref[0] - base) * DEPTH_STEP
    cosine = jnp.cos(angle)
    sine = jnp.sin(angle)
    lensed_real = real_in * cosine - imag_in * sine
    lensed_imag = real_in * sine + imag_in * cosine
    slabs = [
        (lensed_real[:, a * inner:(a + 1) * inner], lensed_imag[:, a * inner:(a + 1) * inner])
        for a in range(outer)
    ]
    spec = fft_slabs(slabs, -1)
    both = jnp.concatenate([w_ref[0], w_ref[1]], axis=1)
    count = lensed_real.shape[0]
    for k in range(outer):
        zr, zi = spec[k]
        tr = tw_ref[0, k:k + 1, :]
        ti = tw_ref[1, k:k + 1, :]
        zr, zi = zr * tr - zi * ti, zr * ti + zi * tr
        prod = jnp.dot(
            jnp.concatenate([zr, zi], axis=0), both,
            precision=lax.Precision.HIGH, preferred_element_type=jnp.float32,
        )
        o_ref[0, :, k * inner:(k + 1) * inner] = prod[:count, :inner] - prod[count:, inner:]
        o_ref[1, :, k * inner:(k + 1) * inner] = prod[:count, inner:] + prod[count:, :inner]


def lanes_inverse_kernel(x_ref, src_ref, w_ref, tw_ref, ext_ref, img_ref):
    outer = tw_ref.shape[1]
    inner = tw_ref.shape[2]
    count = x_ref.shape[1]
    both = jnp.concatenate([w_ref[0], -w_ref[1]], axis=1)
    outs = []
    for k in range(outer):
        yr = x_ref[0, :, k * inner:(k + 1) * inner]
        yi = x_ref[1, :, k * inner:(k + 1) * inner]
        prod = jnp.dot(
            jnp.concatenate([yr, yi], axis=0), both,
            precision=lax.Precision.HIGH, preferred_element_type=jnp.float32,
        )
        sr = prod[:count, :inner] - prod[count:, inner:]
        si = prod[:count, inner:] + prod[count:, :inner]
        tr = tw_ref[0, k:k + 1, :]
        ti = tw_ref[1, k:k + 1, :]
        outs.append((sr * tr + si * ti, si * tr - sr * ti))
    res = fft_slabs(outs, 1)
    for a in range(outer):
        out_real, out_imag = res[a]
        lanes = slice(a * inner, (a + 1) * inner)
        ext_ref[0, 0, :, lanes] = out_real.astype(ext_ref.dtype)
        ext_ref[0, 1, :, lanes] = out_imag.astype(ext_ref.dtype)
        img_ref[0, :, lanes] = (
            src_ref[0, 0, :, lanes].astype(jnp.float32) * out_real
            + src_ref[0, 1, :, lanes].astype(jnp.float32) * out_imag
        )


def lane_tables(length):
    outer, inner = factor_pair(length)
    table = jnp.stack(dft_table(inner, -1.0))
    turn = jnp.stack(twiddle_table(outer, inner, length, -1.0))
    return outer, inner, table, turn


def lanes_forward(wavefield, handed, source, slowness, reflectivity, base, first, step):
    length = wavefield.shape[3]
    outer, inner, table, turn = lane_tables(length)
    block = min(step, 32)
    offset = first // block
    quad = lambda i: (0, 0, offset + i, 0)
    flat = lambda i: (0, offset + i, 0)
    return pl.pallas_call(
        lanes_forward_kernel,
        grid=(step // block,),
        in_specs=[
            pl.BlockSpec(memory_space=pltpu.SMEM),
            pl.BlockSpec((1, 2, block, length), quad),
            pl.BlockSpec((2, block, length), lambda i: (0, i, 0)),
            pl.BlockSpec((1, 2, block, length), quad),
            pl.BlockSpec((1, block, length), flat),
            pl.BlockSpec((1, block, length), flat),
            pl.BlockSpec((2, inner, inner), lambda i: (0, 0, 0)),
            pl.BlockSpec((2, outer, inner), lambda i: (0, 0, 0)),
        ],
        out_specs=pl.BlockSpec((2, block, length), lambda i: (0, i, 0)),
        out_shape=jax.ShapeDtypeStruct((2, step, length), jnp.float32),
    )(base.reshape(1, 1), wavefield, handed, source, slowness, reflectivity, table, turn)


def lanes_inverse(back, source):
    _, step, length = back.shape
    outer, inner, table, turn = lane_tables(length)
    block = min(step, 32)
    return pl.pallas_call(
        lanes_inverse_kernel,
        grid=(step // block,),
        in_specs=[
            pl.BlockSpec((2, block, length), lambda i: (0, i, 0)),
            pl.BlockSpec((1, 2, block, length), lambda i: (0, 0, i, 0)),
            pl.BlockSpec((2, inner, inner), lambda i: (0, 0, 0)),
            pl.BlockSpec((2, outer, inner), lambda i: (0, 0, 0)),
        ],
        out_specs=[
            pl.BlockSpec((1, 2, block, length), lambda i: (0, 0, i, 0)),
            pl.BlockSpec((1, block, length), lambda i: (0, i, 0)),
        ],
        out_shape=[
            jax.ShapeDtypeStruct((1, 2, step, length), jnp.bfloat16),
            jax.ShapeDtypeStruct((1, step, length), jnp.float32),
        ],
    )(back, source, table, turn)


def signed_freq(index, length):
    signed = jnp.where(index < length // 2, index, index - length)
    return signed.astype(jnp.float32) * (2.0 * math.pi / length)


def permuted_freq(position, length):
    outer, inner = factor_pair(length)
    index = position // inner + outer * (position % inner)
    return signed_freq(index, length)


def propagator(freq_row, freq_col, base, scale):
    kz_square = (OMEGA * base) ** 2 - freq_row * freq_row - freq_col * freq_col
    root = jnp.sqrt(jnp.abs(kz_square))
    upward = kz_square >= 0.0
    real_part = jnp.where(upward, jnp.cos(root * DEPTH_STEP), jnp.exp(-root * DEPTH_STEP))
    imag_part = jnp.where(upward, -jnp.sin(root * DEPTH_STEP), jnp.zeros_like(root))
    return (real_part * scale, imag_part * scale)


CHUNKS = 1


def lens_rows(wave, handed, source, slow, refl, base):
    wave = wave.astype(jnp.float32)
    handed = handed.astype(jnp.float32)
    source = source.astype(jnp.float32)
    real_in = wave[0] + handed[0] + OMEGA * OMEGA * refl * source[0]
    imag_in = wave[1] + handed[1] + OMEGA * OMEGA * refl * source[1]
    angle = -OMEGA * (slow - base) * DEPTH_STEP
    cosine = jnp.cos(angle)
    sine = jnp.sin(angle)
    return (real_in * cosine - imag_in * sine, real_in * sine + imag_in * cosine)


def body(wavefield, boundary, source, slowness, reflectivity, ref_slowness):
    count = wavefield.shape[2]
    columns = wavefield.shape[3]
    chunks = CHUNKS if count % CHUNKS == 0 else 1
    step = count // chunks
    groups = lax.axis_size("gx")
    device = lax.axis_index("gx")
    total_rows = count * groups
    width = columns // groups
    scale = 1.0 / (total_rows * columns)
    base = ref_slowness[0]
    pieces = []
    for c in range(chunks):
        rows = slice(c * step, (c + 1) * step)
        handed = shifted(boundary[0, :, rows], "slab", -1)
        field = lanes_forward(wavefield, handed, source, slowness, reflectivity, base, c * step, step)
        sent = lax.all_to_all(field, "gx", split_axis=2, concat_axis=1, tiled=True)
        pieces.append(sent.reshape(2, groups, step, width))
    turned = jnp.stack(pieces, axis=2).reshape(2, total_rows, width)
    freq_row = permuted_freq(jnp.arange(total_rows, dtype=jnp.int32), total_rows)
    freq_col = permuted_freq(device * width + jnp.arange(width, dtype=jnp.int32), columns)
    factor = propagator(freq_row[:, None], freq_col[None, :], base, scale)
    spatial = rows_shift(turned, jnp.stack(factor)).reshape(2, groups, chunks, step, width)
    extrapolated = []
    images = []
    for c in range(chunks):
        part = spatial[:, :, c].reshape(2, groups * step, width)
        back = lax.all_to_all(part, "gx", split_axis=1, concat_axis=2, tiled=True)
        ext, img = lanes_inverse(back, source[:, :, c * step:(c + 1) * step])
        extrapolated.append(ext)
        images.append(img)
    return (jnp.concatenate(extrapolated, axis=2), jnp.concatenate(images, axis=1))


def solution(mesh):
    return jax.shard_map(
        body,
        mesh=mesh,
        in_specs=(
            P("slab", None, "gx", None),
            P("slab", None, "gx", None),
            P("slab", None, "gx", None),
            P("slab", "gx", None),
            P("slab", "gx", None),
            P("slab"),
        ),
        out_specs=(P("slab", None, "gx", None), P("slab", "gx", None)),
        check_vma=False,
    )
```

```python
from functools import partial
import math

import jax
import jax.numpy as jnp
from jax import lax
from jax.sharding import PartitionSpec as P
from jax.experimental import pallas as pl
from jax.experimental.pallas import tpu as pltpu

OMEGA = 2.5
DEPTH_STEP = 1.0
precise = lax.Precision.HIGHEST


def shifted(block, axis, distance):
    devices = range(lax.axis_size(axis))
    route = [(i - distance, i) for i in devices if i - distance in devices]
    return lax.ppermute(block, axis, route)


def factor_pair(length):
    outer = math.gcd(length, 16)
    return (outer, length // outer)


def dft_table(length, orient):
    position = jnp.arange(length, dtype=jnp.int32)
    product = position[:, None] * position[None, :] % length
    angle = orient * 2.0 * math.pi * product.astype(jnp.float32) / length
    return (jnp.cos(angle), jnp.sin(angle))


def twiddle_table(first, second, length, orient):
    product = (
        jnp.arange(first, dtype=jnp.int32)[:, None]
        * jnp.arange(second, dtype=jnp.int32)[None, :]
        % length
    )
    angle = orient * 2.0 * math.pi * product.astype(jnp.float32) / length
    return (jnp.cos(angle), jnp.sin(angle))


def complex_einsum(form, table, field):
    mixing = partial(jnp.einsum, form, precision=precise)
    return (
        mixing(table[0], field[0]) - mixing(table[1], field[1]),
        mixing(table[0], field[1]) + mixing(table[1], field[0]),
    )


def times_complex(field, factor):
    return (
        field[0] * factor[0] - field[1] * factor[1],
        field[0] * factor[1] + field[1] * factor[0],
    )


def columns_forward(field):
    count, length = field[0].shape
    outer, inner = factor_pair(length)
    shaped = tuple((part.reshape(count, outer, inner) for part in field))
    section = complex_einsum("ka,rab->rkb", dft_table(outer, -1.0), shaped)
    section = times_complex(section, twiddle_table(outer, inner, length, -1.0))
    section = complex_einsum("mb,rkb->rkm", dft_table(inner, -1.0), section)
    return tuple((part.reshape(count, length) for part in section))


def columns_inverse(field):
    count, length = field[0].shape
    outer, inner = factor_pair(length)
    shaped = tuple((part.reshape(count, outer, inner) for part in field))
    section = complex_einsum("mb,rkm->rkb", dft_table(inner, 1.0), shaped)
    section = times_complex(section, twiddle_table(outer, inner, length, 1.0))
    section = complex_einsum("ka,rkb->rab", dft_table(outer, 1.0), section)
    return tuple((part.reshape(count, length) for part in section))


def rows_forward(field):
    length, count = field[0].shape
    outer, inner = factor_pair(length)
    shaped = tuple((part.reshape(outer, inner, count) for part in field))
    section = complex_einsum("ka,abc->kbc", dft_table(outer, -1.0), shaped)
    turned = twiddle_table(outer, inner, length, -1.0)
    section = times_complex(section, (turned[0][:, :, None], turned[1][:, :, None]))
    section = complex_einsum("mb,kbc->kmc", dft_table(inner, -1.0), section)
    return tuple((part.reshape(length, count) for part in section))


def rows_inverse(field):
    length, count = field[0].shape
    outer, inner = factor_pair(length)
    shaped = tuple((part.reshape(outer, inner, count) for part in field))
    section = complex_einsum("mb,kmc->kbc", dft_table(inner, 1.0), shaped)
    turned = twiddle_table(outer, inner, length, 1.0)
    section = times_complex(section, (turned[0][:, :, None], turned[1][:, :, None]))
    section = complex_einsum("ka,kbc->abc", dft_table(outer, 1.0), section)
    return tuple((part.reshape(length, count) for part in section))


def rotate(part, step, count):
    step %= count
    if step == 0:
        return part
    if 4 * step == count:
        return (-part[1], part[0])
    if 2 * step == count:
        return (-part[0], -part[1])
    if 4 * step == 3 * count:
        return (part[1], -part[0])
    cosine = math.cos(2.0 * math.pi * step / count)
    sine = math.sin(2.0 * math.pi * step / count)
    return (part[0] * cosine - part[1] * sine, part[0] * sine + part[1] * cosine)


def fft_slabs(parts, orient):
    count = len(parts)
    if count == 1:
        return list(parts)
    even = fft_slabs(parts[0::2], orient)
    odd = fft_slabs(parts[1::2], orient)
    half = count // 2
    out = [None] * count
    for k in range(half):
        turned = rotate(odd[k], orient * k, count)
        out[k] = (even[k][0] + turned[0], even[k][1] + turned[1])
        out[k + half] = (even[k][0] - turned[0], even[k][1] - turned[1])
    return out


def stacked_matmul(stacked, real, imag):
    size = real.shape[1]
    rows = stacked.shape[0] // 2
    both = jnp.concatenate([real, imag], axis=1)
    prod = jnp.dot(stacked, both, precision=lax.Precision.HIGH, preferred_element_type=jnp.float32)
    return (
        prod[:rows, :size] - prod[rows:, size:],
        prod[:rows, size:] + prod[rows:, :size],
    )


def rows_kernel(x_ref, p_ref, w_ref, tw_ref, o_ref):
    outer = tw_ref.shape[1]
    inner = tw_ref.shape[2]
    count = x_ref.shape[2]

    def place(a):
        return (a * inner) // count, slice((a * inner) % count, (a * inner) % count + inner)

    slabs = []
    for a in range(outer):
        origin, rows = place(a)
        slabs.append((x_ref[origin, 0, rows, :], x_ref[origin, 1, rows, :]))
    spec = fft_slabs(slabs, -1)
    wr = w_ref[0]
    wi = w_ref[1]
    forward = jnp.concatenate([wr, wi], axis=0)
    backward = jnp.concatenate([wr, -wi], axis=0)
    outs = []
    for k in range(outer):
        zr, zi = spec[k]
        tr = tw_ref[0, k]
        ti = tw_ref[1, k]
        zr, zi = zr * tr - zi * ti, zr * ti + zi * tr
        yr, yi = stacked_matmul(forward, zr, zi)
        pr = p_ref[0, k * inner:(k + 1) * inner, :]
        pi = p_ref[1, k * inner:(k + 1) * inner, :]
        yr, yi = yr * pr - yi * pi, yr * pi + yi * pr
        sr, si = stacked_matmul(backward, yr, yi)
        outs.append((sr * tr + si * ti, si * tr - sr * ti))
    res = fft_slabs(outs, 1)
    for a in range(outer):
        origin, rows = place(a)
        o_ref[origin, 0, rows, :] = res[a][0]
        o_ref[origin, 1, rows, :] = res[a][1]


def rows_shift(turned, factor):
    groups, _, count, width = turned.shape
    length = groups * count
    outer, inner = factor_pair(length)
    block = min(width, 128)
    table = dft_table(inner, -1.0)
    turn = twiddle_table(outer, inner, length, -1.0)
    table = jnp.stack(table)
    turn = jnp.stack(turn)[..., None]
    field_spec = pl.BlockSpec((groups, 2, count, block), lambda j: (0, 0, 0, j))
    return pl.pallas_call(
        rows_kernel,
        grid=(width // block,),
        in_specs=[
            field_spec,
            pl.BlockSpec((2, length, block), lambda j: (0, 0, j)),
            pl.BlockSpec((2, inner, inner), lambda j: (0, 0, 0)),
            pl.BlockSpec((2, outer, inner, 1), lambda j: (0, 0, 0, 0)),
        ],
        out_specs=field_spec,
        out_shape=jax.ShapeDtypeStruct(turned.shape, jnp.float32),
    )(turned, factor, table, turn)


def lanes_forward_kernel(base_ref, wave_ref, hand_ref, src_ref, slow_ref, refl_ref, w_ref, tw_ref, o_ref):
    outer = tw_ref.shape[1]
    inner = tw_ref.shape[2]
    base = base_ref[0, 0]
    gain = OMEGA * OMEGA * refl_ref[0]
    real_in = (
        wave_ref[0, 0].astype(jnp.float32)
        + hand_ref[0].astype(jnp.float32)
        + gain * src_ref[0, 0].astype(jnp.float32)
    )
    imag_in = (
        wave_ref[0, 1].astype(jnp.float32)
        + hand_ref[1].astype(jnp.float32)
        + gain * src_ref[0, 1].astype(jnp.float32)
    )
    angle = -OMEGA * (slow_ref[0] - base) * DEPTH_STEP
    cosine = jnp.cos(angle)
    sine = jnp.sin(angle)
    lensed_real = real_in * cosine - imag_in * sine
    lensed_imag = real_in * sine + imag_in * cosine
    slabs = [
        (lensed_real[:, a * inner:(a + 1) * inner], lensed_imag[:, a * inner:(a + 1) * inner])
        for a in range(outer)
    ]
    spec = fft_slabs(slabs, -1)
    both = jnp.concatenate([w_ref[0], w_ref[1]], axis=1)
    count = lensed_real.shape[0]
    for k in range(outer):
        zr, zi = spec[k]
        tr = tw_ref[0, k:k + 1, :]
        ti = tw_ref[1, k:k + 1, :]
        zr, zi = zr * tr - zi * ti, zr * ti + zi * tr
        prod = jnp.dot(
            jnp.concatenate([zr, zi], axis=0), both,
            precision=lax.Precision.HIGH, preferred_element_type=jnp.float32,
        )
        width = o_ref.shape[3]
        dest = (k * inner) // width
        lanes = slice((k * inner) % width, (k * inner) % width + inner)
        o_ref[dest, 0, :, lanes] = prod[:count, :inner] - prod[count:, inner:]
        o_ref[dest, 1, :, lanes] = prod[:count, inner:] + prod[count:, :inner]


def lanes_inverse_kernel(x_ref, src_ref, w_ref, tw_ref, ext_ref, img_ref):
    outer = tw_ref.shape[1]
    inner = tw_ref.shape[2]
    count = x_ref.shape[2]
    both = jnp.concatenate([w_ref[0], -w_ref[1]], axis=1)
    outs = []
    for k in range(outer):
        width = x_ref.shape[3]
        origin = (k * inner) // width
        lanes = slice((k * inner) % width, (k * inner) % width + inner)
        yr = x_ref[origin, 0, :, lanes]
        yi = x_ref[origin, 1, :, lanes]
        prod = jnp.dot(
            jnp.concatenate([yr, yi], axis=0), both,
            precision=lax.Precision.HIGH, preferred_element_type=jnp.float32,
        )
        sr = prod[:count, :inner] - prod[count:, inner:]
        si = prod[:count, inner:] + prod[count:, :inner]
        tr = tw_ref[0, k:k + 1, :]
        ti = tw_ref[1, k:k + 1, :]
        outs.append((sr * tr + si * ti, si * tr - sr * ti))
    res = fft_slabs(outs, 1)
    for a in range(outer):
        out_real, out_imag = res[a]
        lanes = slice(a * inner, (a + 1) * inner)
        ext_ref[0, 0, :, lanes] = out_real.astype(ext_ref.dtype)
        ext_ref[0, 1, :, lanes] = out_imag.astype(ext_ref.dtype)
        img_ref[0, :, lanes] = (
            src_ref[0, 0, :, lanes].astype(jnp.float32) * out_real
            + src_ref[0, 1, :, lanes].astype(jnp.float32) * out_imag
        )


def lane_tables(length):
    outer, inner = factor_pair(length)
    table = jnp.stack(dft_table(inner, -1.0))
    turn = jnp.stack(twiddle_table(outer, inner, length, -1.0))
    return outer, inner, table, turn


def lanes_forward(wavefield, handed, source, slowness, reflectivity, base, first, step, groups):
    length = wavefield.shape[3]
    outer, inner, table, turn = lane_tables(length)
    block = min(step, 32)
    offset = first // block
    quad = lambda i: (0, 0, offset + i, 0)
    flat = lambda i: (0, offset + i, 0)
    return pl.pallas_call(
        lanes_forward_kernel,
        grid=(step // block,),
        in_specs=[
            pl.BlockSpec(memory_space=pltpu.SMEM),
            pl.BlockSpec((1, 2, block, length), quad),
            pl.BlockSpec((2, block, length), lambda i: (0, i, 0)),
            pl.BlockSpec((1, 2, block, length), quad),
            pl.BlockSpec((1, block, length), flat),
            pl.BlockSpec((1, block, length), flat),
            pl.BlockSpec((2, inner, inner), lambda i: (0, 0, 0)),
            pl.BlockSpec((2, outer, inner), lambda i: (0, 0, 0)),
        ],
        out_specs=pl.BlockSpec((groups, 2, block, length // groups), lambda i: (0, 0, i, 0)),
        out_shape=jax.ShapeDtypeStruct((groups, 2, step, length // groups), jnp.float32),
    )(base.reshape(1, 1), wavefield, handed, source, slowness, reflectivity, table, turn)


def lanes_inverse(back, source):
    groups, _, step, width = back.shape
    length = groups * width
    outer, inner, table, turn = lane_tables(length)
    block = min(step, 32)
    return pl.pallas_call(
        lanes_inverse_kernel,
        grid=(step // block,),
        in_specs=[
            pl.BlockSpec((groups, 2, block, width), lambda i: (0, 0, i, 0)),
            pl.BlockSpec((1, 2, block, length), lambda i: (0, 0, i, 0)),
            pl.BlockSpec((2, inner, inner), lambda i: (0, 0, 0)),
            pl.BlockSpec((2, outer, inner), lambda i: (0, 0, 0)),
        ],
        out_specs=[
            pl.BlockSpec((1, 2, block, length), lambda i: (0, 0, i, 0)),
            pl.BlockSpec((1, block, length), lambda i: (0, i, 0)),
        ],
        out_shape=[
            jax.ShapeDtypeStruct((1, 2, step, length), jnp.bfloat16),
            jax.ShapeDtypeStruct((1, step, length), jnp.float32),
        ],
    )(back, source, table, turn)


def signed_freq(index, length):
    signed = jnp.where(index < length // 2, index, index - length)
    return signed.astype(jnp.float32) * (2.0 * math.pi / length)


def permuted_freq(position, length):
    outer, inner = factor_pair(length)
    index = position // inner + outer * (position % inner)
    return signed_freq(index, length)


def propagator(freq_row, freq_col, base, scale):
    kz_square = (OMEGA * base) ** 2 - freq_row * freq_row - freq_col * freq_col
    root = jnp.sqrt(jnp.abs(kz_square))
    upward = kz_square >= 0.0
    real_part = jnp.where(upward, jnp.cos(root * DEPTH_STEP), jnp.exp(-root * DEPTH_STEP))
    imag_part = jnp.where(upward, -jnp.sin(root * DEPTH_STEP), jnp.zeros_like(root))
    return (real_part * scale, imag_part * scale)


CHUNKS = 1


def lens_rows(wave, handed, source, slow, refl, base):
    wave = wave.astype(jnp.float32)
    handed = handed.astype(jnp.float32)
    source = source.astype(jnp.float32)
    real_in = wave[0] + handed[0] + OMEGA * OMEGA * refl * source[0]
    imag_in = wave[1] + handed[1] + OMEGA * OMEGA * refl * source[1]
    angle = -OMEGA * (slow - base) * DEPTH_STEP
    cosine = jnp.cos(angle)
    sine = jnp.sin(angle)
    return (real_in * cosine - imag_in * sine, real_in * sine + imag_in * cosine)


def body(wavefield, boundary, source, slowness, reflectivity, ref_slowness):
    count = wavefield.shape[2]
    columns = wavefield.shape[3]
    chunks = CHUNKS if count % CHUNKS == 0 else 1
    step = count // chunks
    groups = lax.axis_size("gx")
    device = lax.axis_index("gx")
    total_rows = count * groups
    width = columns // groups
    scale = 1.0 / (total_rows * columns)
    base = ref_slowness[0]
    pieces = []
    for c in range(chunks):
        rows = slice(c * step, (c + 1) * step)
        handed = shifted(boundary[0, :, rows], "slab", -1)
        field = lanes_forward(wavefield, handed, source, slowness, reflectivity, base, c * step, step, groups)
        pieces.append(lax.all_to_all(field, "gx", split_axis=0, concat_axis=0, tiled=True))
    turned = pieces[0] if chunks == 1 else jnp.concatenate(pieces, axis=2)
    freq_row = permuted_freq(jnp.arange(total_rows, dtype=jnp.int32), total_rows)
    freq_col = permuted_freq(device * width + jnp.arange(width, dtype=jnp.int32), columns)
    factor = propagator(freq_row[:, None], freq_col[None, :], base, scale)
    spatial = rows_shift(turned, jnp.stack(factor))
    extrapolated = []
    images = []
    for c in range(chunks):
        part = spatial[:, :, c * step:(c + 1) * step]
        back = lax.all_to_all(part, "gx", split_axis=0, concat_axis=0, tiled=True)
        ext, img = lanes_inverse(back, source[:, :, c * step:(c + 1) * step])
        extrapolated.append(ext)
        images.append(img)
    return (jnp.concatenate(extrapolated, axis=2), jnp.concatenate(images, axis=1))


def solution(mesh):
    return jax.shard_map(
        body,
        mesh=mesh,
        in_specs=(
            P("slab", None, "gx", None),
            P("slab", None, "gx", None),
            P("slab", None, "gx", None),
            P("slab", "gx", None),
            P("slab", "gx", None),
            P("slab"),
        ),
        out_specs=(P("slab", None, "gx", None), P("slab", "gx", None)),
        check_vma=False,
    )
```

```python
from functools import partial
import math

import jax
import jax.numpy as jnp
from jax import lax
from jax.sharding import PartitionSpec as P
from jax.experimental import pallas as pl
from jax.experimental.pallas import tpu as pltpu

OMEGA = 2.5
DEPTH_STEP = 1.0
precise = lax.Precision.HIGHEST


def shifted(block, axis, distance):
    devices = range(lax.axis_size(axis))
    route = [(i - distance, i) for i in devices if i - distance in devices]
    return lax.ppermute(block, axis, route)


def factor_pair(length):
    outer = math.gcd(length, 16)
    return (outer, length // outer)


def dft_table(length, orient):
    position = jnp.arange(length, dtype=jnp.int32)
    product = position[:, None] * position[None, :] % length
    angle = orient * 2.0 * math.pi * product.astype(jnp.float32) / length
    return (jnp.cos(angle), jnp.sin(angle))


def twiddle_table(first, second, length, orient):
    product = (
        jnp.arange(first, dtype=jnp.int32)[:, None]
        * jnp.arange(second, dtype=jnp.int32)[None, :]
        % length
    )
    angle = orient * 2.0 * math.pi * product.astype(jnp.float32) / length
    return (jnp.cos(angle), jnp.sin(angle))


def complex_einsum(form, table, field):
    mixing = partial(jnp.einsum, form, precision=precise)
    return (
        mixing(table[0], field[0]) - mixing(table[1], field[1]),
        mixing(table[0], field[1]) + mixing(table[1], field[0]),
    )


def times_complex(field, factor):
    return (
        field[0] * factor[0] - field[1] * factor[1],
        field[0] * factor[1] + field[1] * factor[0],
    )


def columns_forward(field):
    count, length = field[0].shape
    outer, inner = factor_pair(length)
    shaped = tuple((part.reshape(count, outer, inner) for part in field))
    section = complex_einsum("ka,rab->rkb", dft_table(outer, -1.0), shaped)
    section = times_complex(section, twiddle_table(outer, inner, length, -1.0))
    section = complex_einsum("mb,rkb->rkm", dft_table(inner, -1.0), section)
    return tuple((part.reshape(count, length) for part in section))


def columns_inverse(field):
    count, length = field[0].shape
    outer, inner = factor_pair(length)
    shaped = tuple((part.reshape(count, outer, inner) for part in field))
    section = complex_einsum("mb,rkm->rkb", dft_table(inner, 1.0), shaped)
    section = times_complex(section, twiddle_table(outer, inner, length, 1.0))
    section = complex_einsum("ka,rkb->rab", dft_table(outer, 1.0), section)
    return tuple((part.reshape(count, length) for part in section))


def rows_forward(field):
    length, count = field[0].shape
    outer, inner = factor_pair(length)
    shaped = tuple((part.reshape(outer, inner, count) for part in field))
    section = complex_einsum("ka,abc->kbc", dft_table(outer, -1.0), shaped)
    turned = twiddle_table(outer, inner, length, -1.0)
    section = times_complex(section, (turned[0][:, :, None], turned[1][:, :, None]))
    section = complex_einsum("mb,kbc->kmc", dft_table(inner, -1.0), section)
    return tuple((part.reshape(length, count) for part in section))


def rows_inverse(field):
    length, count = field[0].shape
    outer, inner = factor_pair(length)
    shaped = tuple((part.reshape(outer, inner, count) for part in field))
    section = complex_einsum("mb,kmc->kbc", dft_table(inner, 1.0), shaped)
    turned = twiddle_table(outer, inner, length, 1.0)
    section = times_complex(section, (turned[0][:, :, None], turned[1][:, :, None]))
    section = complex_einsum("ka,kbc->abc", dft_table(outer, 1.0), section)
    return tuple((part.reshape(length, count) for part in section))


def rotate(part, step, count):
    step %= count
    if step == 0:
        return part
    if 4 * step == count:
        return (-part[1], part[0])
    if 2 * step == count:
        return (-part[0], -part[1])
    if 4 * step == 3 * count:
        return (part[1], -part[0])
    cosine = math.cos(2.0 * math.pi * step / count)
    sine = math.sin(2.0 * math.pi * step / count)
    return (part[0] * cosine - part[1] * sine, part[0] * sine + part[1] * cosine)


def fft_slabs(parts, orient):
    count = len(parts)
    if count == 1:
        return list(parts)
    even = fft_slabs(parts[0::2], orient)
    odd = fft_slabs(parts[1::2], orient)
    half = count // 2
    out = [None] * count
    for k in range(half):
        turned = rotate(odd[k], orient * k, count)
        out[k] = (even[k][0] + turned[0], even[k][1] + turned[1])
        out[k + half] = (even[k][0] - turned[0], even[k][1] - turned[1])
    return out


def stacked_matmul(stacked, real, imag):
    size = real.shape[1]
    rows = stacked.shape[0] // 2
    both = jnp.concatenate([real, imag], axis=1)
    prod = jnp.dot(stacked, both, precision=lax.Precision.HIGH, preferred_element_type=jnp.float32)
    return (
        prod[:rows, :size] - prod[rows:, size:],
        prod[:rows, size:] + prod[rows:, :size],
    )


def rows_kernel(*refs):
    x_refs = refs[:-4]
    p_ref, w_ref, tw_ref, o_ref = refs[-4:]
    outer = tw_ref.shape[1]
    inner = tw_ref.shape[2]
    step = x_refs[0].shape[2]
    count = step * len(x_refs)

    def place(a):
        return (a * inner) // count, slice((a * inner) % count, (a * inner) % count + inner)

    slabs = []
    for a in range(outer):
        origin = (a * inner) // count
        part = x_refs[((a * inner) % count) // step]
        first = (a * inner) % step
        slabs.append((part[origin, 0, first:first + inner, :], part[origin, 1, first:first + inner, :]))
    spec = fft_slabs(slabs, -1)
    wr = w_ref[0]
    wi = w_ref[1]
    forward = jnp.concatenate([wr, wi], axis=0)
    backward = jnp.concatenate([wr, -wi], axis=0)
    outs = []
    for k in range(outer):
        zr, zi = spec[k]
        tr = tw_ref[0, k]
        ti = tw_ref[1, k]
        zr, zi = zr * tr - zi * ti, zr * ti + zi * tr
        yr, yi = stacked_matmul(forward, zr, zi)
        pr = p_ref[0, k * inner:(k + 1) * inner, :]
        pi = p_ref[1, k * inner:(k + 1) * inner, :]
        yr, yi = yr * pr - yi * pi, yr * pi + yi * pr
        sr, si = stacked_matmul(backward, yr, yi)
        outs.append((sr * tr + si * ti, si * tr - sr * ti))
    res = fft_slabs(outs, 1)
    for a in range(outer):
        origin, rows = place(a)
        o_ref[origin, 0, rows, :] = res[a][0]
        o_ref[origin, 1, rows, :] = res[a][1]


def rows_shift(turned, factor):
    groups, _, step, width = turned[0].shape
    length = groups * step * len(turned)
    outer, inner = factor_pair(length)
    block = min(width, 128)
    table = dft_table(inner, -1.0)
    turn = twiddle_table(outer, inner, length, -1.0)
    table = jnp.stack(table)
    turn = jnp.stack(turn)[..., None]
    field_spec = pl.BlockSpec((groups, 2, step, block), lambda j: (0, 0, 0, j))
    return pl.pallas_call(
        rows_kernel,
        grid=(width // block,),
        in_specs=[field_spec] * len(turned) + [
            pl.BlockSpec((2, length, block), lambda j: (0, 0, j)),
            pl.BlockSpec((2, inner, inner), lambda j: (0, 0, 0)),
            pl.BlockSpec((2, outer, inner, 1), lambda j: (0, 0, 0, 0)),
        ],
        out_specs=pl.BlockSpec((groups, 2, step * len(turned), block), lambda j: (0, 0, 0, j)),
        out_shape=jax.ShapeDtypeStruct((groups, 2, step * len(turned), width), jnp.float32),
    )(*turned, factor, table, turn)


def lanes_forward_kernel(base_ref, wave_ref, hand_ref, src_ref, slow_ref, refl_ref, w_ref, tw_ref, o_ref):
    outer = tw_ref.shape[1]
    inner = tw_ref.shape[2]
    base = base_ref[0, 0]
    gain = OMEGA * OMEGA * refl_ref[0]
    real_in = (
        wave_ref[0, 0].astype(jnp.float32)
        + hand_ref[0].astype(jnp.float32)
        + gain * src_ref[0, 0].astype(jnp.float32)
    )
    imag_in = (
        wave_ref[0, 1].astype(jnp.float32)
        + hand_ref[1].astype(jnp.float32)
        + gain * src_ref[0, 1].astype(jnp.float32)
    )
    angle = -OMEGA * (slow_ref[0] - base) * DEPTH_STEP
    cosine = jnp.cos(angle)
    sine = jnp.sin(angle)
    lensed_real = real_in * cosine - imag_in * sine
    lensed_imag = real_in * sine + imag_in * cosine
    slabs = [
        (lensed_real[:, a * inner:(a + 1) * inner], lensed_imag[:, a * inner:(a + 1) * inner])
        for a in range(outer)
    ]
    spec = fft_slabs(slabs, -1)
    both = jnp.concatenate([w_ref[0], w_ref[1]], axis=1)
    count = lensed_real.shape[0]
    for k in range(outer):
        zr, zi = spec[k]
        tr = tw_ref[0, k:k + 1, :]
        ti = tw_ref[1, k:k + 1, :]
        zr, zi = zr * tr - zi * ti, zr * ti + zi * tr
        prod = jnp.dot(
            jnp.concatenate([zr, zi], axis=0), both,
            precision=lax.Precision.HIGH, preferred_element_type=jnp.float32,
        )
        width = o_ref.shape[3]
        dest = (k * inner) // width
        lanes = slice((k * inner) % width, (k * inner) % width + inner)
        o_ref[dest, 0, :, lanes] = prod[:count, :inner] - prod[count:, inner:]
        o_ref[dest, 1, :, lanes] = prod[:count, inner:] + prod[count:, :inner]


def lanes_inverse_kernel(x_ref, src_ref, w_ref, tw_ref, ext_ref, img_ref):
    outer = tw_ref.shape[1]
    inner = tw_ref.shape[2]
    count = x_ref.shape[2]
    both = jnp.concatenate([w_ref[0], -w_ref[1]], axis=1)
    outs = []
    for k in range(outer):
        width = x_ref.shape[3]
        origin = (k * inner) // width
        lanes = slice((k * inner) % width, (k * inner) % width + inner)
        yr = x_ref[origin, 0, :, lanes]
        yi = x_ref[origin, 1, :, lanes]
        prod = jnp.dot(
            jnp.concatenate([yr, yi], axis=0), both,
            precision=lax.Precision.HIGH, preferred_element_type=jnp.float32,
        )
        sr = prod[:count, :inner] - prod[count:, inner:]
        si = prod[:count, inner:] + prod[count:, :inner]
        tr = tw_ref[0, k:k + 1, :]
        ti = tw_ref[1, k:k + 1, :]
        outs.append((sr * tr + si * ti, si * tr - sr * ti))
    res = fft_slabs(outs, 1)
    for a in range(outer):
        out_real, out_imag = res[a]
        lanes = slice(a * inner, (a + 1) * inner)
        ext_ref[0, 0, :, lanes] = out_real.astype(ext_ref.dtype)
        ext_ref[0, 1, :, lanes] = out_imag.astype(ext_ref.dtype)
        img_ref[0, :, lanes] = (
            src_ref[0, 0, :, lanes].astype(jnp.float32) * out_real
            + src_ref[0, 1, :, lanes].astype(jnp.float32) * out_imag
        )


def lane_tables(length):
    outer, inner = factor_pair(length)
    table = jnp.stack(dft_table(inner, -1.0))
    turn = jnp.stack(twiddle_table(outer, inner, length, -1.0))
    return outer, inner, table, turn


def lanes_forward(wavefield, handed, source, slowness, reflectivity, base, first, step, groups):
    length = wavefield.shape[3]
    outer, inner, table, turn = lane_tables(length)
    block = min(step, 32)
    offset = first // block
    quad = lambda i: (0, 0, offset + i, 0)
    flat = lambda i: (0, offset + i, 0)
    return pl.pallas_call(
        lanes_forward_kernel,
        grid=(step // block,),
        in_specs=[
            pl.BlockSpec(memory_space=pltpu.SMEM),
            pl.BlockSpec((1, 2, block, length), quad),
            pl.BlockSpec((2, block, length), lambda i: (0, i, 0)),
            pl.BlockSpec((1, 2, block, length), quad),
            pl.BlockSpec((1, block, length), flat),
            pl.BlockSpec((1, block, length), flat),
            pl.BlockSpec((2, inner, inner), lambda i: (0, 0, 0)),
            pl.BlockSpec((2, outer, inner), lambda i: (0, 0, 0)),
        ],
        out_specs=pl.BlockSpec((groups, 2, block, length // groups), lambda i: (0, 0, i, 0)),
        out_shape=jax.ShapeDtypeStruct((groups, 2, step, length // groups), jnp.float32),
    )(base.reshape(1, 1), wavefield, handed, source, slowness, reflectivity, table, turn)


def lanes_inverse(back, source):
    groups, _, step, width = back.shape
    length = groups * width
    outer, inner, table, turn = lane_tables(length)
    block = min(step, 32)
    return pl.pallas_call(
        lanes_inverse_kernel,
        grid=(step // block,),
        in_specs=[
            pl.BlockSpec((groups, 2, block, width), lambda i: (0, 0, i, 0)),
            pl.BlockSpec((1, 2, block, length), lambda i: (0, 0, i, 0)),
            pl.BlockSpec((2, inner, inner), lambda i: (0, 0, 0)),
            pl.BlockSpec((2, outer, inner), lambda i: (0, 0, 0)),
        ],
        out_specs=[
            pl.BlockSpec((1, 2, block, length), lambda i: (0, 0, i, 0)),
            pl.BlockSpec((1, block, length), lambda i: (0, i, 0)),
        ],
        out_shape=[
            jax.ShapeDtypeStruct((1, 2, step, length), jnp.bfloat16),
            jax.ShapeDtypeStruct((1, step, length), jnp.float32),
        ],
    )(back, source, table, turn)


def signed_freq(index, length):
    signed = jnp.where(index < length // 2, index, index - length)
    return signed.astype(jnp.float32) * (2.0 * math.pi / length)


def permuted_freq(position, length):
    outer, inner = factor_pair(length)
    index = position // inner + outer * (position % inner)
    return signed_freq(index, length)


def propagator(freq_row, freq_col, base, scale):
    kz_square = (OMEGA * base) ** 2 - freq_row * freq_row - freq_col * freq_col
    root = jnp.sqrt(jnp.abs(kz_square))
    upward = kz_square >= 0.0
    real_part = jnp.where(upward, jnp.cos(root * DEPTH_STEP), jnp.exp(-root * DEPTH_STEP))
    imag_part = jnp.where(upward, -jnp.sin(root * DEPTH_STEP), jnp.zeros_like(root))
    return (real_part * scale, imag_part * scale)


CHUNKS = 2


def lens_rows(wave, handed, source, slow, refl, base):
    wave = wave.astype(jnp.float32)
    handed = handed.astype(jnp.float32)
    source = source.astype(jnp.float32)
    real_in = wave[0] + handed[0] + OMEGA * OMEGA * refl * source[0]
    imag_in = wave[1] + handed[1] + OMEGA * OMEGA * refl * source[1]
    angle = -OMEGA * (slow - base) * DEPTH_STEP
    cosine = jnp.cos(angle)
    sine = jnp.sin(angle)
    return (real_in * cosine - imag_in * sine, real_in * sine + imag_in * cosine)


def body(wavefield, boundary, source, slowness, reflectivity, ref_slowness):
    count = wavefield.shape[2]
    columns = wavefield.shape[3]
    chunks = CHUNKS if count % CHUNKS == 0 else 1
    step = count // chunks
    groups = lax.axis_size("gx")
    device = lax.axis_index("gx")
    total_rows = count * groups
    width = columns // groups
    scale = 1.0 / (total_rows * columns)
    base = ref_slowness[0]
    pieces = []
    for c in range(chunks):
        rows = slice(c * step, (c + 1) * step)
        handed = shifted(boundary[0, :, rows], "slab", -1)
        field = lanes_forward(wavefield, handed, source, slowness, reflectivity, base, c * step, step, groups)
        pieces.append(lax.all_to_all(field, "gx", split_axis=0, concat_axis=0, tiled=True))
    if (step % factor_pair(total_rows)[1]) != 0:
        pieces = [jnp.concatenate(pieces, axis=2)]
    freq_row = permuted_freq(jnp.arange(total_rows, dtype=jnp.int32), total_rows)
    freq_col = permuted_freq(device * width + jnp.arange(width, dtype=jnp.int32), columns)
    factor = propagator(freq_row[:, None], freq_col[None, :], base, scale)
    spatial = rows_shift(pieces, jnp.stack(factor))
    back = lax.all_to_all(spatial, "gx", split_axis=0, concat_axis=0, tiled=True)
    return lanes_inverse(back, source)


def solution(mesh):
    return jax.shard_map(
        body,
        mesh=mesh,
        in_specs=(
            P("slab", None, "gx", None),
            P("slab", None, "gx", None),
            P("slab", None, "gx", None),
            P("slab", "gx", None),
            P("slab", "gx", None),
            P("slab"),
        ),
        out_specs=(P("slab", None, "gx", None), P("slab", "gx", None)),
        check_vma=False,
    )
```

```python
from functools import partial
import math

import jax
import jax.numpy as jnp
from jax import lax
from jax.sharding import PartitionSpec as P
from jax.experimental import pallas as pl
from jax.experimental.pallas import tpu as pltpu

OMEGA = 2.5
DEPTH_STEP = 1.0
precise = lax.Precision.HIGHEST


def shifted(block, axis, distance):
    devices = range(lax.axis_size(axis))
    route = [(i - distance, i) for i in devices if i - distance in devices]
    return lax.ppermute(block, axis, route)


def factor_pair(length):
    outer = math.gcd(length, 16)
    return (outer, length // outer)


def dft_table(length, orient):
    position = jnp.arange(length, dtype=jnp.int32)
    product = position[:, None] * position[None, :] % length
    angle = orient * 2.0 * math.pi * product.astype(jnp.float32) / length
    return (jnp.cos(angle), jnp.sin(angle))


def twiddle_table(first, second, length, orient):
    product = (
        jnp.arange(first, dtype=jnp.int32)[:, None]
        * jnp.arange(second, dtype=jnp.int32)[None, :]
        % length
    )
    angle = orient * 2.0 * math.pi * product.astype(jnp.float32) / length
    return (jnp.cos(angle), jnp.sin(angle))


def complex_einsum(form, table, field):
    mixing = partial(jnp.einsum, form, precision=precise)
    return (
        mixing(table[0], field[0]) - mixing(table[1], field[1]),
        mixing(table[0], field[1]) + mixing(table[1], field[0]),
    )


def times_complex(field, factor):
    return (
        field[0] * factor[0] - field[1] * factor[1],
        field[0] * factor[1] + field[1] * factor[0],
    )


def columns_forward(field):
    count, length = field[0].shape
    outer, inner = factor_pair(length)
    shaped = tuple((part.reshape(count, outer, inner) for part in field))
    section = complex_einsum("ka,rab->rkb", dft_table(outer, -1.0), shaped)
    section = times_complex(section, twiddle_table(outer, inner, length, -1.0))
    section = complex_einsum("mb,rkb->rkm", dft_table(inner, -1.0), section)
    return tuple((part.reshape(count, length) for part in section))


def columns_inverse(field):
    count, length = field[0].shape
    outer, inner = factor_pair(length)
    shaped = tuple((part.reshape(count, outer, inner) for part in field))
    section = complex_einsum("mb,rkm->rkb", dft_table(inner, 1.0), shaped)
    section = times_complex(section, twiddle_table(outer, inner, length, 1.0))
    section = complex_einsum("ka,rkb->rab", dft_table(outer, 1.0), section)
    return tuple((part.reshape(count, length) for part in section))


def rows_forward(field):
    length, count = field[0].shape
    outer, inner = factor_pair(length)
    shaped = tuple((part.reshape(outer, inner, count) for part in field))
    section = complex_einsum("ka,abc->kbc", dft_table(outer, -1.0), shaped)
    turned = twiddle_table(outer, inner, length, -1.0)
    section = times_complex(section, (turned[0][:, :, None], turned[1][:, :, None]))
    section = complex_einsum("mb,kbc->kmc", dft_table(inner, -1.0), section)
    return tuple((part.reshape(length, count) for part in section))


def rows_inverse(field):
    length, count = field[0].shape
    outer, inner = factor_pair(length)
    shaped = tuple((part.reshape(outer, inner, count) for part in field))
    section = complex_einsum("mb,kmc->kbc", dft_table(inner, 1.0), shaped)
    turned = twiddle_table(outer, inner, length, 1.0)
    section = times_complex(section, (turned[0][:, :, None], turned[1][:, :, None]))
    section = complex_einsum("ka,kbc->abc", dft_table(outer, 1.0), section)
    return tuple((part.reshape(length, count) for part in section))


def rotate(part, step, count):
    step %= count
    if step == 0:
        return part
    if 4 * step == count:
        return (-part[1], part[0])
    if 2 * step == count:
        return (-part[0], -part[1])
    if 4 * step == 3 * count:
        return (part[1], -part[0])
    cosine = math.cos(2.0 * math.pi * step / count)
    sine = math.sin(2.0 * math.pi * step / count)
    return (part[0] * cosine - part[1] * sine, part[0] * sine + part[1] * cosine)


def fft_slabs(parts, orient):
    count = len(parts)
    if count == 1:
        return list(parts)
    even = fft_slabs(parts[0::2], orient)
    odd = fft_slabs(parts[1::2], orient)
    half = count // 2
    out = [None] * count
    for k in range(half):
        turned = rotate(odd[k], orient * k, count)
        out[k] = (even[k][0] + turned[0], even[k][1] + turned[1])
        out[k + half] = (even[k][0] - turned[0], even[k][1] - turned[1])
    return out


def stacked_matmul(stacked, real, imag):
    size = real.shape[1]
    rows = stacked.shape[0] // 2
    both = jnp.concatenate([real, imag], axis=1)
    prod = jnp.dot(stacked, both, precision=lax.Precision.HIGH, preferred_element_type=jnp.float32)
    return (
        prod[:rows, :size] - prod[rows:, size:],
        prod[:rows, size:] + prod[rows:, :size],
    )


def rows_kernel(*refs):
    x_refs = refs[:-4]
    p_ref, w_ref, tw_ref, o_ref = refs[-4:]
    outer = tw_ref.shape[1]
    inner = tw_ref.shape[2]
    step = x_refs[0].shape[2]
    count = step * len(x_refs)

    def place(a):
        return (a * inner) // count, slice((a * inner) % count, (a * inner) % count + inner)

    slabs = []
    for a in range(outer):
        origin = (a * inner) // count
        part = x_refs[((a * inner) % count) // step]
        first = (a * inner) % step
        slabs.append((part[origin, 0, first:first + inner, :], part[origin, 1, first:first + inner, :]))
    spec = fft_slabs(slabs, -1)
    wr = w_ref[0]
    wi = w_ref[1]
    forward = jnp.concatenate([wr, wi], axis=0)
    backward = jnp.concatenate([wr, -wi], axis=0)
    outs = []
    for k in range(outer):
        zr, zi = spec[k]
        tr = tw_ref[0, k]
        ti = tw_ref[1, k]
        zr, zi = zr * tr - zi * ti, zr * ti + zi * tr
        yr, yi = stacked_matmul(forward, zr, zi)
        pr = p_ref[0, k * inner:(k + 1) * inner, :]
        pi = p_ref[1, k * inner:(k + 1) * inner, :]
        yr, yi = yr * pr - yi * pi, yr * pi + yi * pr
        sr, si = stacked_matmul(backward, yr, yi)
        outs.append((sr * tr + si * ti, si * tr - sr * ti))
    res = fft_slabs(outs, 1)
    for a in range(outer):
        origin, rows = place(a)
        o_ref[origin, 0, rows, :] = res[a][0]
        o_ref[origin, 1, rows, :] = res[a][1]


def rows_shift(turned, factor):
    groups, _, step, width = turned[0].shape
    length = groups * step * len(turned)
    outer, inner = factor_pair(length)
    block = min(width, 128)
    table = dft_table(inner, -1.0)
    turn = twiddle_table(outer, inner, length, -1.0)
    table = jnp.stack(table)
    turn = jnp.stack(turn)[..., None]
    field_spec = pl.BlockSpec((groups, 2, step, block), lambda j: (0, 0, 0, j))
    return pl.pallas_call(
        rows_kernel,
        grid=(width // block,),
        in_specs=[field_spec] * len(turned) + [
            pl.BlockSpec((2, length, block), lambda j: (0, 0, j)),
            pl.BlockSpec((2, inner, inner), lambda j: (0, 0, 0)),
            pl.BlockSpec((2, outer, inner, 1), lambda j: (0, 0, 0, 0)),
        ],
        out_specs=pl.BlockSpec((groups, 2, step * len(turned), block), lambda j: (0, 0, 0, j)),
        out_shape=jax.ShapeDtypeStruct((groups, 2, step * len(turned), width), jnp.float32),
    )(*turned, factor, table, turn)


def lanes_forward_kernel(base_ref, wave_ref, hand_ref, src_ref, slow_ref, refl_ref, w_ref, tw_ref, o_ref):
    outer = tw_ref.shape[1]
    inner = tw_ref.shape[2]
    base = base_ref[0, 0]
    gain = OMEGA * OMEGA * refl_ref[0]
    real_in = (
        wave_ref[0, 0].astype(jnp.float32)
        + hand_ref[0].astype(jnp.float32)
        + gain * src_ref[0, 0].astype(jnp.float32)
    )
    imag_in = (
        wave_ref[0, 1].astype(jnp.float32)
        + hand_ref[1].astype(jnp.float32)
        + gain * src_ref[0, 1].astype(jnp.float32)
    )
    angle = -OMEGA * (slow_ref[0] - base) * DEPTH_STEP
    cosine = jnp.cos(angle)
    sine = jnp.sin(angle)
    lensed_real = real_in * cosine - imag_in * sine
    lensed_imag = real_in * sine + imag_in * cosine
    slabs = [
        (lensed_real[:, a * inner:(a + 1) * inner], lensed_imag[:, a * inner:(a + 1) * inner])
        for a in range(outer)
    ]
    spec = fft_slabs(slabs, -1)
    both = jnp.concatenate([w_ref[0], w_ref[1]], axis=1)
    count = lensed_real.shape[0]
    for k in range(outer):
        zr, zi = spec[k]
        tr = tw_ref[0, k:k + 1, :]
        ti = tw_ref[1, k:k + 1, :]
        zr, zi = zr * tr - zi * ti, zr * ti + zi * tr
        prod = jnp.dot(
            jnp.concatenate([zr, zi], axis=0), both,
            precision=lax.Precision.HIGH, preferred_element_type=jnp.float32,
        )
        width = o_ref.shape[3]
        dest = (k * inner) // width
        lanes = slice((k * inner) % width, (k * inner) % width + inner)
        o_ref[dest, 0, :, lanes] = prod[:count, :inner] - prod[count:, inner:]
        o_ref[dest, 1, :, lanes] = prod[:count, inner:] + prod[count:, :inner]


def lanes_inverse_kernel(x_ref, src_ref, w_ref, tw_ref, ext_ref, img_ref):
    outer = tw_ref.shape[1]
    inner = tw_ref.shape[2]
    count = x_ref.shape[2]
    both = jnp.concatenate([w_ref[0], -w_ref[1]], axis=1)
    outs = []
    for k in range(outer):
        width = x_ref.shape[3]
        origin = (k * inner) // width
        lanes = slice((k * inner) % width, (k * inner) % width + inner)
        yr = x_ref[origin, 0, :, lanes]
        yi = x_ref[origin, 1, :, lanes]
        prod = jnp.dot(
            jnp.concatenate([yr, yi], axis=0), both,
            precision=lax.Precision.HIGH, preferred_element_type=jnp.float32,
        )
        sr = prod[:count, :inner] - prod[count:, inner:]
        si = prod[:count, inner:] + prod[count:, :inner]
        tr = tw_ref[0, k:k + 1, :]
        ti = tw_ref[1, k:k + 1, :]
        outs.append((sr * tr + si * ti, si * tr - sr * ti))
    res = fft_slabs(outs, 1)
    for a in range(outer):
        out_real, out_imag = res[a]
        lanes = slice(a * inner, (a + 1) * inner)
        ext_ref[0, 0, :, lanes] = out_real.astype(ext_ref.dtype)
        ext_ref[0, 1, :, lanes] = out_imag.astype(ext_ref.dtype)
        img_ref[0, :, lanes] = (
            src_ref[0, 0, :, lanes].astype(jnp.float32) * out_real
            + src_ref[0, 1, :, lanes].astype(jnp.float32) * out_imag
        )


def lane_tables(length):
    outer, inner = factor_pair(length)
    table = jnp.stack(dft_table(inner, -1.0))
    turn = jnp.stack(twiddle_table(outer, inner, length, -1.0))
    return outer, inner, table, turn


def lanes_forward(wavefield, handed, source, slowness, reflectivity, base, first, step, groups):
    length = wavefield.shape[3]
    outer, inner, table, turn = lane_tables(length)
    block = min(step, 32)
    offset = first // block
    quad = lambda i: (0, 0, offset + i, 0)
    flat = lambda i: (0, offset + i, 0)
    return pl.pallas_call(
        lanes_forward_kernel,
        grid=(step // block,),
        in_specs=[
            pl.BlockSpec(memory_space=pltpu.SMEM),
            pl.BlockSpec((1, 2, block, length), quad),
            pl.BlockSpec((2, block, length), lambda i: (0, i, 0)),
            pl.BlockSpec((1, 2, block, length), quad),
            pl.BlockSpec((1, block, length), flat),
            pl.BlockSpec((1, block, length), flat),
            pl.BlockSpec((2, inner, inner), lambda i: (0, 0, 0)),
            pl.BlockSpec((2, outer, inner), lambda i: (0, 0, 0)),
        ],
        out_specs=pl.BlockSpec((groups, 2, block, length // groups), lambda i: (0, 0, i, 0)),
        out_shape=jax.ShapeDtypeStruct((groups, 2, step, length // groups), jnp.float32),
    )(base.reshape(1, 1), wavefield, handed, source, slowness, reflectivity, table, turn)


def lanes_inverse(back, source):
    groups, _, step, width = back.shape
    length = groups * width
    outer, inner, table, turn = lane_tables(length)
    block = min(step, 32)
    return pl.pallas_call(
        lanes_inverse_kernel,
        grid=(step // block,),
        in_specs=[
            pl.BlockSpec((groups, 2, block, width), lambda i: (0, 0, i, 0)),
            pl.BlockSpec((1, 2, block, length), lambda i: (0, 0, i, 0)),
            pl.BlockSpec((2, inner, inner), lambda i: (0, 0, 0)),
            pl.BlockSpec((2, outer, inner), lambda i: (0, 0, 0)),
        ],
        out_specs=[
            pl.BlockSpec((1, 2, block, length), lambda i: (0, 0, i, 0)),
            pl.BlockSpec((1, block, length), lambda i: (0, i, 0)),
        ],
        out_shape=[
            jax.ShapeDtypeStruct((1, 2, step, length), jnp.bfloat16),
            jax.ShapeDtypeStruct((1, step, length), jnp.float32),
        ],
    )(back, source, table, turn)


def signed_freq(index, length):
    signed = jnp.where(index < length // 2, index, index - length)
    return signed.astype(jnp.float32) * (2.0 * math.pi / length)


def permuted_freq(position, length):
    outer, inner = factor_pair(length)
    index = position // inner + outer * (position % inner)
    return signed_freq(index, length)


def propagator(freq_row, freq_col, base, scale):
    kz_square = (OMEGA * base) ** 2 - freq_row * freq_row - freq_col * freq_col
    root = jnp.sqrt(jnp.abs(kz_square))
    upward = kz_square >= 0.0
    real_part = jnp.where(upward, jnp.cos(root * DEPTH_STEP), jnp.exp(-root * DEPTH_STEP))
    imag_part = jnp.where(upward, -jnp.sin(root * DEPTH_STEP), jnp.zeros_like(root))
    return (real_part * scale, imag_part * scale)


CHUNKS = 2


def lens_rows(wave, handed, source, slow, refl, base):
    wave = wave.astype(jnp.float32)
    handed = handed.astype(jnp.float32)
    source = source.astype(jnp.float32)
    real_in = wave[0] + handed[0] + OMEGA * OMEGA * refl * source[0]
    imag_in = wave[1] + handed[1] + OMEGA * OMEGA * refl * source[1]
    angle = -OMEGA * (slow - base) * DEPTH_STEP
    cosine = jnp.cos(angle)
    sine = jnp.sin(angle)
    return (real_in * cosine - imag_in * sine, real_in * sine + imag_in * cosine)


def body(wavefield, boundary, source, slowness, reflectivity, ref_slowness):
    count = wavefield.shape[2]
    columns = wavefield.shape[3]
    chunks = CHUNKS if count % CHUNKS == 0 else 1
    step = count // chunks
    groups = lax.axis_size("gx")
    device = lax.axis_index("gx")
    total_rows = count * groups
    width = columns // groups
    scale = 1.0 / (total_rows * columns)
    base = ref_slowness[0]
    pieces = []
    for c in range(chunks):
        rows = slice(c * step, (c + 1) * step)
        handed = shifted(boundary[0, :, rows], "slab", -1)
        field = lanes_forward(wavefield, handed, source, slowness, reflectivity, base, c * step, step, groups)
        pieces.append(lax.all_to_all(field, "gx", split_axis=0, concat_axis=0, tiled=True))
    if (step % factor_pair(total_rows)[1]) != 0:
        pieces = [jnp.concatenate(pieces, axis=2)]
    freq_row = permuted_freq(jnp.arange(total_rows, dtype=jnp.int32), total_rows)
    freq_col = permuted_freq(device * width + jnp.arange(width, dtype=jnp.int32), columns)
    factor = propagator(freq_row[:, None], freq_col[None, :], base, scale)
    spatial = rows_shift(pieces, jnp.stack(factor))
    back = lax.all_to_all(spatial, "gx", split_axis=0, concat_axis=0, tiled=True)
    return lanes_inverse(back, source.astype(jnp.float32))


def solution(mesh):
    return jax.shard_map(
        body,
        mesh=mesh,
        in_specs=(
            P("slab", None, "gx", None),
            P("slab", None, "gx", None),
            P("slab", None, "gx", None),
            P("slab", "gx", None),
            P("slab", "gx", None),
            P("slab"),
        ),
        out_specs=(P("slab", None, "gx", None), P("slab", "gx", None)),
        check_vma=False,
    )
```

```python
from functools import partial
import math

import jax
import jax.numpy as jnp
from jax import lax
from jax.sharding import PartitionSpec as P
from jax.experimental import pallas as pl
from jax.experimental.pallas import tpu as pltpu

OMEGA = 2.5
DEPTH_STEP = 1.0
precise = lax.Precision.HIGHEST


def shifted(block, axis, distance):
    devices = range(lax.axis_size(axis))
    route = [(i - distance, i) for i in devices if i - distance in devices]
    return lax.ppermute(block, axis, route)


def factor_pair(length):
    outer = math.gcd(length, 16)
    return (outer, length // outer)


def dft_table(length, orient):
    position = jnp.arange(length, dtype=jnp.int32)
    product = position[:, None] * position[None, :] % length
    angle = orient * 2.0 * math.pi * product.astype(jnp.float32) / length
    return (jnp.cos(angle), jnp.sin(angle))


def twiddle_table(first, second, length, orient):
    product = (
        jnp.arange(first, dtype=jnp.int32)[:, None]
        * jnp.arange(second, dtype=jnp.int32)[None, :]
        % length
    )
    angle = orient * 2.0 * math.pi * product.astype(jnp.float32) / length
    return (jnp.cos(angle), jnp.sin(angle))


def complex_einsum(form, table, field):
    mixing = partial(jnp.einsum, form, precision=precise)
    return (
        mixing(table[0], field[0]) - mixing(table[1], field[1]),
        mixing(table[0], field[1]) + mixing(table[1], field[0]),
    )


def times_complex(field, factor):
    return (
        field[0] * factor[0] - field[1] * factor[1],
        field[0] * factor[1] + field[1] * factor[0],
    )


def columns_forward(field):
    count, length = field[0].shape
    outer, inner = factor_pair(length)
    shaped = tuple((part.reshape(count, outer, inner) for part in field))
    section = complex_einsum("ka,rab->rkb", dft_table(outer, -1.0), shaped)
    section = times_complex(section, twiddle_table(outer, inner, length, -1.0))
    section = complex_einsum("mb,rkb->rkm", dft_table(inner, -1.0), section)
    return tuple((part.reshape(count, length) for part in section))


def columns_inverse(field):
    count, length = field[0].shape
    outer, inner = factor_pair(length)
    shaped = tuple((part.reshape(count, outer, inner) for part in field))
    section = complex_einsum("mb,rkm->rkb", dft_table(inner, 1.0), shaped)
    section = times_complex(section, twiddle_table(outer, inner, length, 1.0))
    section = complex_einsum("ka,rkb->rab", dft_table(outer, 1.0), section)
    return tuple((part.reshape(count, length) for part in section))


def rows_forward(field):
    length, count = field[0].shape
    outer, inner = factor_pair(length)
    shaped = tuple((part.reshape(outer, inner, count) for part in field))
    section = complex_einsum("ka,abc->kbc", dft_table(outer, -1.0), shaped)
    turned = twiddle_table(outer, inner, length, -1.0)
    section = times_complex(section, (turned[0][:, :, None], turned[1][:, :, None]))
    section = complex_einsum("mb,kbc->kmc", dft_table(inner, -1.0), section)
    return tuple((part.reshape(length, count) for part in section))


def rows_inverse(field):
    length, count = field[0].shape
    outer, inner = factor_pair(length)
    shaped = tuple((part.reshape(outer, inner, count) for part in field))
    section = complex_einsum("mb,kmc->kbc", dft_table(inner, 1.0), shaped)
    turned = twiddle_table(outer, inner, length, 1.0)
    section = times_complex(section, (turned[0][:, :, None], turned[1][:, :, None]))
    section = complex_einsum("ka,kbc->abc", dft_table(outer, 1.0), section)
    return tuple((part.reshape(length, count) for part in section))


def rotate(part, step, count):
    step %= count
    if step == 0:
        return part
    if 4 * step == count:
        return (-part[1], part[0])
    if 2 * step == count:
        return (-part[0], -part[1])
    if 4 * step == 3 * count:
        return (part[1], -part[0])
    cosine = math.cos(2.0 * math.pi * step / count)
    sine = math.sin(2.0 * math.pi * step / count)
    return (part[0] * cosine - part[1] * sine, part[0] * sine + part[1] * cosine)


def fft_slabs(parts, orient):
    count = len(parts)
    if count == 1:
        return list(parts)
    even = fft_slabs(parts[0::2], orient)
    odd = fft_slabs(parts[1::2], orient)
    half = count // 2
    out = [None] * count
    for k in range(half):
        turned = rotate(odd[k], orient * k, count)
        out[k] = (even[k][0] + turned[0], even[k][1] + turned[1])
        out[k + half] = (even[k][0] - turned[0], even[k][1] - turned[1])
    return out


def stacked_matmul(stacked, real, imag):
    size = real.shape[1]
    rows = stacked.shape[0] // 2
    both = jnp.concatenate([real, imag], axis=1)
    prod = jnp.dot(stacked, both, precision=lax.Precision.HIGH, preferred_element_type=jnp.float32)
    return (
        prod[:rows, :size] - prod[rows:, size:],
        prod[:rows, size:] + prod[rows:, :size],
    )


def rows_kernel(*refs):
    x_refs = refs[:-4]
    p_ref, w_ref, tw_ref, o_ref = refs[-4:]
    outer = tw_ref.shape[1]
    inner = tw_ref.shape[2]
    count = sum(ref.shape[2] for ref in x_refs)

    def place(a):
        return (a * inner) // count, slice((a * inner) % count, (a * inner) % count + inner)

    sizes = [ref.shape[2] for ref in x_refs]
    starts = [sum(sizes[:i]) for i in range(len(sizes))]
    slabs = []
    for a in range(outer):
        origin = (a * inner) // count
        low = (a * inner) % count
        pieces = []
        for ref, start, size in zip(x_refs, starts, sizes):
            top = min(low + inner, start + size)
            bottom = max(low, start)
            if top > bottom:
                pieces.append((ref[origin, 0, bottom - start:top - start, :], ref[origin, 1, bottom - start:top - start, :]))
        if len(pieces) == 1:
            slabs.append(pieces[0])
        else:
            slabs.append((
                jnp.concatenate([p[0] for p in pieces], axis=0),
                jnp.concatenate([p[1] for p in pieces], axis=0),
            ))
    spec = fft_slabs(slabs, -1)
    wr = w_ref[0]
    wi = w_ref[1]
    forward = jnp.concatenate([wr, wi], axis=0)
    backward = jnp.concatenate([wr, -wi], axis=0)
    outs = []
    for k in range(outer):
        zr, zi = spec[k]
        tr = tw_ref[0, k]
        ti = tw_ref[1, k]
        zr, zi = zr * tr - zi * ti, zr * ti + zi * tr
        yr, yi = stacked_matmul(forward, zr, zi)
        pr = p_ref[0, k * inner:(k + 1) * inner, :]
        pi = p_ref[1, k * inner:(k + 1) * inner, :]
        yr, yi = yr * pr - yi * pi, yr * pi + yi * pr
        sr, si = stacked_matmul(backward, yr, yi)
        outs.append((sr * tr + si * ti, si * tr - sr * ti))
    res = fft_slabs(outs, 1)
    for a in range(outer):
        origin, rows = place(a)
        o_ref[origin, 0, rows, :] = res[a][0]
        o_ref[origin, 1, rows, :] = res[a][1]


def rows_shift(turned, factor):
    groups, _, _, width = turned[0].shape
    count = sum(piece.shape[2] for piece in turned)
    length = groups * count
    outer, inner = factor_pair(length)
    block = min(width, 128)
    table = dft_table(inner, -1.0)
    turn = twiddle_table(outer, inner, length, -1.0)
    table = jnp.stack(table)
    turn = jnp.stack(turn)[..., None]
    return pl.pallas_call(
        rows_kernel,
        grid=(width // block,),
        in_specs=[pl.BlockSpec((groups, 2, piece.shape[2], block), lambda j: (0, 0, 0, j)) for piece in turned] + [
            pl.BlockSpec((2, length, block), lambda j: (0, 0, j)),
            pl.BlockSpec((2, inner, inner), lambda j: (0, 0, 0)),
            pl.BlockSpec((2, outer, inner, 1), lambda j: (0, 0, 0, 0)),
        ],
        out_specs=pl.BlockSpec((groups, 2, count, block), lambda j: (0, 0, 0, j)),
        out_shape=jax.ShapeDtypeStruct((groups, 2, count, width), jnp.float32),
    )(*turned, factor, table, turn)


def lanes_forward_kernel(base_ref, wave_ref, hand_ref, src_ref, slow_ref, refl_ref, w_ref, tw_ref, o_ref):
    outer = tw_ref.shape[1]
    inner = tw_ref.shape[2]
    base = base_ref[0, 0]
    gain = OMEGA * OMEGA * refl_ref[0]
    real_in = (
        wave_ref[0, 0].astype(jnp.float32)
        + hand_ref[0].astype(jnp.float32)
        + gain * src_ref[0, 0].astype(jnp.float32)
    )
    imag_in = (
        wave_ref[0, 1].astype(jnp.float32)
        + hand_ref[1].astype(jnp.float32)
        + gain * src_ref[0, 1].astype(jnp.float32)
    )
    angle = -OMEGA * (slow_ref[0] - base) * DEPTH_STEP
    cosine = jnp.cos(angle)
    sine = jnp.sin(angle)
    lensed_real = real_in * cosine - imag_in * sine
    lensed_imag = real_in * sine + imag_in * cosine
    slabs = [
        (lensed_real[:, a * inner:(a + 1) * inner], lensed_imag[:, a * inner:(a + 1) * inner])
        for a in range(outer)
    ]
    spec = fft_slabs(slabs, -1)
    both = jnp.concatenate([w_ref[0], w_ref[1]], axis=1)
    count = lensed_real.shape[0]
    for k in range(outer):
        zr, zi = spec[k]
        tr = tw_ref[0, k:k + 1, :]
        ti = tw_ref[1, k:k + 1, :]
        zr, zi = zr * tr - zi * ti, zr * ti + zi * tr
        prod = jnp.dot(
            jnp.concatenate([zr, zi], axis=0), both,
            precision=lax.Precision.HIGH, preferred_element_type=jnp.float32,
        )
        width = o_ref.shape[3]
        dest = (k * inner) // width
        lanes = slice((k * inner) % width, (k * inner) % width + inner)
        o_ref[dest, 0, :, lanes] = prod[:count, :inner] - prod[count:, inner:]
        o_ref[dest, 1, :, lanes] = prod[:count, inner:] + prod[count:, :inner]


def lanes_inverse_kernel(x_ref, src_ref, w_ref, tw_ref, ext_ref, img_ref):
    outer = tw_ref.shape[1]
    inner = tw_ref.shape[2]
    count = x_ref.shape[2]
    both = jnp.concatenate([w_ref[0], -w_ref[1]], axis=1)
    outs = []
    for k in range(outer):
        width = x_ref.shape[3]
        origin = (k * inner) // width
        lanes = slice((k * inner) % width, (k * inner) % width + inner)
        yr = x_ref[origin, 0, :, lanes]
        yi = x_ref[origin, 1, :, lanes]
        prod = jnp.dot(
            jnp.concatenate([yr, yi], axis=0), both,
            precision=lax.Precision.HIGH, preferred_element_type=jnp.float32,
        )
        sr = prod[:count, :inner] - prod[count:, inner:]
        si = prod[:count, inner:] + prod[count:, :inner]
        tr = tw_ref[0, k:k + 1, :]
        ti = tw_ref[1, k:k + 1, :]
        outs.append((sr * tr + si * ti, si * tr - sr * ti))
    res = fft_slabs(outs, 1)
    for a in range(outer):
        out_real, out_imag = res[a]
        lanes = slice(a * inner, (a + 1) * inner)
        ext_ref[0, 0, :, lanes] = out_real.astype(ext_ref.dtype)
        ext_ref[0, 1, :, lanes] = out_imag.astype(ext_ref.dtype)
        img_ref[0, :, lanes] = (
            src_ref[0, 0, :, lanes].astype(jnp.float32) * out_real
            + src_ref[0, 1, :, lanes].astype(jnp.float32) * out_imag
        )


def lane_tables(length):
    outer, inner = factor_pair(length)
    table = jnp.stack(dft_table(inner, -1.0))
    turn = jnp.stack(twiddle_table(outer, inner, length, -1.0))
    return outer, inner, table, turn


def lanes_forward(wavefield, handed, source, slowness, reflectivity, base, first, step, groups):
    length = wavefield.shape[3]
    outer, inner, table, turn = lane_tables(length)
    block = min(step, 32)
    offset = first // block
    quad = lambda i: (0, 0, offset + i, 0)
    flat = lambda i: (0, offset + i, 0)
    return pl.pallas_call(
        lanes_forward_kernel,
        grid=(step // block,),
        in_specs=[
            pl.BlockSpec(memory_space=pltpu.SMEM),
            pl.BlockSpec((1, 2, block, length), quad),
            pl.BlockSpec((2, block, length), lambda i: (0, i, 0)),
            pl.BlockSpec((1, 2, block, length), quad),
            pl.BlockSpec((1, block, length), flat),
            pl.BlockSpec((1, block, length), flat),
            pl.BlockSpec((2, inner, inner), lambda i: (0, 0, 0)),
            pl.BlockSpec((2, outer, inner), lambda i: (0, 0, 0)),
        ],
        out_specs=pl.BlockSpec((groups, 2, block, length // groups), lambda i: (0, 0, i, 0)),
        out_shape=jax.ShapeDtypeStruct((groups, 2, step, length // groups), jnp.float32),
    )(base.reshape(1, 1), wavefield, handed, source, slowness, reflectivity, table, turn)


def lanes_inverse(back, source):
    groups, _, step, width = back.shape
    length = groups * width
    outer, inner, table, turn = lane_tables(length)
    block = min(step, 32)
    return pl.pallas_call(
        lanes_inverse_kernel,
        grid=(step // block,),
        in_specs=[
            pl.BlockSpec((groups, 2, block, width), lambda i: (0, 0, i, 0)),
            pl.BlockSpec((1, 2, block, length), lambda i: (0, 0, i, 0)),
            pl.BlockSpec((2, inner, inner), lambda i: (0, 0, 0)),
            pl.BlockSpec((2, outer, inner), lambda i: (0, 0, 0)),
        ],
        out_specs=[
            pl.BlockSpec((1, 2, block, length), lambda i: (0, 0, i, 0)),
            pl.BlockSpec((1, block, length), lambda i: (0, i, 0)),
        ],
        out_shape=[
            jax.ShapeDtypeStruct((1, 2, step, length), jnp.bfloat16),
            jax.ShapeDtypeStruct((1, step, length), jnp.float32),
        ],
    )(back, source, table, turn)


def signed_freq(index, length):
    signed = jnp.where(index < length // 2, index, index - length)
    return signed.astype(jnp.float32) * (2.0 * math.pi / length)


def permuted_freq(position, length):
    outer, inner = factor_pair(length)
    index = position // inner + outer * (position % inner)
    return signed_freq(index, length)


def propagator(freq_row, freq_col, base, scale):
    kz_square = (OMEGA * base) ** 2 - freq_row * freq_row - freq_col * freq_col
    root = jnp.sqrt(jnp.abs(kz_square))
    upward = kz_square >= 0.0
    real_part = jnp.where(upward, jnp.cos(root * DEPTH_STEP), jnp.exp(-root * DEPTH_STEP))
    imag_part = jnp.where(upward, -jnp.sin(root * DEPTH_STEP), jnp.zeros_like(root))
    return (real_part * scale, imag_part * scale)


def lens_rows(wave, handed, source, slow, refl, base):
    wave = wave.astype(jnp.float32)
    handed = handed.astype(jnp.float32)
    source = source.astype(jnp.float32)
    real_in = wave[0] + handed[0] + OMEGA * OMEGA * refl * source[0]
    imag_in = wave[1] + handed[1] + OMEGA * OMEGA * refl * source[1]
    angle = -OMEGA * (slow - base) * DEPTH_STEP
    cosine = jnp.cos(angle)
    sine = jnp.sin(angle)
    return (real_in * cosine - imag_in * sine, real_in * sine + imag_in * cosine)


def body(wavefield, boundary, source, slowness, reflectivity, ref_slowness):
    count = wavefield.shape[2]
    columns = wavefield.shape[3]
    eighth = count // 8
    if count % 8 == 0 and eighth % 8 == 0:
        bounds = [0, eighth, 3 * eighth, count]
    else:
        bounds = [0, count]
    groups = lax.axis_size("gx")
    device = lax.axis_index("gx")
    total_rows = count * groups
    width = columns // groups
    scale = 1.0 / (total_rows * columns)
    base = ref_slowness[0]
    pieces = []
    for first, last in zip(bounds[:-1], bounds[1:]):
        handed = shifted(boundary[0, :, first:last], "slab", -1)
        field = lanes_forward(wavefield, handed, source, slowness, reflectivity, base, first, last - first, groups)
        pieces.append(lax.all_to_all(field, "gx", split_axis=0, concat_axis=0, tiled=True))
    freq_row = permuted_freq(jnp.arange(total_rows, dtype=jnp.int32), total_rows)
    freq_col = permuted_freq(device * width + jnp.arange(width, dtype=jnp.int32), columns)
    factor = propagator(freq_row[:, None], freq_col[None, :], base, scale)
    spatial = rows_shift(pieces, jnp.stack(factor))
    back = lax.all_to_all(spatial, "gx", split_axis=0, concat_axis=0, tiled=True)
    return lanes_inverse(back, source)


def solution(mesh):
    return jax.shard_map(
        body,
        mesh=mesh,
        in_specs=(
            P("slab", None, "gx", None),
            P("slab", None, "gx", None),
            P("slab", None, "gx", None),
            P("slab", "gx", None),
            P("slab", "gx", None),
            P("slab"),
        ),
        out_specs=(P("slab", None, "gx", None), P("slab", "gx", None)),
        check_vma=False,
    )
```

```python
from functools import partial
import math

import jax
import jax.numpy as jnp
from jax import lax
from jax.sharding import PartitionSpec as P
from jax.experimental import pallas as pl
from jax.experimental.pallas import tpu as pltpu

OMEGA = 2.5
DEPTH_STEP = 1.0
precise = lax.Precision.HIGHEST


def shifted(block, axis, distance):
    devices = range(lax.axis_size(axis))
    route = [(i - distance, i) for i in devices if i - distance in devices]
    return lax.ppermute(block, axis, route)


def factor_pair(length):
    outer = math.gcd(length, 16)
    return (outer, length // outer)


def dft_table(length, orient):
    position = jnp.arange(length, dtype=jnp.int32)
    product = position[:, None] * position[None, :] % length
    angle = orient * 2.0 * math.pi * product.astype(jnp.float32) / length
    return (jnp.cos(angle), jnp.sin(angle))


def twiddle_table(first, second, length, orient):
    product = (
        jnp.arange(first, dtype=jnp.int32)[:, None]
        * jnp.arange(second, dtype=jnp.int32)[None, :]
        % length
    )
    angle = orient * 2.0 * math.pi * product.astype(jnp.float32) / length
    return (jnp.cos(angle), jnp.sin(angle))


def complex_einsum(form, table, field):
    mixing = partial(jnp.einsum, form, precision=precise)
    return (
        mixing(table[0], field[0]) - mixing(table[1], field[1]),
        mixing(table[0], field[1]) + mixing(table[1], field[0]),
    )


def times_complex(field, factor):
    return (
        field[0] * factor[0] - field[1] * factor[1],
        field[0] * factor[1] + field[1] * factor[0],
    )


def columns_forward(field):
    count, length = field[0].shape
    outer, inner = factor_pair(length)
    shaped = tuple((part.reshape(count, outer, inner) for part in field))
    section = complex_einsum("ka,rab->rkb", dft_table(outer, -1.0), shaped)
    section = times_complex(section, twiddle_table(outer, inner, length, -1.0))
    section = complex_einsum("mb,rkb->rkm", dft_table(inner, -1.0), section)
    return tuple((part.reshape(count, length) for part in section))


def columns_inverse(field):
    count, length = field[0].shape
    outer, inner = factor_pair(length)
    shaped = tuple((part.reshape(count, outer, inner) for part in field))
    section = complex_einsum("mb,rkm->rkb", dft_table(inner, 1.0), shaped)
    section = times_complex(section, twiddle_table(outer, inner, length, 1.0))
    section = complex_einsum("ka,rkb->rab", dft_table(outer, 1.0), section)
    return tuple((part.reshape(count, length) for part in section))


def rows_forward(field):
    length, count = field[0].shape
    outer, inner = factor_pair(length)
    shaped = tuple((part.reshape(outer, inner, count) for part in field))
    section = complex_einsum("ka,abc->kbc", dft_table(outer, -1.0), shaped)
    turned = twiddle_table(outer, inner, length, -1.0)
    section = times_complex(section, (turned[0][:, :, None], turned[1][:, :, None]))
    section = complex_einsum("mb,kbc->kmc", dft_table(inner, -1.0), section)
    return tuple((part.reshape(length, count) for part in section))


def rows_inverse(field):
    length, count = field[0].shape
    outer, inner = factor_pair(length)
    shaped = tuple((part.reshape(outer, inner, count) for part in field))
    section = complex_einsum("mb,kmc->kbc", dft_table(inner, 1.0), shaped)
    turned = twiddle_table(outer, inner, length, 1.0)
    section = times_complex(section, (turned[0][:, :, None], turned[1][:, :, None]))
    section = complex_einsum("ka,kbc->abc", dft_table(outer, 1.0), section)
    return tuple((part.reshape(length, count) for part in section))


def rotate(part, step, count):
    step %= count
    if step == 0:
        return part
    if 4 * step == count:
        return (-part[1], part[0])
    if 2 * step == count:
        return (-part[0], -part[1])
    if 4 * step == 3 * count:
        return (part[1], -part[0])
    cosine = math.cos(2.0 * math.pi * step / count)
    sine = math.sin(2.0 * math.pi * step / count)
    return (part[0] * cosine - part[1] * sine, part[0] * sine + part[1] * cosine)


def fft_slabs(parts, orient):
    count = len(parts)
    if count == 1:
        return list(parts)
    even = fft_slabs(parts[0::2], orient)
    odd = fft_slabs(parts[1::2], orient)
    half = count // 2
    out = [None] * count
    for k in range(half):
        turned = rotate(odd[k], orient * k, count)
        out[k] = (even[k][0] + turned[0], even[k][1] + turned[1])
        out[k + half] = (even[k][0] - turned[0], even[k][1] - turned[1])
    return out


def stacked_matmul(stacked, real, imag):
    size = real.shape[1]
    rows = stacked.shape[0] // 2
    both = jnp.concatenate([real, imag], axis=1)
    prod = jnp.dot(stacked, both, precision=lax.Precision.HIGH, preferred_element_type=jnp.float32)
    return (
        prod[:rows, :size] - prod[rows:, size:],
        prod[:rows, size:] + prod[rows:, :size],
    )


def rows_kernel(*refs):
    x_refs = refs[:-4]
    p_ref, w_ref, tw_ref, o_ref = refs[-4:]
    outer = tw_ref.shape[1]
    inner = tw_ref.shape[2]
    count = sum(ref.shape[2] for ref in x_refs)

    def place(a):
        return (a * inner) // count, slice((a * inner) % count, (a * inner) % count + inner)

    sizes = [ref.shape[2] for ref in x_refs]
    starts = [sum(sizes[:i]) for i in range(len(sizes))]
    slabs = []
    for a in range(outer):
        origin = (a * inner) // count
        low = (a * inner) % count
        pieces = []
        for ref, start, size in zip(x_refs, starts, sizes):
            top = min(low + inner, start + size)
            bottom = max(low, start)
            if top > bottom:
                pieces.append((ref[origin, 0, bottom - start:top - start, :], ref[origin, 1, bottom - start:top - start, :]))
        if len(pieces) == 1:
            slabs.append(pieces[0])
        else:
            slabs.append((
                jnp.concatenate([p[0] for p in pieces], axis=0),
                jnp.concatenate([p[1] for p in pieces], axis=0),
            ))
    spec = fft_slabs(slabs, -1)
    wr = w_ref[0]
    wi = w_ref[1]
    forward = jnp.concatenate([wr, wi], axis=0)
    backward = jnp.concatenate([wr, -wi], axis=0)
    outs = []
    for k in range(outer):
        zr, zi = spec[k]
        tr = tw_ref[0, k]
        ti = tw_ref[1, k]
        zr, zi = zr * tr - zi * ti, zr * ti + zi * tr
        yr, yi = stacked_matmul(forward, zr, zi)
        pr = p_ref[0, k * inner:(k + 1) * inner, :]
        pi = p_ref[1, k * inner:(k + 1) * inner, :]
        yr, yi = yr * pr - yi * pi, yr * pi + yi * pr
        sr, si = stacked_matmul(backward, yr, yi)
        outs.append((sr * tr + si * ti, si * tr - sr * ti))
    res = fft_slabs(outs, 1)
    for a in range(outer):
        origin, rows = place(a)
        o_ref[origin, 0, rows, :] = res[a][0]
        o_ref[origin, 1, rows, :] = res[a][1]


def rows_shift(turned, factor):
    groups, _, _, width = turned[0].shape
    count = sum(piece.shape[2] for piece in turned)
    length = groups * count
    outer, inner = factor_pair(length)
    block = min(width, 128)
    table = dft_table(inner, -1.0)
    turn = twiddle_table(outer, inner, length, -1.0)
    table = jnp.stack(table)
    turn = jnp.stack(turn)[..., None]
    return pl.pallas_call(
        rows_kernel,
        grid=(width // block,),
        in_specs=[pl.BlockSpec((groups, 2, piece.shape[2], block), lambda j: (0, 0, 0, j)) for piece in turned] + [
            pl.BlockSpec((2, length, block), lambda j: (0, 0, j)),
            pl.BlockSpec((2, inner, inner), lambda j: (0, 0, 0)),
            pl.BlockSpec((2, outer, inner, 1), lambda j: (0, 0, 0, 0)),
        ],
        out_specs=pl.BlockSpec((groups, 2, count, block), lambda j: (0, 0, 0, j)),
        out_shape=jax.ShapeDtypeStruct((groups, 2, count, width), jnp.float32),
    )(*turned, factor, table, turn)


def lanes_forward_kernel(base_ref, wave_ref, hand_ref, src_ref, slow_ref, refl_ref, w_ref, tw_ref, o_ref):
    outer = tw_ref.shape[1]
    inner = tw_ref.shape[2]
    base = base_ref[0, 0]
    gain = OMEGA * OMEGA * refl_ref[0]
    real_in = (
        wave_ref[0, 0].astype(jnp.float32)
        + hand_ref[0].astype(jnp.float32)
        + gain * src_ref[0, 0].astype(jnp.float32)
    )
    imag_in = (
        wave_ref[0, 1].astype(jnp.float32)
        + hand_ref[1].astype(jnp.float32)
        + gain * src_ref[0, 1].astype(jnp.float32)
    )
    angle = -OMEGA * (slow_ref[0] - base) * DEPTH_STEP
    cosine = jnp.cos(angle)
    sine = jnp.sin(angle)
    lensed_real = real_in * cosine - imag_in * sine
    lensed_imag = real_in * sine + imag_in * cosine
    slabs = [
        (lensed_real[:, a * inner:(a + 1) * inner], lensed_imag[:, a * inner:(a + 1) * inner])
        for a in range(outer)
    ]
    spec = fft_slabs(slabs, -1)
    both = jnp.concatenate([w_ref[0], w_ref[1]], axis=1)
    count = lensed_real.shape[0]
    for k in range(outer):
        zr, zi = spec[k]
        tr = tw_ref[0, k:k + 1, :]
        ti = tw_ref[1, k:k + 1, :]
        zr, zi = zr * tr - zi * ti, zr * ti + zi * tr
        prod = jnp.dot(
            jnp.concatenate([zr, zi], axis=0), both,
            precision=lax.Precision.HIGH, preferred_element_type=jnp.float32,
        )
        width = o_ref.shape[3]
        dest = (k * inner) // width
        lanes = slice((k * inner) % width, (k * inner) % width + inner)
        o_ref[dest, 0, :, lanes] = prod[:count, :inner] - prod[count:, inner:]
        o_ref[dest, 1, :, lanes] = prod[:count, inner:] + prod[count:, :inner]


def lanes_inverse_kernel(x_ref, src_ref, w_ref, tw_ref, ext_ref, img_ref):
    outer = tw_ref.shape[1]
    inner = tw_ref.shape[2]
    count = x_ref.shape[2]
    both = jnp.concatenate([w_ref[0], -w_ref[1]], axis=1)
    outs = []
    for k in range(outer):
        width = x_ref.shape[3]
        origin = (k * inner) // width
        lanes = slice((k * inner) % width, (k * inner) % width + inner)
        yr = x_ref[origin, 0, :, lanes]
        yi = x_ref[origin, 1, :, lanes]
        prod = jnp.dot(
            jnp.concatenate([yr, yi], axis=0), both,
            precision=lax.Precision.HIGH, preferred_element_type=jnp.float32,
        )
        sr = prod[:count, :inner] - prod[count:, inner:]
        si = prod[:count, inner:] + prod[count:, :inner]
        tr = tw_ref[0, k:k + 1, :]
        ti = tw_ref[1, k:k + 1, :]
        outs.append((sr * tr + si * ti, si * tr - sr * ti))
    res = fft_slabs(outs, 1)
    for a in range(outer):
        out_real, out_imag = res[a]
        lanes = slice(a * inner, (a + 1) * inner)
        ext_ref[0, 0, :, lanes] = out_real.astype(ext_ref.dtype)
        ext_ref[0, 1, :, lanes] = out_imag.astype(ext_ref.dtype)
        img_ref[0, :, lanes] = (
            src_ref[0, 0, :, lanes].astype(jnp.float32) * out_real
            + src_ref[0, 1, :, lanes].astype(jnp.float32) * out_imag
        )


def lane_tables(length):
    outer, inner = factor_pair(length)
    table = jnp.stack(dft_table(inner, -1.0))
    turn = jnp.stack(twiddle_table(outer, inner, length, -1.0))
    return outer, inner, table, turn


def lanes_forward(wavefield, handed, source, slowness, reflectivity, base, first, step, groups):
    length = wavefield.shape[3]
    outer, inner, table, turn = lane_tables(length)
    block = min(step, 32)
    offset = first // block
    quad = lambda i: (0, 0, offset + i, 0)
    flat = lambda i: (0, offset + i, 0)
    return pl.pallas_call(
        lanes_forward_kernel,
        grid=(step // block,),
        in_specs=[
            pl.BlockSpec(memory_space=pltpu.SMEM),
            pl.BlockSpec((1, 2, block, length), quad),
            pl.BlockSpec((2, block, length), lambda i: (0, i, 0)),
            pl.BlockSpec((1, 2, block, length), quad),
            pl.BlockSpec((1, block, length), flat),
            pl.BlockSpec((1, block, length), flat),
            pl.BlockSpec((2, inner, inner), lambda i: (0, 0, 0)),
            pl.BlockSpec((2, outer, inner), lambda i: (0, 0, 0)),
        ],
        out_specs=pl.BlockSpec((groups, 2, block, length // groups), lambda i: (0, 0, i, 0)),
        out_shape=jax.ShapeDtypeStruct((groups, 2, step, length // groups), jnp.float32),
    )(base.reshape(1, 1), wavefield, handed, source, slowness, reflectivity, table, turn)


def lanes_inverse(back, source):
    groups, _, step, width = back.shape
    length = groups * width
    outer, inner, table, turn = lane_tables(length)
    block = min(step, 32)
    return pl.pallas_call(
        lanes_inverse_kernel,
        grid=(step // block,),
        in_specs=[
            pl.BlockSpec((groups, 2, block, width), lambda i: (0, 0, i, 0)),
            pl.BlockSpec((1, 2, block, length), lambda i: (0, 0, i, 0)),
            pl.BlockSpec((2, inner, inner), lambda i: (0, 0, 0)),
            pl.BlockSpec((2, outer, inner), lambda i: (0, 0, 0)),
        ],
        out_specs=[
            pl.BlockSpec((1, 2, block, length), lambda i: (0, 0, i, 0)),
            pl.BlockSpec((1, block, length), lambda i: (0, i, 0)),
        ],
        out_shape=[
            jax.ShapeDtypeStruct((1, 2, step, length), jnp.bfloat16),
            jax.ShapeDtypeStruct((1, step, length), jnp.float32),
        ],
    )(back, source, table, turn)


def signed_freq(index, length):
    signed = jnp.where(index < length // 2, index, index - length)
    return signed.astype(jnp.float32) * (2.0 * math.pi / length)


def permuted_freq(position, length):
    outer, inner = factor_pair(length)
    index = position // inner + outer * (position % inner)
    return signed_freq(index, length)


def propagator(freq_row, freq_col, base, scale):
    kz_square = (OMEGA * base) ** 2 - freq_row * freq_row - freq_col * freq_col
    root = jnp.sqrt(jnp.abs(kz_square))
    upward = kz_square >= 0.0
    real_part = jnp.where(upward, jnp.cos(root * DEPTH_STEP), jnp.exp(-root * DEPTH_STEP))
    imag_part = jnp.where(upward, -jnp.sin(root * DEPTH_STEP), jnp.zeros_like(root))
    return (real_part * scale, imag_part * scale)


def lens_rows(wave, handed, source, slow, refl, base):
    wave = wave.astype(jnp.float32)
    handed = handed.astype(jnp.float32)
    source = source.astype(jnp.float32)
    real_in = wave[0] + handed[0] + OMEGA * OMEGA * refl * source[0]
    imag_in = wave[1] + handed[1] + OMEGA * OMEGA * refl * source[1]
    angle = -OMEGA * (slow - base) * DEPTH_STEP
    cosine = jnp.cos(angle)
    sine = jnp.sin(angle)
    return (real_in * cosine - imag_in * sine, real_in * sine + imag_in * cosine)


def body(wavefield, boundary, source, slowness, reflectivity, ref_slowness):
    count = wavefield.shape[2]
    columns = wavefield.shape[3]
    eighth = count // 8
    if count % 8 == 0 and eighth % 8 == 0:
        bounds = [0, 3 * eighth, count]
    else:
        bounds = [0, count]
    groups = lax.axis_size("gx")
    device = lax.axis_index("gx")
    total_rows = count * groups
    width = columns // groups
    scale = 1.0 / (total_rows * columns)
    base = ref_slowness[0]
    pieces = []
    for first, last in zip(bounds[:-1], bounds[1:]):
        handed = shifted(boundary[0, :, first:last], "slab", -1)
        field = lanes_forward(wavefield, handed, source, slowness, reflectivity, base, first, last - first, groups)
        pieces.append(lax.all_to_all(field, "gx", split_axis=0, concat_axis=0, tiled=True))
    freq_row = permuted_freq(jnp.arange(total_rows, dtype=jnp.int32), total_rows)
    freq_col = permuted_freq(device * width + jnp.arange(width, dtype=jnp.int32), columns)
    factor = propagator(freq_row[:, None], freq_col[None, :], base, scale)
    spatial = rows_shift(pieces, jnp.stack(factor))
    back = lax.all_to_all(spatial, "gx", split_axis=0, concat_axis=0, tiled=True)
    return lanes_inverse(back, source)


def solution(mesh):
    return jax.shard_map(
        body,
        mesh=mesh,
        in_specs=(
            P("slab", None, "gx", None),
            P("slab", None, "gx", None),
            P("slab", None, "gx", None),
            P("slab", "gx", None),
            P("slab", "gx", None),
            P("slab"),
        ),
        out_specs=(P("slab", None, "gx", None), P("slab", "gx", None)),
        check_vma=False,
    )
```

```python
from functools import partial
import math

import jax
import jax.numpy as jnp
from jax import lax
from jax.sharding import PartitionSpec as P
from jax.experimental import pallas as pl
from jax.experimental.pallas import tpu as pltpu

OMEGA = 2.5
DEPTH_STEP = 1.0
precise = lax.Precision.HIGHEST


def shifted(block, axis, distance):
    devices = range(lax.axis_size(axis))
    route = [(i - distance, i) for i in devices if i - distance in devices]
    return lax.ppermute(block, axis, route)


def factor_pair(length):
    outer = math.gcd(length, 16)
    return (outer, length // outer)


def dft_table(length, orient):
    position = jnp.arange(length, dtype=jnp.int32)
    product = position[:, None] * position[None, :] % length
    angle = orient * 2.0 * math.pi * product.astype(jnp.float32) / length
    return (jnp.cos(angle), jnp.sin(angle))


def twiddle_table(first, second, length, orient):
    product = (
        jnp.arange(first, dtype=jnp.int32)[:, None]
        * jnp.arange(second, dtype=jnp.int32)[None, :]
        % length
    )
    angle = orient * 2.0 * math.pi * product.astype(jnp.float32) / length
    return (jnp.cos(angle), jnp.sin(angle))


def complex_einsum(form, table, field):
    mixing = partial(jnp.einsum, form, precision=precise)
    return (
        mixing(table[0], field[0]) - mixing(table[1], field[1]),
        mixing(table[0], field[1]) + mixing(table[1], field[0]),
    )


def times_complex(field, factor):
    return (
        field[0] * factor[0] - field[1] * factor[1],
        field[0] * factor[1] + field[1] * factor[0],
    )


def columns_forward(field):
    count, length = field[0].shape
    outer, inner = factor_pair(length)
    shaped = tuple((part.reshape(count, outer, inner) for part in field))
    section = complex_einsum("ka,rab->rkb", dft_table(outer, -1.0), shaped)
    section = times_complex(section, twiddle_table(outer, inner, length, -1.0))
    section = complex_einsum("mb,rkb->rkm", dft_table(inner, -1.0), section)
    return tuple((part.reshape(count, length) for part in section))


def columns_inverse(field):
    count, length = field[0].shape
    outer, inner = factor_pair(length)
    shaped = tuple((part.reshape(count, outer, inner) for part in field))
    section = complex_einsum("mb,rkm->rkb", dft_table(inner, 1.0), shaped)
    section = times_complex(section, twiddle_table(outer, inner, length, 1.0))
    section = complex_einsum("ka,rkb->rab", dft_table(outer, 1.0), section)
    return tuple((part.reshape(count, length) for part in section))


def rows_forward(field):
    length, count = field[0].shape
    outer, inner = factor_pair(length)
    shaped = tuple((part.reshape(outer, inner, count) for part in field))
    section = complex_einsum("ka,abc->kbc", dft_table(outer, -1.0), shaped)
    turned = twiddle_table(outer, inner, length, -1.0)
    section = times_complex(section, (turned[0][:, :, None], turned[1][:, :, None]))
    section = complex_einsum("mb,kbc->kmc", dft_table(inner, -1.0), section)
    return tuple((part.reshape(length, count) for part in section))


def rows_inverse(field):
    length, count = field[0].shape
    outer, inner = factor_pair(length)
    shaped = tuple((part.reshape(outer, inner, count) for part in field))
    section = complex_einsum("mb,kmc->kbc", dft_table(inner, 1.0), shaped)
    turned = twiddle_table(outer, inner, length, 1.0)
    section = times_complex(section, (turned[0][:, :, None], turned[1][:, :, None]))
    section = complex_einsum("ka,kbc->abc", dft_table(outer, 1.0), section)
    return tuple((part.reshape(length, count) for part in section))


def rotate(part, step, count):
    step %= count
    if step == 0:
        return part
    if 4 * step == count:
        return (-part[1], part[0])
    if 2 * step == count:
        return (-part[0], -part[1])
    if 4 * step == 3 * count:
        return (part[1], -part[0])
    cosine = math.cos(2.0 * math.pi * step / count)
    sine = math.sin(2.0 * math.pi * step / count)
    return (part[0] * cosine - part[1] * sine, part[0] * sine + part[1] * cosine)


def fft_slabs(parts, orient):
    count = len(parts)
    if count == 1:
        return list(parts)
    even = fft_slabs(parts[0::2], orient)
    odd = fft_slabs(parts[1::2], orient)
    half = count // 2
    out = [None] * count
    for k in range(half):
        turned = rotate(odd[k], orient * k, count)
        out[k] = (even[k][0] + turned[0], even[k][1] + turned[1])
        out[k + half] = (even[k][0] - turned[0], even[k][1] - turned[1])
    return out


def stacked_matmul(stacked, real, imag):
    size = real.shape[1]
    rows = stacked.shape[0] // 2
    both = jnp.concatenate([real, imag], axis=1)
    prod = jnp.dot(stacked, both, precision=lax.Precision.HIGH, preferred_element_type=jnp.float32)
    return (
        prod[:rows, :size] - prod[rows:, size:],
        prod[:rows, size:] + prod[rows:, :size],
    )


def rows_kernel(*refs):
    x_refs = refs[:-4]
    p_ref, w_ref, tw_ref, o_ref = refs[-4:]
    outer = tw_ref.shape[1]
    inner = tw_ref.shape[2]
    count = sum(ref.shape[2] for ref in x_refs)

    def place(a):
        return (a * inner) // count, slice((a * inner) % count, (a * inner) % count + inner)

    sizes = [ref.shape[2] for ref in x_refs]
    starts = [sum(sizes[:i]) for i in range(len(sizes))]
    slabs = []
    for a in range(outer):
        origin = (a * inner) // count
        low = (a * inner) % count
        pieces = []
        for ref, start, size in zip(x_refs, starts, sizes):
            top = min(low + inner, start + size)
            bottom = max(low, start)
            if top > bottom:
                pieces.append((ref[origin, 0, bottom - start:top - start, :], ref[origin, 1, bottom - start:top - start, :]))
        if len(pieces) == 1:
            slabs.append(pieces[0])
        else:
            slabs.append((
                jnp.concatenate([p[0] for p in pieces], axis=0),
                jnp.concatenate([p[1] for p in pieces], axis=0),
            ))
    spec = fft_slabs(slabs, -1)
    wr = w_ref[0]
    wi = w_ref[1]
    forward = jnp.concatenate([wr, wi], axis=0)
    backward = jnp.concatenate([wr, -wi], axis=0)
    outs = []
    for k in range(outer):
        zr, zi = spec[k]
        tr = tw_ref[0, k]
        ti = tw_ref[1, k]
        zr, zi = zr * tr - zi * ti, zr * ti + zi * tr
        yr, yi = stacked_matmul(forward, zr, zi)
        pr = p_ref[0, k * inner:(k + 1) * inner, :]
        pi = p_ref[1, k * inner:(k + 1) * inner, :]
        yr, yi = yr * pr - yi * pi, yr * pi + yi * pr
        sr, si = stacked_matmul(backward, yr, yi)
        outs.append((sr * tr + si * ti, si * tr - sr * ti))
    res = fft_slabs(outs, 1)
    for a in range(outer):
        origin, rows = place(a)
        o_ref[origin, 0, rows, :] = res[a][0]
        o_ref[origin, 1, rows, :] = res[a][1]


def rows_shift(turned, factor):
    groups, _, _, width = turned[0].shape
    count = sum(piece.shape[2] for piece in turned)
    length = groups * count
    outer, inner = factor_pair(length)
    block = min(width, 128)
    table = dft_table(inner, -1.0)
    turn = twiddle_table(outer, inner, length, -1.0)
    table = jnp.stack(table)
    turn = jnp.stack(turn)[..., None]
    return pl.pallas_call(
        rows_kernel,
        grid=(width // block,),
        in_specs=[pl.BlockSpec((groups, 2, piece.shape[2], block), lambda j: (0, 0, 0, j)) for piece in turned] + [
            pl.BlockSpec((2, length, block), lambda j: (0, 0, j)),
            pl.BlockSpec((2, inner, inner), lambda j: (0, 0, 0)),
            pl.BlockSpec((2, outer, inner, 1), lambda j: (0, 0, 0, 0)),
        ],
        out_specs=pl.BlockSpec((groups, 2, count, block), lambda j: (0, 0, 0, j)),
        out_shape=jax.ShapeDtypeStruct((groups, 2, count, width), jnp.float32),
    )(*turned, factor, table, turn)


def prelens_kernel(base_ref, wave_ref, src_ref, slow_ref, refl_ref, o_ref):
    base = base_ref[0, 0]
    gain = OMEGA * OMEGA * refl_ref[0]
    real_in = wave_ref[0, 0].astype(jnp.float32) + gain * src_ref[0, 0].astype(jnp.float32)
    imag_in = wave_ref[0, 1].astype(jnp.float32) + gain * src_ref[0, 1].astype(jnp.float32)
    angle = -OMEGA * (slow_ref[0] - base) * DEPTH_STEP
    cosine = jnp.cos(angle)
    sine = jnp.sin(angle)
    o_ref[0] = real_in * cosine - imag_in * sine
    o_ref[1] = real_in * sine + imag_in * cosine
    o_ref[2] = cosine
    o_ref[3] = sine


def prelens(wavefield, source, slowness, reflectivity, base):
    _, _, count, length = wavefield.shape
    block = min(count, 32)
    quad = lambda i: (0, 0, i, 0)
    flat = lambda i: (0, i, 0)
    return pl.pallas_call(
        prelens_kernel,
        grid=(count // block,),
        in_specs=[
            pl.BlockSpec(memory_space=pltpu.SMEM),
            pl.BlockSpec((1, 2, block, length), quad),
            pl.BlockSpec((1, 2, block, length), quad),
            pl.BlockSpec((1, block, length), flat),
            pl.BlockSpec((1, block, length), flat),
        ],
        out_specs=pl.BlockSpec((4, block, length), flat),
        out_shape=jax.ShapeDtypeStruct((4, count, length), jnp.float32),
    )(base.reshape(1, 1), wavefield, source, slowness, reflectivity)


def lanes_forward_kernel(pre_ref, hand_ref, w_ref, tw_ref, o_ref):
    outer = tw_ref.shape[1]
    inner = tw_ref.shape[2]
    hand_real = hand_ref[0].astype(jnp.float32)
    hand_imag = hand_ref[1].astype(jnp.float32)
    cosine = pre_ref[2]
    sine = pre_ref[3]
    lensed_real = pre_ref[0] + (hand_real * cosine - hand_imag * sine)
    lensed_imag = pre_ref[1] + (hand_real * sine + hand_imag * cosine)
    slabs = [
        (lensed_real[:, a * inner:(a + 1) * inner], lensed_imag[:, a * inner:(a + 1) * inner])
        for a in range(outer)
    ]
    spec = fft_slabs(slabs, -1)
    both = jnp.concatenate([w_ref[0], w_ref[1]], axis=1)
    count = lensed_real.shape[0]
    for k in range(outer):
        zr, zi = spec[k]
        tr = tw_ref[0, k:k + 1, :]
        ti = tw_ref[1, k:k + 1, :]
        zr, zi = zr * tr - zi * ti, zr * ti + zi * tr
        prod = jnp.dot(
            jnp.concatenate([zr, zi], axis=0), both,
            precision=lax.Precision.HIGH, preferred_element_type=jnp.float32,
        )
        width = o_ref.shape[3]
        dest = (k * inner) // width
        lanes = slice((k * inner) % width, (k * inner) % width + inner)
        o_ref[dest, 0, :, lanes] = prod[:count, :inner] - prod[count:, inner:]
        o_ref[dest, 1, :, lanes] = prod[:count, inner:] + prod[count:, :inner]


def lanes_inverse_kernel(x_ref, src_ref, w_ref, tw_ref, ext_ref, img_ref):
    outer = tw_ref.shape[1]
    inner = tw_ref.shape[2]
    count = x_ref.shape[2]
    both = jnp.concatenate([w_ref[0], -w_ref[1]], axis=1)
    outs = []
    for k in range(outer):
        width = x_ref.shape[3]
        origin = (k * inner) // width
        lanes = slice((k * inner) % width, (k * inner) % width + inner)
        yr = x_ref[origin, 0, :, lanes]
        yi = x_ref[origin, 1, :, lanes]
        prod = jnp.dot(
            jnp.concatenate([yr, yi], axis=0), both,
            precision=lax.Precision.HIGH, preferred_element_type=jnp.float32,
        )
        sr = prod[:count, :inner] - prod[count:, inner:]
        si = prod[:count, inner:] + prod[count:, :inner]
        tr = tw_ref[0, k:k + 1, :]
        ti = tw_ref[1, k:k + 1, :]
        outs.append((sr * tr + si * ti, si * tr - sr * ti))
    res = fft_slabs(outs, 1)
    for a in range(outer):
        out_real, out_imag = res[a]
        lanes = slice(a * inner, (a + 1) * inner)
        ext_ref[0, 0, :, lanes] = out_real.astype(ext_ref.dtype)
        ext_ref[0, 1, :, lanes] = out_imag.astype(ext_ref.dtype)
        img_ref[0, :, lanes] = (
            src_ref[0, 0, :, lanes].astype(jnp.float32) * out_real
            + src_ref[0, 1, :, lanes].astype(jnp.float32) * out_imag
        )


def lane_tables(length):
    outer, inner = factor_pair(length)
    table = jnp.stack(dft_table(inner, -1.0))
    turn = jnp.stack(twiddle_table(outer, inner, length, -1.0))
    return outer, inner, table, turn


def lanes_forward(lensed, handed, first, step, groups):
    length = lensed.shape[2]
    outer, inner, table, turn = lane_tables(length)
    block = min(step, 32)
    offset = first // block
    return pl.pallas_call(
        lanes_forward_kernel,
        grid=(step // block,),
        in_specs=[
            pl.BlockSpec((4, block, length), lambda i: (0, offset + i, 0)),
            pl.BlockSpec((2, block, length), lambda i: (0, i, 0)),
            pl.BlockSpec((2, inner, inner), lambda i: (0, 0, 0)),
            pl.BlockSpec((2, outer, inner), lambda i: (0, 0, 0)),
        ],
        out_specs=pl.BlockSpec((groups, 2, block, length // groups), lambda i: (0, 0, i, 0)),
        out_shape=jax.ShapeDtypeStruct((groups, 2, step, length // groups), jnp.float32),
    )(lensed, handed, table, turn)


def lanes_inverse(back, source):
    groups, _, step, width = back.shape
    length = groups * width
    outer, inner, table, turn = lane_tables(length)
    block = min(step, 32)
    return pl.pallas_call(
        lanes_inverse_kernel,
        grid=(step // block,),
        in_specs=[
            pl.BlockSpec((groups, 2, block, width), lambda i: (0, 0, i, 0)),
            pl.BlockSpec((1, 2, block, length), lambda i: (0, 0, i, 0)),
            pl.BlockSpec((2, inner, inner), lambda i: (0, 0, 0)),
            pl.BlockSpec((2, outer, inner), lambda i: (0, 0, 0)),
        ],
        out_specs=[
            pl.BlockSpec((1, 2, block, length), lambda i: (0, 0, i, 0)),
            pl.BlockSpec((1, block, length), lambda i: (0, i, 0)),
        ],
        out_shape=[
            jax.ShapeDtypeStruct((1, 2, step, length), jnp.bfloat16),
            jax.ShapeDtypeStruct((1, step, length), jnp.float32),
        ],
    )(back, source, table, turn)


def signed_freq(index, length):
    signed = jnp.where(index < length // 2, index, index - length)
    return signed.astype(jnp.float32) * (2.0 * math.pi / length)


def permuted_freq(position, length):
    outer, inner = factor_pair(length)
    index = position // inner + outer * (position % inner)
    return signed_freq(index, length)


def propagator(freq_row, freq_col, base, scale):
    kz_square = (OMEGA * base) ** 2 - freq_row * freq_row - freq_col * freq_col
    root = jnp.sqrt(jnp.abs(kz_square))
    upward = kz_square >= 0.0
    real_part = jnp.where(upward, jnp.cos(root * DEPTH_STEP), jnp.exp(-root * DEPTH_STEP))
    imag_part = jnp.where(upward, -jnp.sin(root * DEPTH_STEP), jnp.zeros_like(root))
    return (real_part * scale, imag_part * scale)


def lens_rows(wave, handed, source, slow, refl, base):
    wave = wave.astype(jnp.float32)
    handed = handed.astype(jnp.float32)
    source = source.astype(jnp.float32)
    real_in = wave[0] + handed[0] + OMEGA * OMEGA * refl * source[0]
    imag_in = wave[1] + handed[1] + OMEGA * OMEGA * refl * source[1]
    angle = -OMEGA * (slow - base) * DEPTH_STEP
    cosine = jnp.cos(angle)
    sine = jnp.sin(angle)
    return (real_in * cosine - imag_in * sine, real_in * sine + imag_in * cosine)


def body(wavefield, boundary, source, slowness, reflectivity, ref_slowness):
    count = wavefield.shape[2]
    columns = wavefield.shape[3]
    eighth = count // 8
    if count % 8 == 0 and eighth % 8 == 0:
        bounds = [0, 3 * eighth, count]
    else:
        bounds = [0, count]
    groups = lax.axis_size("gx")
    device = lax.axis_index("gx")
    total_rows = count * groups
    width = columns // groups
    scale = 1.0 / (total_rows * columns)
    base = ref_slowness[0]
    pieces = []
    lensed = prelens(wavefield, source, slowness, reflectivity, base)
    for first, last in zip(bounds[:-1], bounds[1:]):
        handed = shifted(boundary[0, :, first:last], "slab", -1)
        field = lanes_forward(lensed, handed, first, last - first, groups)
        pieces.append(lax.all_to_all(field, "gx", split_axis=0, concat_axis=0, tiled=True))
    freq_row = permuted_freq(jnp.arange(total_rows, dtype=jnp.int32), total_rows)
    freq_col = permuted_freq(device * width + jnp.arange(width, dtype=jnp.int32), columns)
    factor = propagator(freq_row[:, None], freq_col[None, :], base, scale)
    spatial = rows_shift(pieces, jnp.stack(factor))
    back = lax.all_to_all(spatial, "gx", split_axis=0, concat_axis=0, tiled=True)
    return lanes_inverse(back, source)


def solution(mesh):
    return jax.shard_map(
        body,
        mesh=mesh,
        in_specs=(
            P("slab", None, "gx", None),
            P("slab", None, "gx", None),
            P("slab", None, "gx", None),
            P("slab", "gx", None),
            P("slab", "gx", None),
            P("slab"),
        ),
        out_specs=(P("slab", None, "gx", None), P("slab", "gx", None)),
        check_vma=False,
    )
```

```python
from functools import partial
import math

import jax
import ml_dtypes
import numpy as np
import jax.numpy as jnp
from jax import lax
from jax.sharding import PartitionSpec as P
from jax.experimental import pallas as pl
from jax.experimental.pallas import tpu as pltpu

OMEGA = 2.5
DEPTH_STEP = 1.0
precise = lax.Precision.HIGHEST


def shifted(block, axis, distance):
    devices = range(lax.axis_size(axis))
    route = [(i - distance, i) for i in devices if i - distance in devices]
    return lax.ppermute(block, axis, route)


def factor_pair(length):
    outer = math.gcd(length, 16)
    return (outer, length // outer)


def dft_table(length, orient):
    position = jnp.arange(length, dtype=jnp.int32)
    product = position[:, None] * position[None, :] % length
    angle = orient * 2.0 * math.pi * product.astype(jnp.float32) / length
    return (jnp.cos(angle), jnp.sin(angle))


def twiddle_table(first, second, length, orient):
    product = (
        jnp.arange(first, dtype=jnp.int32)[:, None]
        * jnp.arange(second, dtype=jnp.int32)[None, :]
        % length
    )
    angle = orient * 2.0 * math.pi * product.astype(jnp.float32) / length
    return (jnp.cos(angle), jnp.sin(angle))


def complex_einsum(form, table, field):
    mixing = partial(jnp.einsum, form, precision=precise)
    return (
        mixing(table[0], field[0]) - mixing(table[1], field[1]),
        mixing(table[0], field[1]) + mixing(table[1], field[0]),
    )


def times_complex(field, factor):
    return (
        field[0] * factor[0] - field[1] * factor[1],
        field[0] * factor[1] + field[1] * factor[0],
    )


def columns_forward(field):
    count, length = field[0].shape
    outer, inner = factor_pair(length)
    shaped = tuple((part.reshape(count, outer, inner) for part in field))
    section = complex_einsum("ka,rab->rkb", dft_table(outer, -1.0), shaped)
    section = times_complex(section, twiddle_table(outer, inner, length, -1.0))
    section = complex_einsum("mb,rkb->rkm", dft_table(inner, -1.0), section)
    return tuple((part.reshape(count, length) for part in section))


def columns_inverse(field):
    count, length = field[0].shape
    outer, inner = factor_pair(length)
    shaped = tuple((part.reshape(count, outer, inner) for part in field))
    section = complex_einsum("mb,rkm->rkb", dft_table(inner, 1.0), shaped)
    section = times_complex(section, twiddle_table(outer, inner, length, 1.0))
    section = complex_einsum("ka,rkb->rab", dft_table(outer, 1.0), section)
    return tuple((part.reshape(count, length) for part in section))


def rows_forward(field):
    length, count = field[0].shape
    outer, inner = factor_pair(length)
    shaped = tuple((part.reshape(outer, inner, count) for part in field))
    section = complex_einsum("ka,abc->kbc", dft_table(outer, -1.0), shaped)
    turned = twiddle_table(outer, inner, length, -1.0)
    section = times_complex(section, (turned[0][:, :, None], turned[1][:, :, None]))
    section = complex_einsum("mb,kbc->kmc", dft_table(inner, -1.0), section)
    return tuple((part.reshape(length, count) for part in section))


def rows_inverse(field):
    length, count = field[0].shape
    outer, inner = factor_pair(length)
    shaped = tuple((part.reshape(outer, inner, count) for part in field))
    section = complex_einsum("mb,kmc->kbc", dft_table(inner, 1.0), shaped)
    turned = twiddle_table(outer, inner, length, 1.0)
    section = times_complex(section, (turned[0][:, :, None], turned[1][:, :, None]))
    section = complex_einsum("ka,kbc->abc", dft_table(outer, 1.0), section)
    return tuple((part.reshape(length, count) for part in section))


def rotate(part, step, count):
    step %= count
    if step == 0:
        return part
    if 4 * step == count:
        return (-part[1], part[0])
    if 2 * step == count:
        return (-part[0], -part[1])
    if 4 * step == 3 * count:
        return (part[1], -part[0])
    cosine = math.cos(2.0 * math.pi * step / count)
    sine = math.sin(2.0 * math.pi * step / count)
    return (part[0] * cosine - part[1] * sine, part[0] * sine + part[1] * cosine)


def fft_slabs(parts, orient):
    count = len(parts)
    if count == 1:
        return list(parts)
    even = fft_slabs(parts[0::2], orient)
    odd = fft_slabs(parts[1::2], orient)
    half = count // 2
    out = [None] * count
    for k in range(half):
        turned = rotate(odd[k], orient * k, count)
        out[k] = (even[k][0] + turned[0], even[k][1] + turned[1])
        out[k + half] = (even[k][0] - turned[0], even[k][1] - turned[1])
    return out


def split_bf16(value):
    spread = value * 65537.0
    high = spread - (spread - value)
    return high.astype(jnp.bfloat16), (value - high).astype(jnp.bfloat16)


def split_table(table):
    table = np.asarray(table, np.float32)
    high = table.astype(ml_dtypes.bfloat16)
    low = (table - high.astype(np.float32)).astype(ml_dtypes.bfloat16)
    return high, low


def dft_numpy(length, orient):
    position = np.arange(length)
    angle = orient * 2.0 * np.pi * (position[:, None] * position[None, :] % length) / length
    return np.cos(angle), np.sin(angle)


def stacked_matmul(stacked, real, imag):
    size = real.shape[1]
    rows = stacked.shape[0] // 2
    high, low = split_bf16(jnp.concatenate([real, imag], axis=1))
    both = jnp.concatenate([high, low, high], axis=0)
    prod = jnp.dot(stacked, both, preferred_element_type=jnp.float32)
    return (
        prod[:rows, :size] - prod[rows:, size:],
        prod[:rows, size:] + prod[rows:, :size],
    )


def rows_kernel(*refs):
    x_refs = refs[:-4]
    p_ref, w_ref, tw_ref, o_ref = refs[-4:]
    outer = tw_ref.shape[1]
    inner = tw_ref.shape[2]
    count = sum(ref.shape[2] for ref in x_refs)

    def place(a):
        return (a * inner) // count, slice((a * inner) % count, (a * inner) % count + inner)

    sizes = [ref.shape[2] for ref in x_refs]
    starts = [sum(sizes[:i]) for i in range(len(sizes))]
    slabs = []
    for a in range(outer):
        origin = (a * inner) // count
        low = (a * inner) % count
        pieces = []
        for ref, start, size in zip(x_refs, starts, sizes):
            top = min(low + inner, start + size)
            bottom = max(low, start)
            if top > bottom:
                pieces.append((ref[origin, 0, bottom - start:top - start, :], ref[origin, 1, bottom - start:top - start, :]))
        if len(pieces) == 1:
            slabs.append(pieces[0])
        else:
            slabs.append((
                jnp.concatenate([p[0] for p in pieces], axis=0),
                jnp.concatenate([p[1] for p in pieces], axis=0),
            ))
    spec = fft_slabs(slabs, -1)
    forward = w_ref[0]
    backward = w_ref[1]
    outs = []
    for k in range(outer):
        zr, zi = spec[k]
        tr = tw_ref[0, k]
        ti = tw_ref[1, k]
        zr, zi = zr * tr - zi * ti, zr * ti + zi * tr
        yr, yi = stacked_matmul(forward, zr, zi)
        pr = p_ref[0, k * inner:(k + 1) * inner, :]
        pi = p_ref[1, k * inner:(k + 1) * inner, :]
        yr, yi = yr * pr - yi * pi, yr * pi + yi * pr
        sr, si = stacked_matmul(backward, yr, yi)
        outs.append((sr * tr + si * ti, si * tr - sr * ti))
    res = fft_slabs(outs, 1)
    for a in range(outer):
        origin, rows = place(a)
        o_ref[origin, 0, rows, :] = res[a][0]
        o_ref[origin, 1, rows, :] = res[a][1]


def rows_shift(turned, factor):
    groups, _, _, width = turned[0].shape
    count = sum(piece.shape[2] for piece in turned)
    length = groups * count
    outer, inner = factor_pair(length)
    block = min(width, 128)
    real, imag = dft_numpy(inner, -1.0)
    turn = twiddle_table(outer, inner, length, -1.0)
    turn = jnp.stack(turn)[..., None]
    parts = [split_table(np.concatenate([real, sign * imag], axis=0)) for sign in (1.0, -1.0)]
    table = jnp.asarray(np.stack([np.concatenate([hi, hi, lo], axis=1) for hi, lo in parts]))
    return pl.pallas_call(
        rows_kernel,
        grid=(width // block,),
        in_specs=[pl.BlockSpec((groups, 2, piece.shape[2], block), lambda j: (0, 0, 0, j)) for piece in turned] + [
            pl.BlockSpec((2, length, block), lambda j: (0, 0, j)),
            pl.BlockSpec((2, 2 * inner, 3 * inner), lambda j: (0, 0, 0)),
            pl.BlockSpec((2, outer, inner, 1), lambda j: (0, 0, 0, 0)),
        ],
        out_specs=pl.BlockSpec((groups, 2, count, block), lambda j: (0, 0, 0, j)),
        out_shape=jax.ShapeDtypeStruct((groups, 2, count, width), jnp.float32),
    )(*turned, factor, table, turn)


def prelens_kernel(base_ref, wave_ref, src_ref, slow_ref, refl_ref, o_ref):
    base = base_ref[0, 0]
    gain = OMEGA * OMEGA * refl_ref[0]
    real_in = wave_ref[0, 0].astype(jnp.float32) + gain * src_ref[0, 0].astype(jnp.float32)
    imag_in = wave_ref[0, 1].astype(jnp.float32) + gain * src_ref[0, 1].astype(jnp.float32)
    angle = -OMEGA * (slow_ref[0] - base) * DEPTH_STEP
    cosine = jnp.cos(angle)
    sine = jnp.sin(angle)
    o_ref[0] = real_in * cosine - imag_in * sine
    o_ref[1] = real_in * sine + imag_in * cosine
    o_ref[2] = cosine
    o_ref[3] = sine


def prelens(wavefield, source, slowness, reflectivity, base):
    _, _, count, length = wavefield.shape
    block = min(count, 32)
    quad = lambda i: (0, 0, i, 0)
    flat = lambda i: (0, i, 0)
    return pl.pallas_call(
        prelens_kernel,
        grid=(count // block,),
        in_specs=[
            pl.BlockSpec(memory_space=pltpu.SMEM),
            pl.BlockSpec((1, 2, block, length), quad),
            pl.BlockSpec((1, 2, block, length), quad),
            pl.BlockSpec((1, block, length), flat),
            pl.BlockSpec((1, block, length), flat),
        ],
        out_specs=pl.BlockSpec((4, block, length), flat),
        out_shape=jax.ShapeDtypeStruct((4, count, length), jnp.float32),
    )(base.reshape(1, 1), wavefield, source, slowness, reflectivity)


def lanes_forward_kernel(pre_ref, hand_ref, w_ref, tw_ref, o_ref):
    outer = tw_ref.shape[1]
    inner = tw_ref.shape[2]
    hand_real = hand_ref[0].astype(jnp.float32)
    hand_imag = hand_ref[1].astype(jnp.float32)
    cosine = pre_ref[2]
    sine = pre_ref[3]
    lensed_real = pre_ref[0] + (hand_real * cosine - hand_imag * sine)
    lensed_imag = pre_ref[1] + (hand_real * sine + hand_imag * cosine)
    slabs = [
        (lensed_real[:, a * inner:(a + 1) * inner], lensed_imag[:, a * inner:(a + 1) * inner])
        for a in range(outer)
    ]
    spec = fft_slabs(slabs, -1)
    both = w_ref[0]
    count = lensed_real.shape[0]
    for k in range(outer):
        zr, zi = spec[k]
        tr = tw_ref[0, k:k + 1, :]
        ti = tw_ref[1, k:k + 1, :]
        zr, zi = zr * tr - zi * ti, zr * ti + zi * tr
        high, low = split_bf16(jnp.concatenate([zr, zi], axis=0))
        prod = jnp.dot(jnp.concatenate([high, low, high], axis=1), both, preferred_element_type=jnp.float32)
        width = o_ref.shape[3]
        dest = (k * inner) // width
        lanes = slice((k * inner) % width, (k * inner) % width + inner)
        o_ref[dest, 0, :, lanes] = prod[:count, :inner] - prod[count:, inner:]
        o_ref[dest, 1, :, lanes] = prod[:count, inner:] + prod[count:, :inner]


def lanes_inverse_kernel(x_ref, src_ref, w_ref, tw_ref, ext_ref, img_ref):
    outer = tw_ref.shape[1]
    inner = tw_ref.shape[2]
    count = x_ref.shape[2]
    both = w_ref[1]
    outs = []
    for k in range(outer):
        width = x_ref.shape[3]
        origin = (k * inner) // width
        lanes = slice((k * inner) % width, (k * inner) % width + inner)
        yr = x_ref[origin, 0, :, lanes]
        yi = x_ref[origin, 1, :, lanes]
        high, low = split_bf16(jnp.concatenate([yr, yi], axis=0))
        prod = jnp.dot(jnp.concatenate([high, low, high], axis=1), both, preferred_element_type=jnp.float32)
        sr = prod[:count, :inner] - prod[count:, inner:]
        si = prod[:count, inner:] + prod[count:, :inner]
        tr = tw_ref[0, k:k + 1, :]
        ti = tw_ref[1, k:k + 1, :]
        outs.append((sr * tr + si * ti, si * tr - sr * ti))
    res = fft_slabs(outs, 1)
    for a in range(outer):
        out_real, out_imag = res[a]
        lanes = slice(a * inner, (a + 1) * inner)
        ext_ref[0, 0, :, lanes] = out_real.astype(ext_ref.dtype)
        ext_ref[0, 1, :, lanes] = out_imag.astype(ext_ref.dtype)
        img_ref[0, :, lanes] = (
            src_ref[0, 0, :, lanes].astype(jnp.float32) * out_real
            + src_ref[0, 1, :, lanes].astype(jnp.float32) * out_imag
        )


def lane_tables(length):
    outer, inner = factor_pair(length)
    real, imag = dft_numpy(inner, -1.0)
    parts = [split_table(np.concatenate([real, sign * imag], axis=1)) for sign in (1.0, -1.0)]
    table = jnp.asarray(np.stack([np.concatenate([hi, hi, lo], axis=0) for hi, lo in parts]))
    turn = jnp.stack(twiddle_table(outer, inner, length, -1.0))
    return outer, inner, table, turn


def lanes_forward(lensed, handed, first, step, groups):
    length = lensed.shape[2]
    outer, inner, table, turn = lane_tables(length)
    block = min(step, 32)
    offset = first // block
    return pl.pallas_call(
        lanes_forward_kernel,
        grid=(step // block,),
        in_specs=[
            pl.BlockSpec((4, block, length), lambda i: (0, offset + i, 0)),
            pl.BlockSpec((2, block, length), lambda i: (0, i, 0)),
            pl.BlockSpec((2, 3 * inner, 2 * inner), lambda i: (0, 0, 0)),
            pl.BlockSpec((2, outer, inner), lambda i: (0, 0, 0)),
        ],
        out_specs=pl.BlockSpec((groups, 2, block, length // groups), lambda i: (0, 0, i, 0)),
        out_shape=jax.ShapeDtypeStruct((groups, 2, step, length // groups), jnp.float32),
    )(lensed, handed, table, turn)


def lanes_inverse(back, source):
    groups, _, step, width = back.shape
    length = groups * width
    outer, inner, table, turn = lane_tables(length)
    block = min(step, 64)
    return pl.pallas_call(
        lanes_inverse_kernel,
        grid=(step // block,),
        in_specs=[
            pl.BlockSpec((groups, 2, block, width), lambda i: (0, 0, i, 0)),
            pl.BlockSpec((1, 2, block, length), lambda i: (0, 0, i, 0)),
            pl.BlockSpec((2, 3 * inner, 2 * inner), lambda i: (0, 0, 0)),
            pl.BlockSpec((2, outer, inner), lambda i: (0, 0, 0)),
        ],
        out_specs=[
            pl.BlockSpec((1, 2, block, length), lambda i: (0, 0, i, 0)),
            pl.BlockSpec((1, block, length), lambda i: (0, i, 0)),
        ],
        out_shape=[
            jax.ShapeDtypeStruct((1, 2, step, length), jnp.bfloat16),
            jax.ShapeDtypeStruct((1, step, length), jnp.float32),
        ],
    )(back, source, table, turn)


def signed_freq(index, length):
    signed = jnp.where(index < length // 2, index, index - length)
    return signed.astype(jnp.float32) * (2.0 * math.pi / length)


def permuted_freq(position, length):
    outer, inner = factor_pair(length)
    index = position // inner + outer * (position % inner)
    return signed_freq(index, length)


def propagator(freq_row, freq_col, base, scale):
    kz_square = (OMEGA * base) ** 2 - freq_row * freq_row - freq_col * freq_col
    root = jnp.sqrt(jnp.abs(kz_square))
    upward = kz_square >= 0.0
    real_part = jnp.where(upward, jnp.cos(root * DEPTH_STEP), jnp.exp(-root * DEPTH_STEP))
    imag_part = jnp.where(upward, -jnp.sin(root * DEPTH_STEP), jnp.zeros_like(root))
    return (real_part * scale, imag_part * scale)


def lens_rows(wave, handed, source, slow, refl, base):
    wave = wave.astype(jnp.float32)
    handed = handed.astype(jnp.float32)
    source = source.astype(jnp.float32)
    real_in = wave[0] + handed[0] + OMEGA * OMEGA * refl * source[0]
    imag_in = wave[1] + handed[1] + OMEGA * OMEGA * refl * source[1]
    angle = -OMEGA * (slow - base) * DEPTH_STEP
    cosine = jnp.cos(angle)
    sine = jnp.sin(angle)
    return (real_in * cosine - imag_in * sine, real_in * sine + imag_in * cosine)


def body(wavefield, boundary, source, slowness, reflectivity, ref_slowness):
    count = wavefield.shape[2]
    columns = wavefield.shape[3]
    eighth = count // 8
    if count % 8 == 0 and eighth % 8 == 0:
        bounds = [0, 3 * eighth, count]
    else:
        bounds = [0, count]
    groups = lax.axis_size("gx")
    device = lax.axis_index("gx")
    total_rows = count * groups
    width = columns // groups
    scale = 1.0 / (total_rows * columns)
    base = ref_slowness[0]
    pieces = []
    lensed = prelens(wavefield, source, slowness, reflectivity, base)
    for first, last in zip(bounds[:-1], bounds[1:]):
        handed = shifted(boundary[0, :, first:last], "slab", -1)
        field = lanes_forward(lensed, handed, first, last - first, groups)
        pieces.append(lax.all_to_all(field, "gx", split_axis=0, concat_axis=0, tiled=True))
    freq_row = permuted_freq(jnp.arange(total_rows, dtype=jnp.int32), total_rows)
    freq_col = permuted_freq(device * width + jnp.arange(width, dtype=jnp.int32), columns)
    factor = propagator(freq_row[:, None], freq_col[None, :], base, scale)
    spatial = rows_shift(pieces, jnp.stack(factor))
    back = lax.all_to_all(spatial, "gx", split_axis=0, concat_axis=0, tiled=True)
    return lanes_inverse(back, source)


def solution(mesh):
    return jax.shard_map(
        body,
        mesh=mesh,
        in_specs=(
            P("slab", None, "gx", None),
            P("slab", None, "gx", None),
            P("slab", None, "gx", None),
            P("slab", "gx", None),
            P("slab", "gx", None),
            P("slab"),
        ),
        out_specs=(P("slab", None, "gx", None), P("slab", "gx", None)),
        check_vma=False,
    )
```

```python
from functools import partial
import math

import jax
import ml_dtypes
import numpy as np
import jax.numpy as jnp
from jax import lax
from jax.sharding import PartitionSpec as P
from jax.experimental import pallas as pl
from jax.experimental.pallas import tpu as pltpu

OMEGA = 2.5
DEPTH_STEP = 1.0
precise = lax.Precision.HIGHEST


def shifted(block, axis, distance):
    devices = range(lax.axis_size(axis))
    route = [(i - distance, i) for i in devices if i - distance in devices]
    return lax.ppermute(block, axis, route)


def factor_pair(length):
    outer = math.gcd(length, 16)
    return (outer, length // outer)


def dft_table(length, orient):
    position = jnp.arange(length, dtype=jnp.int32)
    product = position[:, None] * position[None, :] % length
    angle = orient * 2.0 * math.pi * product.astype(jnp.float32) / length
    return (jnp.cos(angle), jnp.sin(angle))


def twiddle_table(first, second, length, orient):
    product = (
        jnp.arange(first, dtype=jnp.int32)[:, None]
        * jnp.arange(second, dtype=jnp.int32)[None, :]
        % length
    )
    angle = orient * 2.0 * math.pi * product.astype(jnp.float32) / length
    return (jnp.cos(angle), jnp.sin(angle))


def complex_einsum(form, table, field):
    mixing = partial(jnp.einsum, form, precision=precise)
    return (
        mixing(table[0], field[0]) - mixing(table[1], field[1]),
        mixing(table[0], field[1]) + mixing(table[1], field[0]),
    )


def times_complex(field, factor):
    return (
        field[0] * factor[0] - field[1] * factor[1],
        field[0] * factor[1] + field[1] * factor[0],
    )


def columns_forward(field):
    count, length = field[0].shape
    outer, inner = factor_pair(length)
    shaped = tuple((part.reshape(count, outer, inner) for part in field))
    section = complex_einsum("ka,rab->rkb", dft_table(outer, -1.0), shaped)
    section = times_complex(section, twiddle_table(outer, inner, length, -1.0))
    section = complex_einsum("mb,rkb->rkm", dft_table(inner, -1.0), section)
    return tuple((part.reshape(count, length) for part in section))


def columns_inverse(field):
    count, length = field[0].shape
    outer, inner = factor_pair(length)
    shaped = tuple((part.reshape(count, outer, inner) for part in field))
    section = complex_einsum("mb,rkm->rkb", dft_table(inner, 1.0), shaped)
    section = times_complex(section, twiddle_table(outer, inner, length, 1.0))
    section = complex_einsum("ka,rkb->rab", dft_table(outer, 1.0), section)
    return tuple((part.reshape(count, length) for part in section))


def rows_forward(field):
    length, count = field[0].shape
    outer, inner = factor_pair(length)
    shaped = tuple((part.reshape(outer, inner, count) for part in field))
    section = complex_einsum("ka,abc->kbc", dft_table(outer, -1.0), shaped)
    turned = twiddle_table(outer, inner, length, -1.0)
    section = times_complex(section, (turned[0][:, :, None], turned[1][:, :, None]))
    section = complex_einsum("mb,kbc->kmc", dft_table(inner, -1.0), section)
    return tuple((part.reshape(length, count) for part in section))


def rows_inverse(field):
    length, count = field[0].shape
    outer, inner = factor_pair(length)
    shaped = tuple((part.reshape(outer, inner, count) for part in field))
    section = complex_einsum("mb,kmc->kbc", dft_table(inner, 1.0), shaped)
    turned = twiddle_table(outer, inner, length, 1.0)
    section = times_complex(section, (turned[0][:, :, None], turned[1][:, :, None]))
    section = complex_einsum("ka,kbc->abc", dft_table(outer, 1.0), section)
    return tuple((part.reshape(length, count) for part in section))


def rotate(part, step, count):
    step %= count
    if step == 0:
        return part
    if 4 * step == count:
        return (-part[1], part[0])
    if 2 * step == count:
        return (-part[0], -part[1])
    if 4 * step == 3 * count:
        return (part[1], -part[0])
    cosine = math.cos(2.0 * math.pi * step / count)
    sine = math.sin(2.0 * math.pi * step / count)
    return (part[0] * cosine - part[1] * sine, part[0] * sine + part[1] * cosine)


def fft_slabs(parts, orient):
    count = len(parts)
    if count == 1:
        return list(parts)
    even = fft_slabs(parts[0::2], orient)
    odd = fft_slabs(parts[1::2], orient)
    half = count // 2
    out = [None] * count
    for k in range(half):
        turned = rotate(odd[k], orient * k, count)
        out[k] = (even[k][0] + turned[0], even[k][1] + turned[1])
        out[k + half] = (even[k][0] - turned[0], even[k][1] - turned[1])
    return out


def split_bf16(value):
    spread = value * 65537.0
    high = spread - (spread - value)
    return high.astype(jnp.bfloat16), (value - high).astype(jnp.bfloat16)


def split_table(table):
    table = np.asarray(table, np.float32)
    high = table.astype(ml_dtypes.bfloat16)
    low = (table - high.astype(np.float32)).astype(ml_dtypes.bfloat16)
    return high, low


def dft_numpy(length, orient):
    position = np.arange(length)
    angle = orient * 2.0 * np.pi * (position[:, None] * position[None, :] % length) / length
    return np.cos(angle), np.sin(angle)


def stacked_matmul(stacked, real, imag):
    size = real.shape[1]
    rows = stacked.shape[0] // 2
    high, low = split_bf16(jnp.concatenate([real, imag], axis=1))
    both = jnp.concatenate([high, low, high], axis=0)
    prod = jnp.dot(stacked, both, preferred_element_type=jnp.float32)
    return (
        prod[:rows, :size] - prod[rows:, size:],
        prod[:rows, size:] + prod[rows:, :size],
    )


def rows_kernel(*refs):
    x_refs = refs[:-4]
    p_ref, w_ref, tw_ref, o_ref = refs[-4:]
    outer = tw_ref.shape[1]
    inner = tw_ref.shape[2]
    count = sum(ref.shape[2] for ref in x_refs)

    def place(a):
        return (a * inner) // count, slice((a * inner) % count, (a * inner) % count + inner)

    sizes = [ref.shape[2] for ref in x_refs]
    starts = [sum(sizes[:i]) for i in range(len(sizes))]
    slabs = []
    for a in range(outer):
        origin = (a * inner) // count
        low = (a * inner) % count
        pieces = []
        for ref, start, size in zip(x_refs, starts, sizes):
            top = min(low + inner, start + size)
            bottom = max(low, start)
            if top > bottom:
                pieces.append((ref[origin, 0, bottom - start:top - start, :], ref[origin, 1, bottom - start:top - start, :]))
        if len(pieces) == 1:
            slabs.append(pieces[0])
        else:
            slabs.append((
                jnp.concatenate([p[0] for p in pieces], axis=0),
                jnp.concatenate([p[1] for p in pieces], axis=0),
            ))
    spec = fft_slabs(slabs, -1)
    forward = w_ref[0]
    backward = w_ref[1]
    outs = []
    for k in range(outer):
        zr, zi = spec[k]
        tr = tw_ref[0, k]
        ti = tw_ref[1, k]
        zr, zi = zr * tr - zi * ti, zr * ti + zi * tr
        yr, yi = stacked_matmul(forward, zr, zi)
        pr = p_ref[0, k * inner:(k + 1) * inner, :]
        pi = p_ref[1, k * inner:(k + 1) * inner, :]
        yr, yi = yr * pr - yi * pi, yr * pi + yi * pr
        sr, si = stacked_matmul(backward, yr, yi)
        outs.append((sr * tr + si * ti, si * tr - sr * ti))
    res = fft_slabs(outs, 1)
    for a in range(outer):
        origin, rows = place(a)
        o_ref[origin, 0, rows, :] = res[a][0]
        o_ref[origin, 1, rows, :] = res[a][1]


def rows_shift(turned, factor):
    groups, _, _, width = turned[0].shape
    count = sum(piece.shape[2] for piece in turned)
    length = groups * count
    outer, inner = factor_pair(length)
    block = min(width, 128)
    real, imag = dft_numpy(inner, -1.0)
    turn = twiddle_table(outer, inner, length, -1.0)
    turn = jnp.stack(turn)[..., None]
    parts = [split_table(np.concatenate([real, sign * imag], axis=0)) for sign in (1.0, -1.0)]
    table = jnp.asarray(np.stack([np.concatenate([hi, hi, lo], axis=1) for hi, lo in parts]))
    return pl.pallas_call(
        rows_kernel,
        grid=(width // block,),
        in_specs=[pl.BlockSpec((groups, 2, piece.shape[2], block), lambda j: (0, 0, 0, j)) for piece in turned] + [
            pl.BlockSpec((2, length, block), lambda j: (0, 0, j)),
            pl.BlockSpec((2, 2 * inner, 3 * inner), lambda j: (0, 0, 0)),
            pl.BlockSpec((2, outer, inner, 1), lambda j: (0, 0, 0, 0)),
        ],
        out_specs=pl.BlockSpec((groups, 2, count, block), lambda j: (0, 0, 0, j)),
        out_shape=jax.ShapeDtypeStruct((groups, 2, count, width), jnp.float32),
    )(*turned, factor, table, turn)


def prelens_kernel(base_ref, wave_ref, src_ref, slow_ref, refl_ref, o_ref):
    base = base_ref[0, 0]
    gain = OMEGA * OMEGA * refl_ref[0]
    real_in = wave_ref[0, 0].astype(jnp.float32) + gain * src_ref[0, 0].astype(jnp.float32)
    imag_in = wave_ref[0, 1].astype(jnp.float32) + gain * src_ref[0, 1].astype(jnp.float32)
    angle = -OMEGA * (slow_ref[0] - base) * DEPTH_STEP
    cosine = jnp.cos(angle)
    sine = jnp.sin(angle)
    o_ref[0] = real_in * cosine - imag_in * sine
    o_ref[1] = real_in * sine + imag_in * cosine
    o_ref[2] = cosine
    o_ref[3] = sine


def prelens(wavefield, source, slowness, reflectivity, base):
    _, _, count, length = wavefield.shape
    block = min(count, 32)
    quad = lambda i: (0, 0, i, 0)
    flat = lambda i: (0, i, 0)
    return pl.pallas_call(
        prelens_kernel,
        grid=(count // block,),
        in_specs=[
            pl.BlockSpec(memory_space=pltpu.SMEM),
            pl.BlockSpec((1, 2, block, length), quad),
            pl.BlockSpec((1, 2, block, length), quad),
            pl.BlockSpec((1, block, length), flat),
            pl.BlockSpec((1, block, length), flat),
        ],
        out_specs=pl.BlockSpec((4, block, length), flat),
        out_shape=jax.ShapeDtypeStruct((4, count, length), jnp.float32),
    )(base.reshape(1, 1), wavefield, source, slowness, reflectivity)


def lanes_forward_kernel(pre_ref, hand_ref, w_ref, tw_ref, o_ref):
    outer = tw_ref.shape[1]
    inner = tw_ref.shape[2]
    hand_real = hand_ref[0].astype(jnp.float32)
    hand_imag = hand_ref[1].astype(jnp.float32)
    cosine = pre_ref[2]
    sine = pre_ref[3]
    lensed_real = pre_ref[0] + (hand_real * cosine - hand_imag * sine)
    lensed_imag = pre_ref[1] + (hand_real * sine + hand_imag * cosine)
    slabs = [
        (lensed_real[:, a * inner:(a + 1) * inner], lensed_imag[:, a * inner:(a + 1) * inner])
        for a in range(outer)
    ]
    spec = fft_slabs(slabs, -1)
    both = w_ref[0]
    count = lensed_real.shape[0]
    for k in range(outer):
        zr, zi = spec[k]
        tr = tw_ref[0, k:k + 1, :]
        ti = tw_ref[1, k:k + 1, :]
        zr, zi = zr * tr - zi * ti, zr * ti + zi * tr
        high, low = split_bf16(jnp.concatenate([zr, zi], axis=0))
        prod = jnp.dot(jnp.concatenate([high, low, high], axis=1), both, preferred_element_type=jnp.float32)
        width = o_ref.shape[3]
        dest = (k * inner) // width
        lanes = slice((k * inner) % width, (k * inner) % width + inner)
        o_ref[dest, 0, :, lanes] = prod[:count, :inner] - prod[count:, inner:]
        o_ref[dest, 1, :, lanes] = prod[:count, inner:] + prod[count:, :inner]


def lanes_inverse_kernel(x_ref, src_ref, w_ref, tw_ref, ext_ref, img_ref):
    outer = tw_ref.shape[1]
    inner = tw_ref.shape[2]
    count = x_ref.shape[2]
    both = w_ref[1]
    outs = []
    for k in range(outer):
        width = x_ref.shape[3]
        origin = (k * inner) // width
        lanes = slice((k * inner) % width, (k * inner) % width + inner)
        yr = x_ref[origin, 0, :, lanes]
        yi = x_ref[origin, 1, :, lanes]
        high, low = split_bf16(jnp.concatenate([yr, yi], axis=0))
        prod = jnp.dot(jnp.concatenate([high, low, high], axis=1), both, preferred_element_type=jnp.float32)
        sr = prod[:count, :inner] - prod[count:, inner:]
        si = prod[:count, inner:] + prod[count:, :inner]
        tr = tw_ref[0, k:k + 1, :]
        ti = tw_ref[1, k:k + 1, :]
        outs.append((sr * tr + si * ti, si * tr - sr * ti))
    res = fft_slabs(outs, 1)
    for a in range(outer):
        out_real, out_imag = res[a]
        lanes = slice(a * inner, (a + 1) * inner)
        ext_ref[0, 0, :, lanes] = out_real.astype(ext_ref.dtype)
        ext_ref[0, 1, :, lanes] = out_imag.astype(ext_ref.dtype)
        img_ref[0, :, lanes] = (
            src_ref[0, 0, :, lanes].astype(jnp.float32) * out_real
            + src_ref[0, 1, :, lanes].astype(jnp.float32) * out_imag
        )


def lane_tables(length):
    outer, inner = factor_pair(length)
    real, imag = dft_numpy(inner, -1.0)
    parts = [split_table(np.concatenate([real, sign * imag], axis=1)) for sign in (1.0, -1.0)]
    table = jnp.asarray(np.stack([np.concatenate([hi, hi, lo], axis=0) for hi, lo in parts]))
    turn = jnp.stack(twiddle_table(outer, inner, length, -1.0))
    return outer, inner, table, turn


def lanes_forward(lensed, handed, first, step, groups):
    length = lensed.shape[2]
    outer, inner, table, turn = lane_tables(length)
    block = 64 if step % 64 == 0 and first % 64 == 0 else min(step, 32)
    offset = first // block
    return pl.pallas_call(
        lanes_forward_kernel,
        grid=(step // block,),
        in_specs=[
            pl.BlockSpec((4, block, length), lambda i: (0, offset + i, 0)),
            pl.BlockSpec((2, block, length), lambda i: (0, i, 0)),
            pl.BlockSpec((2, 3 * inner, 2 * inner), lambda i: (0, 0, 0)),
            pl.BlockSpec((2, outer, inner), lambda i: (0, 0, 0)),
        ],
        out_specs=pl.BlockSpec((groups, 2, block, length // groups), lambda i: (0, 0, i, 0)),
        out_shape=jax.ShapeDtypeStruct((groups, 2, step, length // groups), jnp.float32),
    )(lensed, handed, table, turn)


def lanes_inverse(back, source):
    groups, _, step, width = back.shape
    length = groups * width
    outer, inner, table, turn = lane_tables(length)
    block = min(step, 64)
    return pl.pallas_call(
        lanes_inverse_kernel,
        grid=(step // block,),
        in_specs=[
            pl.BlockSpec((groups, 2, block, width), lambda i: (0, 0, i, 0)),
            pl.BlockSpec((1, 2, block, length), lambda i: (0, 0, i, 0)),
            pl.BlockSpec((2, 3 * inner, 2 * inner), lambda i: (0, 0, 0)),
            pl.BlockSpec((2, outer, inner), lambda i: (0, 0, 0)),
        ],
        out_specs=[
            pl.BlockSpec((1, 2, block, length), lambda i: (0, 0, i, 0)),
            pl.BlockSpec((1, block, length), lambda i: (0, i, 0)),
        ],
        out_shape=[
            jax.ShapeDtypeStruct((1, 2, step, length), jnp.bfloat16),
            jax.ShapeDtypeStruct((1, step, length), jnp.float32),
        ],
    )(back, source, table, turn)


def signed_freq(index, length):
    signed = jnp.where(index < length // 2, index, index - length)
    return signed.astype(jnp.float32) * (2.0 * math.pi / length)


def permuted_freq(position, length):
    outer, inner = factor_pair(length)
    index = position // inner + outer * (position % inner)
    return signed_freq(index, length)


def propagator(freq_row, freq_col, base, scale):
    kz_square = (OMEGA * base) ** 2 - freq_row * freq_row - freq_col * freq_col
    root = jnp.sqrt(jnp.abs(kz_square))
    upward = kz_square >= 0.0
    real_part = jnp.where(upward, jnp.cos(root * DEPTH_STEP), jnp.exp(-root * DEPTH_STEP))
    imag_part = jnp.where(upward, -jnp.sin(root * DEPTH_STEP), jnp.zeros_like(root))
    return (real_part * scale, imag_part * scale)


def lens_rows(wave, handed, source, slow, refl, base):
    wave = wave.astype(jnp.float32)
    handed = handed.astype(jnp.float32)
    source = source.astype(jnp.float32)
    real_in = wave[0] + handed[0] + OMEGA * OMEGA * refl * source[0]
    imag_in = wave[1] + handed[1] + OMEGA * OMEGA * refl * source[1]
    angle = -OMEGA * (slow - base) * DEPTH_STEP
    cosine = jnp.cos(angle)
    sine = jnp.sin(angle)
    return (real_in * cosine - imag_in * sine, real_in * sine + imag_in * cosine)


def body(wavefield, boundary, source, slowness, reflectivity, ref_slowness):
    count = wavefield.shape[2]
    columns = wavefield.shape[3]
    eighth = count // 8
    if count % 8 == 0 and eighth % 8 == 0:
        bounds = [0, 4 * eighth, count]
    else:
        bounds = [0, count]
    groups = lax.axis_size("gx")
    device = lax.axis_index("gx")
    total_rows = count * groups
    width = columns // groups
    scale = 1.0 / (total_rows * columns)
    base = ref_slowness[0]
    pieces = []
    lensed = prelens(wavefield, source, slowness, reflectivity, base)
    for first, last in zip(bounds[:-1], bounds[1:]):
        handed = shifted(boundary[0, :, first:last], "slab", -1)
        field = lanes_forward(lensed, handed, first, last - first, groups)
        pieces.append(lax.all_to_all(field, "gx", split_axis=0, concat_axis=0, tiled=True))
    freq_row = permuted_freq(jnp.arange(total_rows, dtype=jnp.int32), total_rows)
    freq_col = permuted_freq(device * width + jnp.arange(width, dtype=jnp.int32), columns)
    factor = propagator(freq_row[:, None], freq_col[None, :], base, scale)
    spatial = rows_shift(pieces, jnp.stack(factor))
    back = lax.all_to_all(spatial, "gx", split_axis=0, concat_axis=0, tiled=True)
    return lanes_inverse(back, source)


def solution(mesh):
    return jax.shard_map(
        body,
        mesh=mesh,
        in_specs=(
            P("slab", None, "gx", None),
            P("slab", None, "gx", None),
            P("slab", None, "gx", None),
            P("slab", "gx", None),
            P("slab", "gx", None),
            P("slab"),
        ),
        out_specs=(P("slab", None, "gx", None), P("slab", "gx", None)),
        check_vma=False,
    )
```

```python
from functools import partial
import math

import jax
import ml_dtypes
import numpy as np
import jax.numpy as jnp
from jax import lax
from jax.sharding import PartitionSpec as P
from jax.experimental import pallas as pl
from jax.experimental.pallas import tpu as pltpu

OMEGA = 2.5
DEPTH_STEP = 1.0
precise = lax.Precision.HIGHEST


def shifted(block, axis, distance):
    devices = range(lax.axis_size(axis))
    route = [(i - distance, i) for i in devices if i - distance in devices]
    return lax.ppermute(block, axis, route)


def factor_pair(length):
    outer = math.gcd(length, 16)
    return (outer, length // outer)


def dft_table(length, orient):
    position = jnp.arange(length, dtype=jnp.int32)
    product = position[:, None] * position[None, :] % length
    angle = orient * 2.0 * math.pi * product.astype(jnp.float32) / length
    return (jnp.cos(angle), jnp.sin(angle))


def twiddle_table(first, second, length, orient):
    product = (
        jnp.arange(first, dtype=jnp.int32)[:, None]
        * jnp.arange(second, dtype=jnp.int32)[None, :]
        % length
    )
    angle = orient * 2.0 * math.pi * product.astype(jnp.float32) / length
    return (jnp.cos(angle), jnp.sin(angle))


def complex_einsum(form, table, field):
    mixing = partial(jnp.einsum, form, precision=precise)
    return (
        mixing(table[0], field[0]) - mixing(table[1], field[1]),
        mixing(table[0], field[1]) + mixing(table[1], field[0]),
    )


def times_complex(field, factor):
    return (
        field[0] * factor[0] - field[1] * factor[1],
        field[0] * factor[1] + field[1] * factor[0],
    )


def columns_forward(field):
    count, length = field[0].shape
    outer, inner = factor_pair(length)
    shaped = tuple((part.reshape(count, outer, inner) for part in field))
    section = complex_einsum("ka,rab->rkb", dft_table(outer, -1.0), shaped)
    section = times_complex(section, twiddle_table(outer, inner, length, -1.0))
    section = complex_einsum("mb,rkb->rkm", dft_table(inner, -1.0), section)
    return tuple((part.reshape(count, length) for part in section))


def columns_inverse(field):
    count, length = field[0].shape
    outer, inner = factor_pair(length)
    shaped = tuple((part.reshape(count, outer, inner) for part in field))
    section = complex_einsum("mb,rkm->rkb", dft_table(inner, 1.0), shaped)
    section = times_complex(section, twiddle_table(outer, inner, length, 1.0))
    section = complex_einsum("ka,rkb->rab", dft_table(outer, 1.0), section)
    return tuple((part.reshape(count, length) for part in section))


def rows_forward(field):
    length, count = field[0].shape
    outer, inner = factor_pair(length)
    shaped = tuple((part.reshape(outer, inner, count) for part in field))
    section = complex_einsum("ka,abc->kbc", dft_table(outer, -1.0), shaped)
    turned = twiddle_table(outer, inner, length, -1.0)
    section = times_complex(section, (turned[0][:, :, None], turned[1][:, :, None]))
    section = complex_einsum("mb,kbc->kmc", dft_table(inner, -1.0), section)
    return tuple((part.reshape(length, count) for part in section))


def rows_inverse(field):
    length, count = field[0].shape
    outer, inner = factor_pair(length)
    shaped = tuple((part.reshape(outer, inner, count) for part in field))
    section = complex_einsum("mb,kmc->kbc", dft_table(inner, 1.0), shaped)
    turned = twiddle_table(outer, inner, length, 1.0)
    section = times_complex(section, (turned[0][:, :, None], turned[1][:, :, None]))
    section = complex_einsum("ka,kbc->abc", dft_table(outer, 1.0), section)
    return tuple((part.reshape(length, count) for part in section))


def rotate(part, step, count):
    step %= count
    if step == 0:
        return part
    if 4 * step == count:
        return (-part[1], part[0])
    if 2 * step == count:
        return (-part[0], -part[1])
    if 4 * step == 3 * count:
        return (part[1], -part[0])
    cosine = math.cos(2.0 * math.pi * step / count)
    sine = math.sin(2.0 * math.pi * step / count)
    return (part[0] * cosine - part[1] * sine, part[0] * sine + part[1] * cosine)


def fft_slabs(parts, orient):
    count = len(parts)
    if count == 1:
        return list(parts)
    even = fft_slabs(parts[0::2], orient)
    odd = fft_slabs(parts[1::2], orient)
    half = count // 2
    out = [None] * count
    for k in range(half):
        turned = rotate(odd[k], orient * k, count)
        out[k] = (even[k][0] + turned[0], even[k][1] + turned[1])
        out[k + half] = (even[k][0] - turned[0], even[k][1] - turned[1])
    return out


def split_bf16(value):
    spread = value * 65537.0
    high = spread - (spread - value)
    return high.astype(jnp.bfloat16), (value - high).astype(jnp.bfloat16)


def split_table(table):
    table = np.asarray(table, np.float32)
    high = table.astype(ml_dtypes.bfloat16)
    low = (table - high.astype(np.float32)).astype(ml_dtypes.bfloat16)
    return high, low


def dft_numpy(length, orient):
    position = np.arange(length)
    angle = orient * 2.0 * np.pi * (position[:, None] * position[None, :] % length) / length
    return np.cos(angle), np.sin(angle)


def stacked_matmul(stacked, real, imag):
    size = real.shape[1]
    rows = stacked.shape[0] // 2
    high, low = split_bf16(jnp.concatenate([real, imag], axis=1))
    both = jnp.concatenate([high, low, high], axis=0)
    prod = jnp.dot(stacked, both, preferred_element_type=jnp.float32)
    return (
        prod[:rows, :size] - prod[rows:, size:],
        prod[:rows, size:] + prod[rows:, :size],
    )


def rows_kernel(*refs):
    x_refs = refs[:-4]
    p_ref, w_ref, tw_ref, o_ref = refs[-4:]
    outer = tw_ref.shape[1]
    inner = tw_ref.shape[2]
    count = sum(ref.shape[2] for ref in x_refs)

    def place(a):
        return (a * inner) // count, slice((a * inner) % count, (a * inner) % count + inner)

    sizes = [ref.shape[2] for ref in x_refs]
    starts = [sum(sizes[:i]) for i in range(len(sizes))]
    slabs = []
    for a in range(outer):
        origin = (a * inner) // count
        low = (a * inner) % count
        pieces = []
        for ref, start, size in zip(x_refs, starts, sizes):
            top = min(low + inner, start + size)
            bottom = max(low, start)
            if top > bottom:
                pieces.append((ref[origin, 0, bottom - start:top - start, :], ref[origin, 1, bottom - start:top - start, :]))
        if len(pieces) == 1:
            slabs.append(pieces[0])
        else:
            slabs.append((
                jnp.concatenate([p[0] for p in pieces], axis=0),
                jnp.concatenate([p[1] for p in pieces], axis=0),
            ))
    spec = fft_slabs(slabs, -1)
    forward = w_ref[0]
    backward = w_ref[1]
    outs = []
    for k in range(outer):
        zr, zi = spec[k]
        tr = tw_ref[0, k]
        ti = tw_ref[1, k]
        zr, zi = zr * tr - zi * ti, zr * ti + zi * tr
        yr, yi = stacked_matmul(forward, zr, zi)
        pr = p_ref[0, k * inner:(k + 1) * inner, :]
        pi = p_ref[1, k * inner:(k + 1) * inner, :]
        yr, yi = yr * pr - yi * pi, yr * pi + yi * pr
        sr, si = stacked_matmul(backward, yr, yi)
        outs.append((sr * tr + si * ti, si * tr - sr * ti))
    res = fft_slabs(outs, 1)
    for a in range(outer):
        origin, rows = place(a)
        o_ref[origin, 0, rows, :] = res[a][0]
        o_ref[origin, 1, rows, :] = res[a][1]


def rows_shift(turned, factor):
    groups, _, _, width = turned[0].shape
    count = sum(piece.shape[2] for piece in turned)
    length = groups * count
    outer, inner = factor_pair(length)
    block = min(width, 128)
    real, imag = dft_numpy(inner, -1.0)
    turn = twiddle_table(outer, inner, length, -1.0)
    turn = jnp.stack(turn)[..., None]
    parts = [split_table(np.concatenate([real, sign * imag], axis=0)) for sign in (1.0, -1.0)]
    table = jnp.asarray(np.stack([np.concatenate([hi, hi, lo], axis=1) for hi, lo in parts]))
    return pl.pallas_call(
        rows_kernel,
        grid=(width // block,),
        in_specs=[pl.BlockSpec((groups, 2, piece.shape[2], block), lambda j: (0, 0, 0, j)) for piece in turned] + [
            pl.BlockSpec((2, length, block), lambda j: (0, 0, j)),
            pl.BlockSpec((2, 2 * inner, 3 * inner), lambda j: (0, 0, 0)),
            pl.BlockSpec((2, outer, inner, 1), lambda j: (0, 0, 0, 0)),
        ],
        out_specs=pl.BlockSpec((groups, 2, count, block), lambda j: (0, 0, 0, j)),
        out_shape=jax.ShapeDtypeStruct((groups, 2, count, width), jnp.float32),
    )(*turned, factor, table, turn)


def prelens_kernel(base_ref, wave_ref, src_ref, slow_ref, refl_ref, o_ref):
    base = base_ref[0, 0]
    gain = OMEGA * OMEGA * refl_ref[0]
    real_in = wave_ref[0, 0].astype(jnp.float32) + gain * src_ref[0, 0].astype(jnp.float32)
    imag_in = wave_ref[0, 1].astype(jnp.float32) + gain * src_ref[0, 1].astype(jnp.float32)
    angle = -OMEGA * (slow_ref[0] - base) * DEPTH_STEP
    cosine = jnp.cos(angle)
    sine = jnp.sin(angle)
    o_ref[0] = real_in * cosine - imag_in * sine
    o_ref[1] = real_in * sine + imag_in * cosine
    o_ref[2] = cosine
    o_ref[3] = sine


def prelens(wavefield, source, slowness, reflectivity, base):
    _, _, count, length = wavefield.shape
    block = min(count, 32)
    quad = lambda i: (0, 0, i, 0)
    flat = lambda i: (0, i, 0)
    return pl.pallas_call(
        prelens_kernel,
        grid=(count // block,),
        in_specs=[
            pl.BlockSpec(memory_space=pltpu.SMEM),
            pl.BlockSpec((1, 2, block, length), quad),
            pl.BlockSpec((1, 2, block, length), quad),
            pl.BlockSpec((1, block, length), flat),
            pl.BlockSpec((1, block, length), flat),
        ],
        out_specs=pl.BlockSpec((4, block, length), flat),
        out_shape=jax.ShapeDtypeStruct((4, count, length), jnp.float32),
    )(base.reshape(1, 1), wavefield, source, slowness, reflectivity)


def lanes_forward_kernel(pre_ref, real_ref, imag_ref, w_ref, tw_ref, o_ref):
    outer = tw_ref.shape[1]
    inner = tw_ref.shape[2]
    hand_real = real_ref[...].astype(jnp.float32)
    hand_imag = imag_ref[...].astype(jnp.float32)
    cosine = pre_ref[2]
    sine = pre_ref[3]
    lensed_real = pre_ref[0] + (hand_real * cosine - hand_imag * sine)
    lensed_imag = pre_ref[1] + (hand_real * sine + hand_imag * cosine)
    slabs = [
        (lensed_real[:, a * inner:(a + 1) * inner], lensed_imag[:, a * inner:(a + 1) * inner])
        for a in range(outer)
    ]
    spec = fft_slabs(slabs, -1)
    both = w_ref[0]
    count = lensed_real.shape[0]
    for k in range(outer):
        zr, zi = spec[k]
        tr = tw_ref[0, k:k + 1, :]
        ti = tw_ref[1, k:k + 1, :]
        zr, zi = zr * tr - zi * ti, zr * ti + zi * tr
        high, low = split_bf16(jnp.concatenate([zr, zi], axis=0))
        prod = jnp.dot(jnp.concatenate([high, low, high], axis=1), both, preferred_element_type=jnp.float32)
        width = o_ref.shape[3]
        dest = (k * inner) // width
        lanes = slice((k * inner) % width, (k * inner) % width + inner)
        o_ref[dest, 0, :, lanes] = prod[:count, :inner] - prod[count:, inner:]
        o_ref[dest, 1, :, lanes] = prod[:count, inner:] + prod[count:, :inner]


def lanes_inverse_kernel(x_ref, src_ref, w_ref, tw_ref, ext_ref, img_ref):
    outer = tw_ref.shape[1]
    inner = tw_ref.shape[2]
    count = x_ref.shape[2]
    both = w_ref[1]
    outs = []
    for k in range(outer):
        width = x_ref.shape[3]
        origin = (k * inner) // width
        lanes = slice((k * inner) % width, (k * inner) % width + inner)
        yr = x_ref[origin, 0, :, lanes]
        yi = x_ref[origin, 1, :, lanes]
        high, low = split_bf16(jnp.concatenate([yr, yi], axis=0))
        prod = jnp.dot(jnp.concatenate([high, low, high], axis=1), both, preferred_element_type=jnp.float32)
        sr = prod[:count, :inner] - prod[count:, inner:]
        si = prod[:count, inner:] + prod[count:, :inner]
        tr = tw_ref[0, k:k + 1, :]
        ti = tw_ref[1, k:k + 1, :]
        outs.append((sr * tr + si * ti, si * tr - sr * ti))
    res = fft_slabs(outs, 1)
    for a in range(outer):
        out_real, out_imag = res[a]
        lanes = slice(a * inner, (a + 1) * inner)
        ext_ref[0, 0, :, lanes] = out_real.astype(ext_ref.dtype)
        ext_ref[0, 1, :, lanes] = out_imag.astype(ext_ref.dtype)
        img_ref[0, :, lanes] = (
            src_ref[0, 0, :, lanes].astype(jnp.float32) * out_real
            + src_ref[0, 1, :, lanes].astype(jnp.float32) * out_imag
        )


def lane_tables(length):
    outer, inner = factor_pair(length)
    real, imag = dft_numpy(inner, -1.0)
    parts = [split_table(np.concatenate([real, sign * imag], axis=1)) for sign in (1.0, -1.0)]
    table = jnp.asarray(np.stack([np.concatenate([hi, hi, lo], axis=0) for hi, lo in parts]))
    turn = jnp.stack(twiddle_table(outer, inner, length, -1.0))
    return outer, inner, table, turn


def lanes_forward(lensed, handed, first, step, groups):
    length = lensed.shape[2]
    outer, inner, table, turn = lane_tables(length)
    block = 64 if step % 64 == 0 and first % 64 == 0 else min(step, 32)
    offset = first // block
    return pl.pallas_call(
        lanes_forward_kernel,
        grid=(step // block,),
        in_specs=[
            pl.BlockSpec((4, block, length), lambda i: (0, offset + i, 0)),
            pl.BlockSpec((block, length), lambda i: (i, 0)),
            pl.BlockSpec((block, length), lambda i: (i, 0)),
            pl.BlockSpec((2, 3 * inner, 2 * inner), lambda i: (0, 0, 0)),
            pl.BlockSpec((2, outer, inner), lambda i: (0, 0, 0)),
        ],
        out_specs=pl.BlockSpec((groups, 2, block, length // groups), lambda i: (0, 0, i, 0)),
        out_shape=jax.ShapeDtypeStruct((groups, 2, step, length // groups), jnp.float32),
    )(lensed, handed[0], handed[1], table, turn)


def lanes_inverse(back, source):
    groups, _, step, width = back.shape
    length = groups * width
    outer, inner, table, turn = lane_tables(length)
    block = min(step, 64)
    return pl.pallas_call(
        lanes_inverse_kernel,
        grid=(step // block,),
        in_specs=[
            pl.BlockSpec((groups, 2, block, width), lambda i: (0, 0, i, 0)),
            pl.BlockSpec((1, 2, block, length), lambda i: (0, 0, i, 0)),
            pl.BlockSpec((2, 3 * inner, 2 * inner), lambda i: (0, 0, 0)),
            pl.BlockSpec((2, outer, inner), lambda i: (0, 0, 0)),
        ],
        out_specs=[
            pl.BlockSpec((1, 2, block, length), lambda i: (0, 0, i, 0)),
            pl.BlockSpec((1, block, length), lambda i: (0, i, 0)),
        ],
        out_shape=[
            jax.ShapeDtypeStruct((1, 2, step, length), jnp.bfloat16),
            jax.ShapeDtypeStruct((1, step, length), jnp.float32),
        ],
    )(back, source, table, turn)


def signed_freq(index, length):
    signed = jnp.where(index < length // 2, index, index - length)
    return signed.astype(jnp.float32) * (2.0 * math.pi / length)


def permuted_freq(position, length):
    outer, inner = factor_pair(length)
    index = position // inner + outer * (position % inner)
    return signed_freq(index, length)


def propagator(freq_row, freq_col, base, scale):
    kz_square = (OMEGA * base) ** 2 - freq_row * freq_row - freq_col * freq_col
    root = jnp.sqrt(jnp.abs(kz_square))
    upward = kz_square >= 0.0
    real_part = jnp.where(upward, jnp.cos(root * DEPTH_STEP), jnp.exp(-root * DEPTH_STEP))
    imag_part = jnp.where(upward, -jnp.sin(root * DEPTH_STEP), jnp.zeros_like(root))
    return (real_part * scale, imag_part * scale)


def lens_rows(wave, handed, source, slow, refl, base):
    wave = wave.astype(jnp.float32)
    handed = handed.astype(jnp.float32)
    source = source.astype(jnp.float32)
    real_in = wave[0] + handed[0] + OMEGA * OMEGA * refl * source[0]
    imag_in = wave[1] + handed[1] + OMEGA * OMEGA * refl * source[1]
    angle = -OMEGA * (slow - base) * DEPTH_STEP
    cosine = jnp.cos(angle)
    sine = jnp.sin(angle)
    return (real_in * cosine - imag_in * sine, real_in * sine + imag_in * cosine)


def body(wavefield, boundary, source, slowness, reflectivity, ref_slowness):
    count = wavefield.shape[2]
    columns = wavefield.shape[3]
    eighth = count // 8
    if count % 8 == 0 and eighth % 8 == 0:
        bounds = [0, 4 * eighth, count]
    else:
        bounds = [0, count]
    groups = lax.axis_size("gx")
    device = lax.axis_index("gx")
    total_rows = count * groups
    width = columns // groups
    scale = 1.0 / (total_rows * columns)
    base = ref_slowness[0]
    pieces = []
    lensed = prelens(wavefield, source, slowness, reflectivity, base)
    for first, last in zip(bounds[:-1], bounds[1:]):
        handed = shifted((boundary[0, 0, first:last], boundary[0, 1, first:last]), "slab", -1)
        field = lanes_forward(lensed, handed, first, last - first, groups)
        pieces.append(lax.all_to_all(field, "gx", split_axis=0, concat_axis=0, tiled=True))
    freq_row = permuted_freq(jnp.arange(total_rows, dtype=jnp.int32), total_rows)
    freq_col = permuted_freq(device * width + jnp.arange(width, dtype=jnp.int32), columns)
    factor = propagator(freq_row[:, None], freq_col[None, :], base, scale)
    spatial = rows_shift(pieces, jnp.stack(factor))
    back = lax.all_to_all(spatial, "gx", split_axis=0, concat_axis=0, tiled=True)
    return lanes_inverse(back, source)


def solution(mesh):
    return jax.shard_map(
        body,
        mesh=mesh,
        in_specs=(
            P("slab", None, "gx", None),
            P("slab", None, "gx", None),
            P("slab", None, "gx", None),
            P("slab", "gx", None),
            P("slab", "gx", None),
            P("slab"),
        ),
        out_specs=(P("slab", None, "gx", None), P("slab", "gx", None)),
        check_vma=False,
    )
```

```python
from functools import partial
import math

import jax
import ml_dtypes
import numpy as np
import jax.numpy as jnp
from jax import lax
from jax.sharding import PartitionSpec as P
from jax.experimental import pallas as pl
from jax.experimental.pallas import tpu as pltpu

OMEGA = 2.5
DEPTH_STEP = 1.0
precise = lax.Precision.HIGHEST


def shifted(block, axis, distance):
    devices = range(lax.axis_size(axis))
    route = [(i - distance, i) for i in devices if i - distance in devices]
    return lax.ppermute(block, axis, route)


def factor_pair(length):
    outer = math.gcd(length, 16)
    return (outer, length // outer)


def dft_table(length, orient):
    position = jnp.arange(length, dtype=jnp.int32)
    product = position[:, None] * position[None, :] % length
    angle = orient * 2.0 * math.pi * product.astype(jnp.float32) / length
    return (jnp.cos(angle), jnp.sin(angle))


def twiddle_table(first, second, length, orient):
    product = (
        jnp.arange(first, dtype=jnp.int32)[:, None]
        * jnp.arange(second, dtype=jnp.int32)[None, :]
        % length
    )
    angle = orient * 2.0 * math.pi * product.astype(jnp.float32) / length
    return (jnp.cos(angle), jnp.sin(angle))


def complex_einsum(form, table, field):
    mixing = partial(jnp.einsum, form, precision=precise)
    return (
        mixing(table[0], field[0]) - mixing(table[1], field[1]),
        mixing(table[0], field[1]) + mixing(table[1], field[0]),
    )


def times_complex(field, factor):
    return (
        field[0] * factor[0] - field[1] * factor[1],
        field[0] * factor[1] + field[1] * factor[0],
    )


def columns_forward(field):
    count, length = field[0].shape
    outer, inner = factor_pair(length)
    shaped = tuple((part.reshape(count, outer, inner) for part in field))
    section = complex_einsum("ka,rab->rkb", dft_table(outer, -1.0), shaped)
    section = times_complex(section, twiddle_table(outer, inner, length, -1.0))
    section = complex_einsum("mb,rkb->rkm", dft_table(inner, -1.0), section)
    return tuple((part.reshape(count, length) for part in section))


def columns_inverse(field):
    count, length = field[0].shape
    outer, inner = factor_pair(length)
    shaped = tuple((part.reshape(count, outer, inner) for part in field))
    section = complex_einsum("mb,rkm->rkb", dft_table(inner, 1.0), shaped)
    section = times_complex(section, twiddle_table(outer, inner, length, 1.0))
    section = complex_einsum("ka,rkb->rab", dft_table(outer, 1.0), section)
    return tuple((part.reshape(count, length) for part in section))


def rows_forward(field):
    length, count = field[0].shape
    outer, inner = factor_pair(length)
    shaped = tuple((part.reshape(outer, inner, count) for part in field))
    section = complex_einsum("ka,abc->kbc", dft_table(outer, -1.0), shaped)
    turned = twiddle_table(outer, inner, length, -1.0)
    section = times_complex(section, (turned[0][:, :, None], turned[1][:, :, None]))
    section = complex_einsum("mb,kbc->kmc", dft_table(inner, -1.0), section)
    return tuple((part.reshape(length, count) for part in section))


def rows_inverse(field):
    length, count = field[0].shape
    outer, inner = factor_pair(length)
    shaped = tuple((part.reshape(outer, inner, count) for part in field))
    section = complex_einsum("mb,kmc->kbc", dft_table(inner, 1.0), shaped)
    turned = twiddle_table(outer, inner, length, 1.0)
    section = times_complex(section, (turned[0][:, :, None], turned[1][:, :, None]))
    section = complex_einsum("ka,kbc->abc", dft_table(outer, 1.0), section)
    return tuple((part.reshape(length, count) for part in section))


def rotate(part, step, count):
    step %= count
    if step == 0:
        return part
    if 4 * step == count:
        return (-part[1], part[0])
    if 2 * step == count:
        return (-part[0], -part[1])
    if 4 * step == 3 * count:
        return (part[1], -part[0])
    cosine = math.cos(2.0 * math.pi * step / count)
    sine = math.sin(2.0 * math.pi * step / count)
    return (part[0] * cosine - part[1] * sine, part[0] * sine + part[1] * cosine)


def fft_slabs(parts, orient):
    count = len(parts)
    if count == 1:
        return list(parts)
    even = fft_slabs(parts[0::2], orient)
    odd = fft_slabs(parts[1::2], orient)
    half = count // 2
    out = [None] * count
    for k in range(half):
        turned = rotate(odd[k], orient * k, count)
        out[k] = (even[k][0] + turned[0], even[k][1] + turned[1])
        out[k + half] = (even[k][0] - turned[0], even[k][1] - turned[1])
    return out


def split_bf16(value):
    spread = value * 65537.0
    high = spread - (spread - value)
    return high.astype(jnp.bfloat16), (value - high).astype(jnp.bfloat16)


def split_table(table):
    table = np.asarray(table, np.float32)
    high = table.astype(ml_dtypes.bfloat16)
    low = (table - high.astype(np.float32)).astype(ml_dtypes.bfloat16)
    return high, low


def dft_numpy(length, orient):
    position = np.arange(length)
    angle = orient * 2.0 * np.pi * (position[:, None] * position[None, :] % length) / length
    return np.cos(angle), np.sin(angle)


def stacked_matmul(stacked, real, imag):
    size = real.shape[1]
    rows = stacked.shape[0] // 2
    high, low = split_bf16(jnp.concatenate([real, imag], axis=1))
    both = jnp.concatenate([high, low, high], axis=0)
    prod = jnp.dot(stacked, both, preferred_element_type=jnp.float32)
    return (
        prod[:rows, :size] - prod[rows:, size:],
        prod[:rows, size:] + prod[rows:, :size],
    )


def rows_kernel(*refs):
    x_refs = refs[:-4]
    p_ref, w_ref, tw_ref, o_ref = refs[-4:]
    outer = tw_ref.shape[1]
    inner = tw_ref.shape[2]
    count = sum(ref.shape[2] for ref in x_refs)

    def place(a):
        return (a * inner) // count, slice((a * inner) % count, (a * inner) % count + inner)

    sizes = [ref.shape[2] for ref in x_refs]
    starts = [sum(sizes[:i]) for i in range(len(sizes))]
    slabs = []
    for a in range(outer):
        origin = (a * inner) // count
        low = (a * inner) % count
        pieces = []
        for ref, start, size in zip(x_refs, starts, sizes):
            top = min(low + inner, start + size)
            bottom = max(low, start)
            if top > bottom:
                pieces.append((ref[origin, 0, bottom - start:top - start, :], ref[origin, 1, bottom - start:top - start, :]))
        if len(pieces) == 1:
            slabs.append(pieces[0])
        else:
            slabs.append((
                jnp.concatenate([p[0] for p in pieces], axis=0),
                jnp.concatenate([p[1] for p in pieces], axis=0),
            ))
    spec = fft_slabs(slabs, -1)
    forward = w_ref[0]
    backward = w_ref[1]
    outs = []
    for k in range(outer):
        zr, zi = spec[k]
        tr = tw_ref[0, k]
        ti = tw_ref[1, k]
        zr, zi = zr * tr - zi * ti, zr * ti + zi * tr
        yr, yi = stacked_matmul(forward, zr, zi)
        pr = p_ref[0, k * inner:(k + 1) * inner, :]
        pi = p_ref[1, k * inner:(k + 1) * inner, :]
        yr, yi = yr * pr - yi * pi, yr * pi + yi * pr
        sr, si = stacked_matmul(backward, yr, yi)
        outs.append((sr * tr + si * ti, si * tr - sr * ti))
    res = fft_slabs(outs, 1)
    for a in range(outer):
        origin, rows = place(a)
        o_ref[origin, 0, rows, :] = res[a][0]
        o_ref[origin, 1, rows, :] = res[a][1]


def rows_shift(turned, factor):
    groups, _, _, width = turned[0].shape
    count = sum(piece.shape[2] for piece in turned)
    length = groups * count
    outer, inner = factor_pair(length)
    block = min(width, 128)
    real, imag = dft_numpy(inner, -1.0)
    turn = twiddle_table(outer, inner, length, -1.0)
    turn = jnp.stack(turn)[..., None]
    parts = [split_table(np.concatenate([real, sign * imag], axis=0)) for sign in (1.0, -1.0)]
    table = jnp.asarray(np.stack([np.concatenate([hi, hi, lo], axis=1) for hi, lo in parts]))
    return pl.pallas_call(
        rows_kernel,
        grid=(width // block,),
        in_specs=[pl.BlockSpec((groups, 2, piece.shape[2], block), lambda j: (0, 0, 0, j)) for piece in turned] + [
            pl.BlockSpec((2, length, block), lambda j: (0, 0, j)),
            pl.BlockSpec((2, 2 * inner, 3 * inner), lambda j: (0, 0, 0)),
            pl.BlockSpec((2, outer, inner, 1), lambda j: (0, 0, 0, 0)),
        ],
        out_specs=pl.BlockSpec((groups, 2, count, block), lambda j: (0, 0, 0, j)),
        out_shape=jax.ShapeDtypeStruct((groups, 2, count, width), jnp.float32),
    )(*turned, factor, table, turn)


def prelens_kernel(base_ref, wave_ref, src_ref, slow_ref, refl_ref, o_ref):
    base = base_ref[0, 0]
    gain = OMEGA * OMEGA * refl_ref[0]
    real_in = wave_ref[0, 0].astype(jnp.float32) + gain * src_ref[0, 0].astype(jnp.float32)
    imag_in = wave_ref[0, 1].astype(jnp.float32) + gain * src_ref[0, 1].astype(jnp.float32)
    angle = -OMEGA * (slow_ref[0] - base) * DEPTH_STEP
    cosine = jnp.cos(angle)
    sine = jnp.sin(angle)
    o_ref[0] = real_in * cosine - imag_in * sine
    o_ref[1] = real_in * sine + imag_in * cosine
    o_ref[2] = cosine
    o_ref[3] = sine


def prelens(wavefield, source, slowness, reflectivity, base):
    _, _, count, length = wavefield.shape
    block = min(count, 32)
    quad = lambda i: (0, 0, i, 0)
    flat = lambda i: (0, i, 0)
    return pl.pallas_call(
        prelens_kernel,
        grid=(count // block,),
        in_specs=[
            pl.BlockSpec(memory_space=pltpu.SMEM),
            pl.BlockSpec((1, 2, block, length), quad),
            pl.BlockSpec((1, 2, block, length), quad),
            pl.BlockSpec((1, block, length), flat),
            pl.BlockSpec((1, block, length), flat),
        ],
        out_specs=pl.BlockSpec((4, block, length), flat),
        out_shape=jax.ShapeDtypeStruct((4, count, length), jnp.float32),
    )(base.reshape(1, 1), wavefield, source, slowness, reflectivity)


def lanes_forward_kernel(pre_ref, hand_ref, w_ref, tw_ref, o_ref):
    outer = tw_ref.shape[1]
    inner = tw_ref.shape[2]
    hand_real = hand_ref[0].astype(jnp.float32)
    hand_imag = hand_ref[1].astype(jnp.float32)
    cosine = pre_ref[2]
    sine = pre_ref[3]
    lensed_real = pre_ref[0] + (hand_real * cosine - hand_imag * sine)
    lensed_imag = pre_ref[1] + (hand_real * sine + hand_imag * cosine)
    slabs = [
        (lensed_real[:, a * inner:(a + 1) * inner], lensed_imag[:, a * inner:(a + 1) * inner])
        for a in range(outer)
    ]
    spec = fft_slabs(slabs, -1)
    both = w_ref[0]
    count = lensed_real.shape[0]
    for k in range(outer):
        zr, zi = spec[k]
        tr = tw_ref[0, k:k + 1, :]
        ti = tw_ref[1, k:k + 1, :]
        zr, zi = zr * tr - zi * ti, zr * ti + zi * tr
        high, low = split_bf16(jnp.concatenate([zr, zi], axis=0))
        prod = jnp.dot(jnp.concatenate([high, low, high], axis=1), both, preferred_element_type=jnp.float32)
        width = o_ref.shape[3]
        dest = (k * inner) // width
        lanes = slice((k * inner) % width, (k * inner) % width + inner)
        o_ref[dest, 0, :, lanes] = prod[:count, :inner] - prod[count:, inner:]
        o_ref[dest, 1, :, lanes] = prod[:count, inner:] + prod[count:, :inner]


def lanes_inverse_kernel(x_ref, src_ref, w_ref, tw_ref, ext_ref, img_ref):
    outer = tw_ref.shape[1]
    inner = tw_ref.shape[2]
    count = x_ref.shape[2]
    both = w_ref[1]
    outs = []
    for k in range(outer):
        width = x_ref.shape[3]
        origin = (k * inner) // width
        lanes = slice((k * inner) % width, (k * inner) % width + inner)
        yr = x_ref[origin, 0, :, lanes]
        yi = x_ref[origin, 1, :, lanes]
        high, low = split_bf16(jnp.concatenate([yr, yi], axis=0))
        prod = jnp.dot(jnp.concatenate([high, low, high], axis=1), both, preferred_element_type=jnp.float32)
        sr = prod[:count, :inner] - prod[count:, inner:]
        si = prod[:count, inner:] + prod[count:, :inner]
        tr = tw_ref[0, k:k + 1, :]
        ti = tw_ref[1, k:k + 1, :]
        outs.append((sr * tr + si * ti, si * tr - sr * ti))
    res = fft_slabs(outs, 1)
    for a in range(outer):
        out_real, out_imag = res[a]
        lanes = slice(a * inner, (a + 1) * inner)
        ext_ref[0, 0, :, lanes] = out_real.astype(ext_ref.dtype)
        ext_ref[0, 1, :, lanes] = out_imag.astype(ext_ref.dtype)
        img_ref[0, :, lanes] = (
            src_ref[0, 0, :, lanes].astype(jnp.float32) * out_real
            + src_ref[0, 1, :, lanes].astype(jnp.float32) * out_imag
        )


def lane_tables(length):
    outer, inner = factor_pair(length)
    real, imag = dft_numpy(inner, -1.0)
    parts = [split_table(np.concatenate([real, sign * imag], axis=1)) for sign in (1.0, -1.0)]
    table = jnp.asarray(np.stack([np.concatenate([hi, hi, lo], axis=0) for hi, lo in parts]))
    turn = jnp.stack(twiddle_table(outer, inner, length, -1.0))
    return outer, inner, table, turn


def lanes_forward(lensed, handed, first, step, groups):
    length = lensed.shape[2]
    outer, inner, table, turn = lane_tables(length)
    block = 128 if step % 128 == 0 and first % 128 == 0 else min(step, 32)
    offset = first // block
    return pl.pallas_call(
        lanes_forward_kernel,
        grid=(step // block,),
        in_specs=[
            pl.BlockSpec((4, block, length), lambda i: (0, offset + i, 0)),
            pl.BlockSpec((2, block, length), lambda i: (0, i, 0)),
            pl.BlockSpec((2, 3 * inner, 2 * inner), lambda i: (0, 0, 0)),
            pl.BlockSpec((2, outer, inner), lambda i: (0, 0, 0)),
        ],
        out_specs=pl.BlockSpec((groups, 2, block, length // groups), lambda i: (0, 0, i, 0)),
        out_shape=jax.ShapeDtypeStruct((groups, 2, step, length // groups), jnp.float32),
    )(lensed, handed, table, turn)


def lanes_inverse(back, source):
    groups, _, step, width = back.shape
    length = groups * width
    outer, inner, table, turn = lane_tables(length)
    block = min(step, 64)
    return pl.pallas_call(
        lanes_inverse_kernel,
        grid=(step // block,),
        in_specs=[
            pl.BlockSpec((groups, 2, block, width), lambda i: (0, 0, i, 0)),
            pl.BlockSpec((1, 2, block, length), lambda i: (0, 0, i, 0)),
            pl.BlockSpec((2, 3 * inner, 2 * inner), lambda i: (0, 0, 0)),
            pl.BlockSpec((2, outer, inner), lambda i: (0, 0, 0)),
        ],
        out_specs=[
            pl.BlockSpec((1, 2, block, length), lambda i: (0, 0, i, 0)),
            pl.BlockSpec((1, block, length), lambda i: (0, i, 0)),
        ],
        out_shape=[
            jax.ShapeDtypeStruct((1, 2, step, length), jnp.bfloat16),
            jax.ShapeDtypeStruct((1, step, length), jnp.float32),
        ],
    )(back, source, table, turn)


def signed_freq(index, length):
    signed = jnp.where(index < length // 2, index, index - length)
    return signed.astype(jnp.float32) * (2.0 * math.pi / length)


def permuted_freq(position, length):
    outer, inner = factor_pair(length)
    index = position // inner + outer * (position % inner)
    return signed_freq(index, length)


def propagator(freq_row, freq_col, base, scale):
    kz_square = (OMEGA * base) ** 2 - freq_row * freq_row - freq_col * freq_col
    root = jnp.sqrt(jnp.abs(kz_square))
    upward = kz_square >= 0.0
    real_part = jnp.where(upward, jnp.cos(root * DEPTH_STEP), jnp.exp(-root * DEPTH_STEP))
    imag_part = jnp.where(upward, -jnp.sin(root * DEPTH_STEP), jnp.zeros_like(root))
    return (real_part * scale, imag_part * scale)


def lens_rows(wave, handed, source, slow, refl, base):
    wave = wave.astype(jnp.float32)
    handed = handed.astype(jnp.float32)
    source = source.astype(jnp.float32)
    real_in = wave[0] + handed[0] + OMEGA * OMEGA * refl * source[0]
    imag_in = wave[1] + handed[1] + OMEGA * OMEGA * refl * source[1]
    angle = -OMEGA * (slow - base) * DEPTH_STEP
    cosine = jnp.cos(angle)
    sine = jnp.sin(angle)
    return (real_in * cosine - imag_in * sine, real_in * sine + imag_in * cosine)


def body(wavefield, boundary, source, slowness, reflectivity, ref_slowness):
    count = wavefield.shape[2]
    columns = wavefield.shape[3]
    eighth = count // 8
    if count % 8 == 0 and eighth % 8 == 0:
        bounds = [0, 4 * eighth, count]
    else:
        bounds = [0, count]
    groups = lax.axis_size("gx")
    device = lax.axis_index("gx")
    total_rows = count * groups
    width = columns // groups
    scale = 1.0 / (total_rows * columns)
    base = ref_slowness[0]
    pieces = []
    lensed = prelens(wavefield, source, slowness, reflectivity, base)
    for first, last in zip(bounds[:-1], bounds[1:]):
        handed = shifted(boundary[0, :, first:last], "slab", -1)
        field = lanes_forward(lensed, handed, first, last - first, groups)
        pieces.append(lax.all_to_all(field, "gx", split_axis=0, concat_axis=0, tiled=True))
    freq_row = permuted_freq(jnp.arange(total_rows, dtype=jnp.int32), total_rows)
    freq_col = permuted_freq(device * width + jnp.arange(width, dtype=jnp.int32), columns)
    factor = propagator(freq_row[:, None], freq_col[None, :], base, scale)
    spatial = rows_shift(pieces, jnp.stack(factor))
    back = lax.all_to_all(spatial, "gx", split_axis=0, concat_axis=0, tiled=True)
    return lanes_inverse(back, source)


def solution(mesh):
    return jax.shard_map(
        body,
        mesh=mesh,
        in_specs=(
            P("slab", None, "gx", None),
            P("slab", None, "gx", None),
            P("slab", None, "gx", None),
            P("slab", "gx", None),
            P("slab", "gx", None),
            P("slab"),
        ),
        out_specs=(P("slab", None, "gx", None), P("slab", "gx", None)),
        check_vma=False,
    )
```

```python
from functools import partial
import math

import jax
import ml_dtypes
import numpy as np
import jax.numpy as jnp
from jax import lax
from jax.sharding import PartitionSpec as P
from jax.experimental import pallas as pl
from jax.experimental.pallas import tpu as pltpu

OMEGA = 2.5
DEPTH_STEP = 1.0
precise = lax.Precision.HIGHEST


def shifted(block, axis, distance):
    devices = range(lax.axis_size(axis))
    route = [(i - distance, i) for i in devices if i - distance in devices]
    return lax.ppermute(block, axis, route)


def factor_pair(length):
    outer = math.gcd(length, 16)
    return (outer, length // outer)


def dft_table(length, orient):
    position = jnp.arange(length, dtype=jnp.int32)
    product = position[:, None] * position[None, :] % length
    angle = orient * 2.0 * math.pi * product.astype(jnp.float32) / length
    return (jnp.cos(angle), jnp.sin(angle))


def twiddle_table(first, second, length, orient):
    product = (
        jnp.arange(first, dtype=jnp.int32)[:, None]
        * jnp.arange(second, dtype=jnp.int32)[None, :]
        % length
    )
    angle = orient * 2.0 * math.pi * product.astype(jnp.float32) / length
    return (jnp.cos(angle), jnp.sin(angle))


def complex_einsum(form, table, field):
    mixing = partial(jnp.einsum, form, precision=precise)
    return (
        mixing(table[0], field[0]) - mixing(table[1], field[1]),
        mixing(table[0], field[1]) + mixing(table[1], field[0]),
    )


def times_complex(field, factor):
    return (
        field[0] * factor[0] - field[1] * factor[1],
        field[0] * factor[1] + field[1] * factor[0],
    )


def columns_forward(field):
    count, length = field[0].shape
    outer, inner = factor_pair(length)
    shaped = tuple((part.reshape(count, outer, inner) for part in field))
    section = complex_einsum("ka,rab->rkb", dft_table(outer, -1.0), shaped)
    section = times_complex(section, twiddle_table(outer, inner, length, -1.0))
    section = complex_einsum("mb,rkb->rkm", dft_table(inner, -1.0), section)
    return tuple((part.reshape(count, length) for part in section))


def columns_inverse(field):
    count, length = field[0].shape
    outer, inner = factor_pair(length)
    shaped = tuple((part.reshape(count, outer, inner) for part in field))
    section = complex_einsum("mb,rkm->rkb", dft_table(inner, 1.0), shaped)
    section = times_complex(section, twiddle_table(outer, inner, length, 1.0))
    section = complex_einsum("ka,rkb->rab", dft_table(outer, 1.0), section)
    return tuple((part.reshape(count, length) for part in section))


def rows_forward(field):
    length, count = field[0].shape
    outer, inner = factor_pair(length)
    shaped = tuple((part.reshape(outer, inner, count) for part in field))
    section = complex_einsum("ka,abc->kbc", dft_table(outer, -1.0), shaped)
    turned = twiddle_table(outer, inner, length, -1.0)
    section = times_complex(section, (turned[0][:, :, None], turned[1][:, :, None]))
    section = complex_einsum("mb,kbc->kmc", dft_table(inner, -1.0), section)
    return tuple((part.reshape(length, count) for part in section))


def rows_inverse(field):
    length, count = field[0].shape
    outer, inner = factor_pair(length)
    shaped = tuple((part.reshape(outer, inner, count) for part in field))
    section = complex_einsum("mb,kmc->kbc", dft_table(inner, 1.0), shaped)
    turned = twiddle_table(outer, inner, length, 1.0)
    section = times_complex(section, (turned[0][:, :, None], turned[1][:, :, None]))
    section = complex_einsum("ka,kbc->abc", dft_table(outer, 1.0), section)
    return tuple((part.reshape(length, count) for part in section))


def rotate(part, step, count):
    step %= count
    if step == 0:
        return part
    if 4 * step == count:
        return (-part[1], part[0])
    if 2 * step == count:
        return (-part[0], -part[1])
    if 4 * step == 3 * count:
        return (part[1], -part[0])
    cosine = math.cos(2.0 * math.pi * step / count)
    sine = math.sin(2.0 * math.pi * step / count)
    return (part[0] * cosine - part[1] * sine, part[0] * sine + part[1] * cosine)


def fft_slabs(parts, orient):
    count = len(parts)
    if count == 1:
        return list(parts)
    even = fft_slabs(parts[0::2], orient)
    odd = fft_slabs(parts[1::2], orient)
    half = count // 2
    out = [None] * count
    for k in range(half):
        turned = rotate(odd[k], orient * k, count)
        out[k] = (even[k][0] + turned[0], even[k][1] + turned[1])
        out[k + half] = (even[k][0] - turned[0], even[k][1] - turned[1])
    return out


def split_bf16(value):
    spread = value * 65537.0
    high = spread - (spread - value)
    return high.astype(jnp.bfloat16), (value - high).astype(jnp.bfloat16)


def split_table(table):
    table = np.asarray(table, np.float32)
    high = table.astype(ml_dtypes.bfloat16)
    low = (table - high.astype(np.float32)).astype(ml_dtypes.bfloat16)
    return high, low


def dft_numpy(length, orient):
    position = np.arange(length)
    angle = orient * 2.0 * np.pi * (position[:, None] * position[None, :] % length) / length
    return np.cos(angle), np.sin(angle)


def stacked_matmul(stacked, real, imag):
    size = real.shape[1]
    rows = stacked.shape[0] // 2
    high, low = split_bf16(jnp.concatenate([real, imag], axis=1))
    both = jnp.concatenate([high, low, high], axis=0)
    prod = jnp.dot(stacked, both, preferred_element_type=jnp.float32)
    return (
        prod[:rows, :size] - prod[rows:, size:],
        prod[:rows, size:] + prod[rows:, :size],
    )


def rows_kernel(*refs):
    x_refs = refs[:-4]
    p_ref, w_ref, tw_ref, o_ref = refs[-4:]
    outer = tw_ref.shape[1]
    inner = tw_ref.shape[2]
    count = sum(ref.shape[2] for ref in x_refs)

    def place(a):
        return (a * inner) // count, slice((a * inner) % count, (a * inner) % count + inner)

    sizes = [ref.shape[2] for ref in x_refs]
    starts = [sum(sizes[:i]) for i in range(len(sizes))]
    slabs = []
    for a in range(outer):
        origin = (a * inner) // count
        low = (a * inner) % count
        pieces = []
        for ref, start, size in zip(x_refs, starts, sizes):
            top = min(low + inner, start + size)
            bottom = max(low, start)
            if top > bottom:
                pieces.append((ref[origin, 0, bottom - start:top - start, :], ref[origin, 1, bottom - start:top - start, :]))
        if len(pieces) == 1:
            slabs.append(pieces[0])
        else:
            slabs.append((
                jnp.concatenate([p[0] for p in pieces], axis=0),
                jnp.concatenate([p[1] for p in pieces], axis=0),
            ))
    spec = fft_slabs(slabs, -1)
    forward = w_ref[0]
    backward = w_ref[1]
    outs = []
    for k in range(outer):
        zr, zi = spec[k]
        tr = tw_ref[0, k]
        ti = tw_ref[1, k]
        zr, zi = zr * tr - zi * ti, zr * ti + zi * tr
        yr, yi = stacked_matmul(forward, zr, zi)
        pr = p_ref[0, k * inner:(k + 1) * inner, :]
        pi = p_ref[1, k * inner:(k + 1) * inner, :]
        yr, yi = yr * pr - yi * pi, yr * pi + yi * pr
        sr, si = stacked_matmul(backward, yr, yi)
        outs.append((sr * tr + si * ti, si * tr - sr * ti))
    res = fft_slabs(outs, 1)
    for a in range(outer):
        origin, rows = place(a)
        o_ref[origin, 0, rows, :] = res[a][0]
        o_ref[origin, 1, rows, :] = res[a][1]


def rows_shift(turned, factor):
    groups, _, _, width = turned[0].shape
    count = sum(piece.shape[2] for piece in turned)
    length = groups * count
    outer, inner = factor_pair(length)
    block = min(width, 128)
    real, imag = dft_numpy(inner, -1.0)
    turn = twiddle_table(outer, inner, length, -1.0)
    turn = jnp.stack(turn)[..., None]
    parts = [split_table(np.concatenate([real, sign * imag], axis=0)) for sign in (1.0, -1.0)]
    table = jnp.asarray(np.stack([np.concatenate([hi, hi, lo], axis=1) for hi, lo in parts]))
    return pl.pallas_call(
        rows_kernel,
        grid=(width // block,),
        in_specs=[pl.BlockSpec((groups, 2, piece.shape[2], block), lambda j: (0, 0, 0, j)) for piece in turned] + [
            pl.BlockSpec((2, length, block), lambda j: (0, 0, j)),
            pl.BlockSpec((2, 2 * inner, 3 * inner), lambda j: (0, 0, 0)),
            pl.BlockSpec((2, outer, inner, 1), lambda j: (0, 0, 0, 0)),
        ],
        out_specs=pl.BlockSpec((groups, 2, count, block), lambda j: (0, 0, 0, j)),
        out_shape=jax.ShapeDtypeStruct((groups, 2, count, width), jnp.float32),
    )(*turned, factor, table, turn)


def prelens_kernel(base_ref, wave_ref, src_ref, slow_ref, refl_ref, o_ref):
    base = base_ref[0, 0]
    gain = OMEGA * OMEGA * refl_ref[0]
    real_in = wave_ref[0, 0].astype(jnp.float32) + gain * src_ref[0, 0].astype(jnp.float32)
    imag_in = wave_ref[0, 1].astype(jnp.float32) + gain * src_ref[0, 1].astype(jnp.float32)
    angle = -OMEGA * (slow_ref[0] - base) * DEPTH_STEP
    cosine = jnp.cos(angle)
    sine = jnp.sin(angle)
    o_ref[0] = real_in * cosine - imag_in * sine
    o_ref[1] = real_in * sine + imag_in * cosine
    o_ref[2] = cosine
    o_ref[3] = sine


def prelens(wavefield, source, slowness, reflectivity, base):
    _, _, count, length = wavefield.shape
    block = min(count, 32)
    quad = lambda i: (0, 0, i, 0)
    flat = lambda i: (0, i, 0)
    return pl.pallas_call(
        prelens_kernel,
        grid=(count // block,),
        in_specs=[
            pl.BlockSpec(memory_space=pltpu.SMEM),
            pl.BlockSpec((1, 2, block, length), quad),
            pl.BlockSpec((1, 2, block, length), quad),
            pl.BlockSpec((1, block, length), flat),
            pl.BlockSpec((1, block, length), flat),
        ],
        out_specs=pl.BlockSpec((4, block, length), flat),
        out_shape=jax.ShapeDtypeStruct((4, count, length), jnp.float32),
    )(base.reshape(1, 1), wavefield, source, slowness, reflectivity)


def lanes_forward_kernel(pre_ref, hand_ref, w_ref, tw_ref, o_ref):
    outer = tw_ref.shape[1]
    inner = tw_ref.shape[2]
    hand_real = hand_ref[0].astype(jnp.float32)
    hand_imag = hand_ref[1].astype(jnp.float32)
    cosine = pre_ref[2]
    sine = pre_ref[3]
    lensed_real = pre_ref[0] + (hand_real * cosine - hand_imag * sine)
    lensed_imag = pre_ref[1] + (hand_real * sine + hand_imag * cosine)
    slabs = [
        (lensed_real[:, a * inner:(a + 1) * inner], lensed_imag[:, a * inner:(a + 1) * inner])
        for a in range(outer)
    ]
    spec = fft_slabs(slabs, -1)
    both = jnp.concatenate([w_ref[0], w_ref[1]], axis=1)
    count = lensed_real.shape[0]
    for k in range(outer):
        zr, zi = spec[k]
        tr = tw_ref[0, k:k + 1, :]
        ti = tw_ref[1, k:k + 1, :]
        zr, zi = zr * tr - zi * ti, zr * ti + zi * tr
        prod = jnp.dot(
            jnp.concatenate([zr, zi], axis=0), both,
            precision=lax.Precision.HIGH, preferred_element_type=jnp.float32,
        )
        width = o_ref.shape[3]
        dest = (k * inner) // width
        lanes = slice((k * inner) % width, (k * inner) % width + inner)
        o_ref[dest, 0, :, lanes] = prod[:count, :inner] - prod[count:, inner:]
        o_ref[dest, 1, :, lanes] = prod[:count, inner:] + prod[count:, :inner]


def lanes_inverse_kernel(x_ref, src_ref, w_ref, tw_ref, ext_ref, img_ref):
    outer = tw_ref.shape[1]
    inner = tw_ref.shape[2]
    count = x_ref.shape[2]
    both = w_ref[1]
    outs = []
    for k in range(outer):
        width = x_ref.shape[3]
        origin = (k * inner) // width
        lanes = slice((k * inner) % width, (k * inner) % width + inner)
        yr = x_ref[origin, 0, :, lanes]
        yi = x_ref[origin, 1, :, lanes]
        high, low = split_bf16(jnp.concatenate([yr, yi], axis=0))
        prod = jnp.dot(jnp.concatenate([high, low, high], axis=1), both, preferred_element_type=jnp.float32)
        sr = prod[:count, :inner] - prod[count:, inner:]
        si = prod[:count, inner:] + prod[count:, :inner]
        tr = tw_ref[0, k:k + 1, :]
        ti = tw_ref[1, k:k + 1, :]
        outs.append((sr * tr + si * ti, si * tr - sr * ti))
    res = fft_slabs(outs, 1)
    for a in range(outer):
        out_real, out_imag = res[a]
        lanes = slice(a * inner, (a + 1) * inner)
        ext_ref[0, 0, :, lanes] = out_real.astype(ext_ref.dtype)
        ext_ref[0, 1, :, lanes] = out_imag.astype(ext_ref.dtype)
        img_ref[0, :, lanes] = (
            src_ref[0, 0, :, lanes].astype(jnp.float32) * out_real
            + src_ref[0, 1, :, lanes].astype(jnp.float32) * out_imag
        )


def lane_tables(length):
    outer, inner = factor_pair(length)
    real, imag = dft_numpy(inner, -1.0)
    parts = [split_table(np.concatenate([real, sign * imag], axis=1)) for sign in (1.0, -1.0)]
    table = jnp.asarray(np.stack([np.concatenate([hi, hi, lo], axis=0) for hi, lo in parts]))
    turn = jnp.stack(twiddle_table(outer, inner, length, -1.0))
    return outer, inner, table, turn


def lanes_forward(lensed, handed, first, step, groups):
    length = lensed.shape[2]
    outer, inner, _, turn = lane_tables(length)
    table = jnp.stack(dft_table(inner, -1.0))
    block = 64 if step % 64 == 0 and first % 64 == 0 else min(step, 32)
    offset = first // block
    return pl.pallas_call(
        lanes_forward_kernel,
        grid=(step // block,),
        in_specs=[
            pl.BlockSpec((4, block, length), lambda i: (0, offset + i, 0)),
            pl.BlockSpec((2, block, length), lambda i: (0, i, 0)),
            pl.BlockSpec((2, inner, inner), lambda i: (0, 0, 0)),
            pl.BlockSpec((2, outer, inner), lambda i: (0, 0, 0)),
        ],
        out_specs=pl.BlockSpec((groups, 2, block, length // groups), lambda i: (0, 0, i, 0)),
        out_shape=jax.ShapeDtypeStruct((groups, 2, step, length // groups), jnp.float32),
    )(lensed, handed, table, turn)


def lanes_inverse(back, source):
    groups, _, step, width = back.shape
    length = groups * width
    outer, inner, table, turn = lane_tables(length)
    block = min(step, 64)
    return pl.pallas_call(
        lanes_inverse_kernel,
        grid=(step // block,),
        in_specs=[
            pl.BlockSpec((groups, 2, block, width), lambda i: (0, 0, i, 0)),
            pl.BlockSpec((1, 2, block, length), lambda i: (0, 0, i, 0)),
            pl.BlockSpec((2, 3 * inner, 2 * inner), lambda i: (0, 0, 0)),
            pl.BlockSpec((2, outer, inner), lambda i: (0, 0, 0)),
        ],
        out_specs=[
            pl.BlockSpec((1, 2, block, length), lambda i: (0, 0, i, 0)),
            pl.BlockSpec((1, block, length), lambda i: (0, i, 0)),
        ],
        out_shape=[
            jax.ShapeDtypeStruct((1, 2, step, length), jnp.bfloat16),
            jax.ShapeDtypeStruct((1, step, length), jnp.float32),
        ],
    )(back, source, table, turn)


def signed_freq(index, length):
    signed = jnp.where(index < length // 2, index, index - length)
    return signed.astype(jnp.float32) * (2.0 * math.pi / length)


def permuted_freq(position, length):
    outer, inner = factor_pair(length)
    index = position // inner + outer * (position % inner)
    return signed_freq(index, length)


def propagator(freq_row, freq_col, base, scale):
    kz_square = (OMEGA * base) ** 2 - freq_row * freq_row - freq_col * freq_col
    root = jnp.sqrt(jnp.abs(kz_square))
    upward = kz_square >= 0.0
    real_part = jnp.where(upward, jnp.cos(root * DEPTH_STEP), jnp.exp(-root * DEPTH_STEP))
    imag_part = jnp.where(upward, -jnp.sin(root * DEPTH_STEP), jnp.zeros_like(root))
    return (real_part * scale, imag_part * scale)


def lens_rows(wave, handed, source, slow, refl, base):
    wave = wave.astype(jnp.float32)
    handed = handed.astype(jnp.float32)
    source = source.astype(jnp.float32)
    real_in = wave[0] + handed[0] + OMEGA * OMEGA * refl * source[0]
    imag_in = wave[1] + handed[1] + OMEGA * OMEGA * refl * source[1]
    angle = -OMEGA * (slow - base) * DEPTH_STEP
    cosine = jnp.cos(angle)
    sine = jnp.sin(angle)
    return (real_in * cosine - imag_in * sine, real_in * sine + imag_in * cosine)


def body(wavefield, boundary, source, slowness, reflectivity, ref_slowness):
    count = wavefield.shape[2]
    columns = wavefield.shape[3]
    eighth = count // 8
    if count % 8 == 0 and eighth % 8 == 0:
        bounds = [0, 4 * eighth, count]
    else:
        bounds = [0, count]
    groups = lax.axis_size("gx")
    device = lax.axis_index("gx")
    total_rows = count * groups
    width = columns // groups
    scale = 1.0 / (total_rows * columns)
    base = ref_slowness[0]
    pieces = []
    lensed = prelens(wavefield, source, slowness, reflectivity, base)
    for first, last in zip(bounds[:-1], bounds[1:]):
        handed = shifted(boundary[0, :, first:last], "slab", -1)
        field = lanes_forward(lensed, handed, first, last - first, groups)
        pieces.append(lax.all_to_all(field, "gx", split_axis=0, concat_axis=0, tiled=True))
    freq_row = permuted_freq(jnp.arange(total_rows, dtype=jnp.int32), total_rows)
    freq_col = permuted_freq(device * width + jnp.arange(width, dtype=jnp.int32), columns)
    factor = propagator(freq_row[:, None], freq_col[None, :], base, scale)
    spatial = rows_shift(pieces, jnp.stack(factor))
    back = lax.all_to_all(spatial, "gx", split_axis=0, concat_axis=0, tiled=True)
    return lanes_inverse(back, source)


def solution(mesh):
    return jax.shard_map(
        body,
        mesh=mesh,
        in_specs=(
            P("slab", None, "gx", None),
            P("slab", None, "gx", None),
            P("slab", None, "gx", None),
            P("slab", "gx", None),
            P("slab", "gx", None),
            P("slab"),
        ),
        out_specs=(P("slab", None, "gx", None), P("slab", "gx", None)),
        check_vma=False,
    )
```

```python
from functools import partial
import math

import jax
import ml_dtypes
import numpy as np
import jax.numpy as jnp
from jax import lax
from jax.sharding import PartitionSpec as P
from jax.experimental import pallas as pl
from jax.experimental.pallas import tpu as pltpu

OMEGA = 2.5
DEPTH_STEP = 1.0
precise = lax.Precision.HIGHEST


def shifted(block, axis, distance):
    devices = range(lax.axis_size(axis))
    route = [(i - distance, i) for i in devices if i - distance in devices]
    return lax.ppermute(block, axis, route)


def factor_pair(length):
    outer = math.gcd(length, 16)
    return (outer, length // outer)


def dft_table(length, orient):
    position = jnp.arange(length, dtype=jnp.int32)
    product = position[:, None] * position[None, :] % length
    angle = orient * 2.0 * math.pi * product.astype(jnp.float32) / length
    return (jnp.cos(angle), jnp.sin(angle))


def twiddle_table(first, second, length, orient):
    product = (
        jnp.arange(first, dtype=jnp.int32)[:, None]
        * jnp.arange(second, dtype=jnp.int32)[None, :]
        % length
    )
    angle = orient * 2.0 * math.pi * product.astype(jnp.float32) / length
    return (jnp.cos(angle), jnp.sin(angle))


def complex_einsum(form, table, field):
    mixing = partial(jnp.einsum, form, precision=precise)
    return (
        mixing(table[0], field[0]) - mixing(table[1], field[1]),
        mixing(table[0], field[1]) + mixing(table[1], field[0]),
    )


def times_complex(field, factor):
    return (
        field[0] * factor[0] - field[1] * factor[1],
        field[0] * factor[1] + field[1] * factor[0],
    )


def columns_forward(field):
    count, length = field[0].shape
    outer, inner = factor_pair(length)
    shaped = tuple((part.reshape(count, outer, inner) for part in field))
    section = complex_einsum("ka,rab->rkb", dft_table(outer, -1.0), shaped)
    section = times_complex(section, twiddle_table(outer, inner, length, -1.0))
    section = complex_einsum("mb,rkb->rkm", dft_table(inner, -1.0), section)
    return tuple((part.reshape(count, length) for part in section))


def columns_inverse(field):
    count, length = field[0].shape
    outer, inner = factor_pair(length)
    shaped = tuple((part.reshape(count, outer, inner) for part in field))
    section = complex_einsum("mb,rkm->rkb", dft_table(inner, 1.0), shaped)
    section = times_complex(section, twiddle_table(outer, inner, length, 1.0))
    section = complex_einsum("ka,rkb->rab", dft_table(outer, 1.0), section)
    return tuple((part.reshape(count, length) for part in section))


def rows_forward(field):
    length, count = field[0].shape
    outer, inner = factor_pair(length)
    shaped = tuple((part.reshape(outer, inner, count) for part in field))
    section = complex_einsum("ka,abc->kbc", dft_table(outer, -1.0), shaped)
    turned = twiddle_table(outer, inner, length, -1.0)
    section = times_complex(section, (turned[0][:, :, None], turned[1][:, :, None]))
    section = complex_einsum("mb,kbc->kmc", dft_table(inner, -1.0), section)
    return tuple((part.reshape(length, count) for part in section))


def rows_inverse(field):
    length, count = field[0].shape
    outer, inner = factor_pair(length)
    shaped = tuple((part.reshape(outer, inner, count) for part in field))
    section = complex_einsum("mb,kmc->kbc", dft_table(inner, 1.0), shaped)
    turned = twiddle_table(outer, inner, length, 1.0)
    section = times_complex(section, (turned[0][:, :, None], turned[1][:, :, None]))
    section = complex_einsum("ka,kbc->abc", dft_table(outer, 1.0), section)
    return tuple((part.reshape(length, count) for part in section))


def rotate(part, step, count):
    step %= count
    if step == 0:
        return part
    if 4 * step == count:
        return (-part[1], part[0])
    if 2 * step == count:
        return (-part[0], -part[1])
    if 4 * step == 3 * count:
        return (part[1], -part[0])
    cosine = math.cos(2.0 * math.pi * step / count)
    sine = math.sin(2.0 * math.pi * step / count)
    return (part[0] * cosine - part[1] * sine, part[0] * sine + part[1] * cosine)


def fft_slabs(parts, orient):
    count = len(parts)
    if count == 1:
        return list(parts)
    even = fft_slabs(parts[0::2], orient)
    odd = fft_slabs(parts[1::2], orient)
    half = count // 2
    out = [None] * count
    for k in range(half):
        turned = rotate(odd[k], orient * k, count)
        out[k] = (even[k][0] + turned[0], even[k][1] + turned[1])
        out[k + half] = (even[k][0] - turned[0], even[k][1] - turned[1])
    return out


def split_bf16(value):
    spread = value * 65537.0
    high = spread - (spread - value)
    return high.astype(jnp.bfloat16), (value - high).astype(jnp.bfloat16)


def split_table(table):
    table = np.asarray(table, np.float32)
    high = table.astype(ml_dtypes.bfloat16)
    low = (table - high.astype(np.float32)).astype(ml_dtypes.bfloat16)
    return high, low


def dft_numpy(length, orient):
    position = np.arange(length)
    angle = orient * 2.0 * np.pi * (position[:, None] * position[None, :] % length) / length
    return np.cos(angle), np.sin(angle)


def stacked_matmul(stacked, real, imag):
    size = real.shape[1]
    rows = stacked.shape[0] // 2
    high, low = split_bf16(jnp.concatenate([real, imag], axis=1))
    both = jnp.concatenate([high, low, high], axis=0)
    prod = jnp.dot(stacked, both, preferred_element_type=jnp.float32)
    return (
        prod[:rows, :size] - prod[rows:, size:],
        prod[:rows, size:] + prod[rows:, :size],
    )


def rows_kernel(*refs):
    x_refs = refs[:-4]
    p_ref, w_ref, tw_ref, o_ref = refs[-4:]
    outer = tw_ref.shape[1]
    inner = tw_ref.shape[2]
    count = sum(ref.shape[2] for ref in x_refs)

    def place(a):
        return (a * inner) // count, slice((a * inner) % count, (a * inner) % count + inner)

    sizes = [ref.shape[2] for ref in x_refs]
    starts = [sum(sizes[:i]) for i in range(len(sizes))]
    slabs = []
    for a in range(outer):
        origin = (a * inner) // count
        low = (a * inner) % count
        pieces = []
        for ref, start, size in zip(x_refs, starts, sizes):
            top = min(low + inner, start + size)
            bottom = max(low, start)
            if top > bottom:
                pieces.append((ref[origin, 0, bottom - start:top - start, :], ref[origin, 1, bottom - start:top - start, :]))
        if len(pieces) == 1:
            slabs.append(pieces[0])
        else:
            slabs.append((
                jnp.concatenate([p[0] for p in pieces], axis=0),
                jnp.concatenate([p[1] for p in pieces], axis=0),
            ))
    spec = fft_slabs(slabs, -1)
    forward = w_ref[0]
    backward = w_ref[1]
    outs = []
    for k in range(outer):
        zr, zi = spec[k]
        tr = tw_ref[0, k]
        ti = tw_ref[1, k]
        zr, zi = zr * tr - zi * ti, zr * ti + zi * tr
        yr, yi = stacked_matmul(forward, zr, zi)
        pr = p_ref[0, k * inner:(k + 1) * inner, :]
        pi = p_ref[1, k * inner:(k + 1) * inner, :]
        yr, yi = yr * pr - yi * pi, yr * pi + yi * pr
        sr, si = stacked_matmul(backward, yr, yi)
        outs.append((sr * tr + si * ti, si * tr - sr * ti))
    res = fft_slabs(outs, 1)
    for a in range(outer):
        origin, rows = place(a)
        o_ref[origin, 0, rows, :] = res[a][0]
        o_ref[origin, 1, rows, :] = res[a][1]


def rows_shift(turned, factor):
    groups, _, _, width = turned[0].shape
    count = sum(piece.shape[2] for piece in turned)
    length = groups * count
    outer, inner = factor_pair(length)
    block = min(width, 128)
    real, imag = dft_numpy(inner, -1.0)
    turn = twiddle_table(outer, inner, length, -1.0)
    turn = jnp.stack(turn)[..., None]
    parts = [split_table(np.concatenate([real, sign * imag], axis=0)) for sign in (1.0, -1.0)]
    table = jnp.asarray(np.stack([np.concatenate([hi, hi, lo], axis=1) for hi, lo in parts]))
    return pl.pallas_call(
        rows_kernel,
        grid=(width // block,),
        in_specs=[pl.BlockSpec((groups, 2, piece.shape[2], block), lambda j: (0, 0, 0, j)) for piece in turned] + [
            pl.BlockSpec((2, length, block), lambda j: (0, 0, j)),
            pl.BlockSpec((2, 2 * inner, 3 * inner), lambda j: (0, 0, 0)),
            pl.BlockSpec((2, outer, inner, 1), lambda j: (0, 0, 0, 0)),
        ],
        out_specs=pl.BlockSpec((groups, 2, count, block), lambda j: (0, 0, 0, j)),
        out_shape=jax.ShapeDtypeStruct((groups, 2, count, width), jnp.float32),
    )(*turned, factor, table, turn)


def prelens_kernel(base_ref, wave_ref, src_ref, slow_ref, refl_ref, o_ref):
    base = base_ref[0, 0]
    gain = OMEGA * OMEGA * refl_ref[0]
    real_in = wave_ref[0, 0].astype(jnp.float32) + gain * src_ref[0, 0].astype(jnp.float32)
    imag_in = wave_ref[0, 1].astype(jnp.float32) + gain * src_ref[0, 1].astype(jnp.float32)
    angle = -OMEGA * (slow_ref[0] - base) * DEPTH_STEP
    cosine = jnp.cos(angle)
    sine = jnp.sin(angle)
    o_ref[0] = real_in * cosine - imag_in * sine
    o_ref[1] = real_in * sine + imag_in * cosine
    o_ref[2] = cosine
    o_ref[3] = sine


def prelens(wavefield, source, slowness, reflectivity, base):
    _, _, count, length = wavefield.shape
    block = min(count, 32)
    quad = lambda i: (0, 0, i, 0)
    flat = lambda i: (0, i, 0)
    return pl.pallas_call(
        prelens_kernel,
        grid=(count // block,),
        in_specs=[
            pl.BlockSpec(memory_space=pltpu.SMEM),
            pl.BlockSpec((1, 2, block, length), quad),
            pl.BlockSpec((1, 2, block, length), quad),
            pl.BlockSpec((1, block, length), flat),
            pl.BlockSpec((1, block, length), flat),
        ],
        out_specs=pl.BlockSpec((4, block, length), flat),
        out_shape=jax.ShapeDtypeStruct((4, count, length), jnp.float32),
    )(base.reshape(1, 1), wavefield, source, slowness, reflectivity)


def lanes_forward_kernel(pre_ref, hand_ref, w_ref, tw_ref, o_ref):
    outer = tw_ref.shape[1]
    inner = tw_ref.shape[2]
    hand_real = hand_ref[0].astype(jnp.float32)
    hand_imag = hand_ref[1].astype(jnp.float32)
    cosine = pre_ref[2]
    sine = pre_ref[3]
    lensed_real = pre_ref[0] + (hand_real * cosine - hand_imag * sine)
    lensed_imag = pre_ref[1] + (hand_real * sine + hand_imag * cosine)
    slabs = [
        (lensed_real[:, a * inner:(a + 1) * inner], lensed_imag[:, a * inner:(a + 1) * inner])
        for a in range(outer)
    ]
    spec = fft_slabs(slabs, -1)
    both = w_ref[0]
    count = lensed_real.shape[0]
    for k in range(outer):
        zr, zi = spec[k]
        tr = tw_ref[0, k:k + 1, :]
        ti = tw_ref[1, k:k + 1, :]
        zr, zi = zr * tr - zi * ti, zr * ti + zi * tr
        high, low = split_bf16(jnp.concatenate([zr, zi], axis=0))
        prod = jnp.dot(jnp.concatenate([high, low, high], axis=1), both, preferred_element_type=jnp.float32)
        width = o_ref.shape[3]
        dest = (k * inner) // width
        lanes = slice((k * inner) % width, (k * inner) % width + inner)
        o_ref[dest, 0, :, lanes] = prod[:count, :inner] - prod[count:, inner:]
        o_ref[dest, 1, :, lanes] = prod[:count, inner:] + prod[count:, :inner]


def lanes_inverse_kernel(x_ref, src_ref, w_ref, tw_ref, ext_ref, img_ref):
    outer = tw_ref.shape[1]
    inner = tw_ref.shape[2]
    count = x_ref.shape[2]
    both = w_ref[1]
    outs = []
    for k in range(outer):
        width = x_ref.shape[3]
        origin = (k * inner) // width
        lanes = slice((k * inner) % width, (k * inner) % width + inner)
        yr = x_ref[origin, 0, :, lanes]
        yi = x_ref[origin, 1, :, lanes]
        high, low = split_bf16(jnp.concatenate([yr, yi], axis=0))
        prod = jnp.dot(jnp.concatenate([high, low, high], axis=1), both, preferred_element_type=jnp.float32)
        sr = prod[:count, :inner] - prod[count:, inner:]
        si = prod[:count, inner:] + prod[count:, :inner]
        tr = tw_ref[0, k:k + 1, :]
        ti = tw_ref[1, k:k + 1, :]
        outs.append((sr * tr + si * ti, si * tr - sr * ti))
    res = fft_slabs(outs, 1)
    for a in range(outer):
        out_real, out_imag = res[a]
        lanes = slice(a * inner, (a + 1) * inner)
        ext_ref[0, 0, :, lanes] = out_real.astype(ext_ref.dtype)
        ext_ref[0, 1, :, lanes] = out_imag.astype(ext_ref.dtype)
        img_ref[0, :, lanes] = (
            src_ref[0, 0, :, lanes].astype(jnp.float32) * out_real
            + src_ref[0, 1, :, lanes].astype(jnp.float32) * out_imag
        )


def lane_tables(length):
    outer, inner = factor_pair(length)
    real, imag = dft_numpy(inner, -1.0)
    parts = [split_table(np.concatenate([real, sign * imag], axis=1)) for sign in (1.0, -1.0)]
    table = jnp.asarray(np.stack([np.concatenate([hi, hi, lo], axis=0) for hi, lo in parts]))
    turn = jnp.stack(twiddle_table(outer, inner, length, -1.0))
    return outer, inner, table, turn


def lanes_forward(lensed, handed, first, step, groups):
    length = lensed.shape[2]
    outer, inner, table, turn = lane_tables(length)
    block = 64 if step % 64 == 0 and first % 64 == 0 else min(step, 32)
    offset = first // block
    return pl.pallas_call(
        lanes_forward_kernel,
        grid=(step // block,),
        in_specs=[
            pl.BlockSpec((4, block, length), lambda i: (0, offset + i, 0)),
            pl.BlockSpec((2, block, length), lambda i: (0, i, 0)),
            pl.BlockSpec((2, 3 * inner, 2 * inner), lambda i: (0, 0, 0)),
            pl.BlockSpec((2, outer, inner), lambda i: (0, 0, 0)),
        ],
        out_specs=pl.BlockSpec((groups, 2, block, length // groups), lambda i: (0, 0, i, 0)),
        out_shape=jax.ShapeDtypeStruct((groups, 2, step, length // groups), jnp.float32),
    )(lensed, handed, table, turn)


def lanes_inverse(back, source):
    groups, _, step, width = back.shape
    length = groups * width
    outer, inner, table, turn = lane_tables(length)
    block = min(step, 128)
    return pl.pallas_call(
        lanes_inverse_kernel,
        grid=(step // block,),
        in_specs=[
            pl.BlockSpec((groups, 2, block, width), lambda i: (0, 0, i, 0)),
            pl.BlockSpec((1, 2, block, length), lambda i: (0, 0, i, 0)),
            pl.BlockSpec((2, 3 * inner, 2 * inner), lambda i: (0, 0, 0)),
            pl.BlockSpec((2, outer, inner), lambda i: (0, 0, 0)),
        ],
        out_specs=[
            pl.BlockSpec((1, 2, block, length), lambda i: (0, 0, i, 0)),
            pl.BlockSpec((1, block, length), lambda i: (0, i, 0)),
        ],
        out_shape=[
            jax.ShapeDtypeStruct((1, 2, step, length), jnp.bfloat16),
            jax.ShapeDtypeStruct((1, step, length), jnp.float32),
        ],
    )(back, source, table, turn)


def signed_freq(index, length):
    signed = jnp.where(index < length // 2, index, index - length)
    return signed.astype(jnp.float32) * (2.0 * math.pi / length)


def permuted_freq(position, length):
    outer, inner = factor_pair(length)
    index = position // inner + outer * (position % inner)
    return signed_freq(index, length)


def propagator(freq_row, freq_col, base, scale):
    kz_square = (OMEGA * base) ** 2 - freq_row * freq_row - freq_col * freq_col
    root = jnp.sqrt(jnp.abs(kz_square))
    upward = kz_square >= 0.0
    real_part = jnp.where(upward, jnp.cos(root * DEPTH_STEP), jnp.exp(-root * DEPTH_STEP))
    imag_part = jnp.where(upward, -jnp.sin(root * DEPTH_STEP), jnp.zeros_like(root))
    return (real_part * scale, imag_part * scale)


def lens_rows(wave, handed, source, slow, refl, base):
    wave = wave.astype(jnp.float32)
    handed = handed.astype(jnp.float32)
    source = source.astype(jnp.float32)
    real_in = wave[0] + handed[0] + OMEGA * OMEGA * refl * source[0]
    imag_in = wave[1] + handed[1] + OMEGA * OMEGA * refl * source[1]
    angle = -OMEGA * (slow - base) * DEPTH_STEP
    cosine = jnp.cos(angle)
    sine = jnp.sin(angle)
    return (real_in * cosine - imag_in * sine, real_in * sine + imag_in * cosine)


def body(wavefield, boundary, source, slowness, reflectivity, ref_slowness):
    count = wavefield.shape[2]
    columns = wavefield.shape[3]
    eighth = count // 8
    if count % 8 == 0 and eighth % 8 == 0:
        bounds = [0, 4 * eighth, count]
    else:
        bounds = [0, count]
    groups = lax.axis_size("gx")
    device = lax.axis_index("gx")
    total_rows = count * groups
    width = columns // groups
    scale = 1.0 / (total_rows * columns)
    base = ref_slowness[0]
    pieces = []
    lensed = prelens(wavefield, source, slowness, reflectivity, base)
    for first, last in zip(bounds[:-1], bounds[1:]):
        handed = shifted(boundary[0, :, first:last], "slab", -1)
        field = lanes_forward(lensed, handed, first, last - first, groups)
        pieces.append(lax.all_to_all(field, "gx", split_axis=0, concat_axis=0, tiled=True))
    freq_row = permuted_freq(jnp.arange(total_rows, dtype=jnp.int32), total_rows)
    freq_col = permuted_freq(device * width + jnp.arange(width, dtype=jnp.int32), columns)
    factor = propagator(freq_row[:, None], freq_col[None, :], base, scale)
    spatial = rows_shift(pieces, jnp.stack(factor))
    back = lax.all_to_all(spatial, "gx", split_axis=0, concat_axis=0, tiled=True)
    return lanes_inverse(back, source)


def solution(mesh):
    return jax.shard_map(
        body,
        mesh=mesh,
        in_specs=(
            P("slab", None, "gx", None),
            P("slab", None, "gx", None),
            P("slab", None, "gx", None),
            P("slab", "gx", None),
            P("slab", "gx", None),
            P("slab"),
        ),
        out_specs=(P("slab", None, "gx", None), P("slab", "gx", None)),
        check_vma=False,
    )
```

```python
from functools import partial
import math

import jax
import ml_dtypes
import numpy as np
import jax.numpy as jnp
from jax import lax
from jax.sharding import PartitionSpec as P
from jax.experimental import pallas as pl
from jax.experimental.pallas import tpu as pltpu

OMEGA = 2.5
DEPTH_STEP = 1.0
precise = lax.Precision.HIGHEST


def shifted(block, axis, distance):
    devices = range(lax.axis_size(axis))
    route = [(i - distance, i) for i in devices if i - distance in devices]
    return lax.ppermute(block, axis, route)


def factor_pair(length):
    outer = math.gcd(length, 16)
    return (outer, length // outer)


def dft_table(length, orient):
    position = jnp.arange(length, dtype=jnp.int32)
    product = position[:, None] * position[None, :] % length
    angle = orient * 2.0 * math.pi * product.astype(jnp.float32) / length
    return (jnp.cos(angle), jnp.sin(angle))


def twiddle_table(first, second, length, orient):
    product = (
        jnp.arange(first, dtype=jnp.int32)[:, None]
        * jnp.arange(second, dtype=jnp.int32)[None, :]
        % length
    )
    angle = orient * 2.0 * math.pi * product.astype(jnp.float32) / length
    return (jnp.cos(angle), jnp.sin(angle))


def complex_einsum(form, table, field):
    mixing = partial(jnp.einsum, form, precision=precise)
    return (
        mixing(table[0], field[0]) - mixing(table[1], field[1]),
        mixing(table[0], field[1]) + mixing(table[1], field[0]),
    )


def times_complex(field, factor):
    return (
        field[0] * factor[0] - field[1] * factor[1],
        field[0] * factor[1] + field[1] * factor[0],
    )


def columns_forward(field):
    count, length = field[0].shape
    outer, inner = factor_pair(length)
    shaped = tuple((part.reshape(count, outer, inner) for part in field))
    section = complex_einsum("ka,rab->rkb", dft_table(outer, -1.0), shaped)
    section = times_complex(section, twiddle_table(outer, inner, length, -1.0))
    section = complex_einsum("mb,rkb->rkm", dft_table(inner, -1.0), section)
    return tuple((part.reshape(count, length) for part in section))


def columns_inverse(field):
    count, length = field[0].shape
    outer, inner = factor_pair(length)
    shaped = tuple((part.reshape(count, outer, inner) for part in field))
    section = complex_einsum("mb,rkm->rkb", dft_table(inner, 1.0), shaped)
    section = times_complex(section, twiddle_table(outer, inner, length, 1.0))
    section = complex_einsum("ka,rkb->rab", dft_table(outer, 1.0), section)
    return tuple((part.reshape(count, length) for part in section))


def rows_forward(field):
    length, count = field[0].shape
    outer, inner = factor_pair(length)
    shaped = tuple((part.reshape(outer, inner, count) for part in field))
    section = complex_einsum("ka,abc->kbc", dft_table(outer, -1.0), shaped)
    turned = twiddle_table(outer, inner, length, -1.0)
    section = times_complex(section, (turned[0][:, :, None], turned[1][:, :, None]))
    section = complex_einsum("mb,kbc->kmc", dft_table(inner, -1.0), section)
    return tuple((part.reshape(length, count) for part in section))


def rows_inverse(field):
    length, count = field[0].shape
    outer, inner = factor_pair(length)
    shaped = tuple((part.reshape(outer, inner, count) for part in field))
    section = complex_einsum("mb,kmc->kbc", dft_table(inner, 1.0), shaped)
    turned = twiddle_table(outer, inner, length, 1.0)
    section = times_complex(section, (turned[0][:, :, None], turned[1][:, :, None]))
    section = complex_einsum("ka,kbc->abc", dft_table(outer, 1.0), section)
    return tuple((part.reshape(length, count) for part in section))


def rotate(part, step, count):
    step %= count
    if step == 0:
        return part
    if 4 * step == count:
        return (-part[1], part[0])
    if 2 * step == count:
        return (-part[0], -part[1])
    if 4 * step == 3 * count:
        return (part[1], -part[0])
    cosine = math.cos(2.0 * math.pi * step / count)
    sine = math.sin(2.0 * math.pi * step / count)
    return (part[0] * cosine - part[1] * sine, part[0] * sine + part[1] * cosine)


def fft_slabs(parts, orient):
    count = len(parts)
    if count == 1:
        return list(parts)
    even = fft_slabs(parts[0::2], orient)
    odd = fft_slabs(parts[1::2], orient)
    half = count // 2
    out = [None] * count
    for k in range(half):
        turned = rotate(odd[k], orient * k, count)
        out[k] = (even[k][0] + turned[0], even[k][1] + turned[1])
        out[k + half] = (even[k][0] - turned[0], even[k][1] - turned[1])
    return out


def split_bf16(value):
    spread = value * 65537.0
    high = spread - (spread - value)
    return high.astype(jnp.bfloat16), (value - high).astype(jnp.bfloat16)


def split_table(table):
    table = np.asarray(table, np.float32)
    high = table.astype(ml_dtypes.bfloat16)
    low = (table - high.astype(np.float32)).astype(ml_dtypes.bfloat16)
    return high, low


def dft_numpy(length, orient):
    position = np.arange(length)
    angle = orient * 2.0 * np.pi * (position[:, None] * position[None, :] % length) / length
    return np.cos(angle), np.sin(angle)


def stacked_matmul(stacked, real, imag):
    size = real.shape[1]
    rows = stacked.shape[0] // 2
    high, low = split_bf16(jnp.concatenate([real, imag], axis=1))
    both = jnp.concatenate([high, low, high], axis=0)
    prod = jnp.dot(stacked, both, preferred_element_type=jnp.float32)
    return (
        prod[:rows, :size] - prod[rows:, size:],
        prod[:rows, size:] + prod[rows:, :size],
    )


def rows_kernel(*refs):
    x_refs = refs[:-4]
    p_ref, w_ref, tw_ref, o_ref = refs[-4:]
    outer = tw_ref.shape[1]
    inner = tw_ref.shape[2]
    count = sum(ref.shape[2] for ref in x_refs)

    def place(a):
        return (a * inner) // count, slice((a * inner) % count, (a * inner) % count + inner)

    sizes = [ref.shape[2] for ref in x_refs]
    starts = [sum(sizes[:i]) for i in range(len(sizes))]
    slabs = []
    for a in range(outer):
        origin = (a * inner) // count
        low = (a * inner) % count
        pieces = []
        for ref, start, size in zip(x_refs, starts, sizes):
            top = min(low + inner, start + size)
            bottom = max(low, start)
            if top > bottom:
                pieces.append((ref[origin, 0, bottom - start:top - start, :], ref[origin, 1, bottom - start:top - start, :]))
        if len(pieces) == 1:
            slabs.append(pieces[0])
        else:
            slabs.append((
                jnp.concatenate([p[0] for p in pieces], axis=0),
                jnp.concatenate([p[1] for p in pieces], axis=0),
            ))
    spec = fft_slabs(slabs, -1)
    forward = w_ref[0]
    backward = w_ref[1]
    outs = []
    for k in range(outer):
        zr, zi = spec[k]
        tr = tw_ref[0, k]
        ti = tw_ref[1, k]
        zr, zi = zr * tr - zi * ti, zr * ti + zi * tr
        yr, yi = stacked_matmul(forward, zr, zi)
        pr = p_ref[0, k * inner:(k + 1) * inner, :]
        pi = p_ref[1, k * inner:(k + 1) * inner, :]
        yr, yi = yr * pr - yi * pi, yr * pi + yi * pr
        sr, si = stacked_matmul(backward, yr, yi)
        outs.append((sr * tr + si * ti, si * tr - sr * ti))
    res = fft_slabs(outs, 1)
    for a in range(outer):
        origin, rows = place(a)
        o_ref[origin, 0, rows, :] = res[a][0]
        o_ref[origin, 1, rows, :] = res[a][1]


def rows_shift(turned, factor):
    groups, _, _, width = turned[0].shape
    count = sum(piece.shape[2] for piece in turned)
    length = groups * count
    outer, inner = factor_pair(length)
    block = min(width, 128)
    real, imag = dft_numpy(inner, -1.0)
    turn = twiddle_table(outer, inner, length, -1.0)
    turn = jnp.stack(turn)[..., None]
    parts = [split_table(np.concatenate([real, sign * imag], axis=0)) for sign in (1.0, -1.0)]
    table = jnp.asarray(np.stack([np.concatenate([hi, hi, lo], axis=1) for hi, lo in parts]))
    return pl.pallas_call(
        rows_kernel,
        grid=(width // block,),
        in_specs=[pl.BlockSpec((groups, 2, piece.shape[2], block), lambda j: (0, 0, 0, j)) for piece in turned] + [
            pl.BlockSpec((2, length, block), lambda j: (0, 0, j)),
            pl.BlockSpec((2, 2 * inner, 3 * inner), lambda j: (0, 0, 0)),
            pl.BlockSpec((2, outer, inner, 1), lambda j: (0, 0, 0, 0)),
        ],
        out_specs=pl.BlockSpec((groups, 2, count, block), lambda j: (0, 0, 0, j)),
        out_shape=jax.ShapeDtypeStruct((groups, 2, count, width), jnp.float32),
    )(*turned, factor, table, turn)


def prelens_kernel(base_ref, wave_ref, src_ref, slow_ref, refl_ref, o_ref):
    base = base_ref[0, 0]
    gain = OMEGA * OMEGA * refl_ref[0]
    real_in = wave_ref[0, 0].astype(jnp.float32) + gain * src_ref[0, 0].astype(jnp.float32)
    imag_in = wave_ref[0, 1].astype(jnp.float32) + gain * src_ref[0, 1].astype(jnp.float32)
    angle = -OMEGA * (slow_ref[0] - base) * DEPTH_STEP
    cosine = jnp.cos(angle)
    sine = jnp.sin(angle)
    o_ref[0] = real_in * cosine - imag_in * sine
    o_ref[1] = real_in * sine + imag_in * cosine
    o_ref[2] = cosine
    o_ref[3] = sine


def prelens(wavefield, source, slowness, reflectivity, base):
    _, _, count, length = wavefield.shape
    block = min(count, 64)
    quad = lambda i: (0, 0, i, 0)
    flat = lambda i: (0, i, 0)
    return pl.pallas_call(
        prelens_kernel,
        grid=(count // block,),
        in_specs=[
            pl.BlockSpec(memory_space=pltpu.SMEM),
            pl.BlockSpec((1, 2, block, length), quad),
            pl.BlockSpec((1, 2, block, length), quad),
            pl.BlockSpec((1, block, length), flat),
            pl.BlockSpec((1, block, length), flat),
        ],
        out_specs=pl.BlockSpec((4, block, length), flat),
        out_shape=jax.ShapeDtypeStruct((4, count, length), jnp.float32),
    )(base.reshape(1, 1), wavefield, source, slowness, reflectivity)


def lanes_forward_kernel(pre_ref, hand_ref, w_ref, tw_ref, o_ref):
    outer = tw_ref.shape[1]
    inner = tw_ref.shape[2]
    hand_real = hand_ref[0].astype(jnp.float32)
    hand_imag = hand_ref[1].astype(jnp.float32)
    cosine = pre_ref[2]
    sine = pre_ref[3]
    lensed_real = pre_ref[0] + (hand_real * cosine - hand_imag * sine)
    lensed_imag = pre_ref[1] + (hand_real * sine + hand_imag * cosine)
    slabs = [
        (lensed_real[:, a * inner:(a + 1) * inner], lensed_imag[:, a * inner:(a + 1) * inner])
        for a in range(outer)
    ]
    spec = fft_slabs(slabs, -1)
    both = w_ref[0]
    count = lensed_real.shape[0]
    for k in range(outer):
        zr, zi = spec[k]
        tr = tw_ref[0, k:k + 1, :]
        ti = tw_ref[1, k:k + 1, :]
        zr, zi = zr * tr - zi * ti, zr * ti + zi * tr
        high, low = split_bf16(jnp.concatenate([zr, zi], axis=0))
        prod = jnp.dot(jnp.concatenate([high, low, high], axis=1), both, preferred_element_type=jnp.float32)
        width = o_ref.shape[3]
        dest = (k * inner) // width
        lanes = slice((k * inner) % width, (k * inner) % width + inner)
        o_ref[dest, 0, :, lanes] = prod[:count, :inner] - prod[count:, inner:]
        o_ref[dest, 1, :, lanes] = prod[:count, inner:] + prod[count:, :inner]


def lanes_inverse_kernel(x_ref, src_ref, w_ref, tw_ref, ext_ref, img_ref):
    outer = tw_ref.shape[1]
    inner = tw_ref.shape[2]
    count = x_ref.shape[2]
    both = w_ref[1]
    outs = []
    for k in range(outer):
        width = x_ref.shape[3]
        origin = (k * inner) // width
        lanes = slice((k * inner) % width, (k * inner) % width + inner)
        yr = x_ref[origin, 0, :, lanes]
        yi = x_ref[origin, 1, :, lanes]
        high, low = split_bf16(jnp.concatenate([yr, yi], axis=0))
        prod = jnp.dot(jnp.concatenate([high, low, high], axis=1), both, preferred_element_type=jnp.float32)
        sr = prod[:count, :inner] - prod[count:, inner:]
        si = prod[:count, inner:] + prod[count:, :inner]
        tr = tw_ref[0, k:k + 1, :]
        ti = tw_ref[1, k:k + 1, :]
        outs.append((sr * tr + si * ti, si * tr - sr * ti))
    res = fft_slabs(outs, 1)
    for a in range(outer):
        out_real, out_imag = res[a]
        lanes = slice(a * inner, (a + 1) * inner)
        ext_ref[0, 0, :, lanes] = out_real.astype(ext_ref.dtype)
        ext_ref[0, 1, :, lanes] = out_imag.astype(ext_ref.dtype)
        img_ref[0, :, lanes] = (
            src_ref[0, 0, :, lanes].astype(jnp.float32) * out_real
            + src_ref[0, 1, :, lanes].astype(jnp.float32) * out_imag
        )


def lane_tables(length):
    outer, inner = factor_pair(length)
    real, imag = dft_numpy(inner, -1.0)
    parts = [split_table(np.concatenate([real, sign * imag], axis=1)) for sign in (1.0, -1.0)]
    table = jnp.asarray(np.stack([np.concatenate([hi, hi, lo], axis=0) for hi, lo in parts]))
    turn = jnp.stack(twiddle_table(outer, inner, length, -1.0))
    return outer, inner, table, turn


def lanes_forward(lensed, handed, first, step, groups):
    length = lensed.shape[2]
    outer, inner, table, turn = lane_tables(length)
    block = 64 if step % 64 == 0 and first % 64 == 0 else min(step, 32)
    offset = first // block
    return pl.pallas_call(
        lanes_forward_kernel,
        grid=(step // block,),
        in_specs=[
            pl.BlockSpec((4, block, length), lambda i: (0, offset + i, 0)),
            pl.BlockSpec((2, block, length), lambda i: (0, i, 0)),
            pl.BlockSpec((2, 3 * inner, 2 * inner), lambda i: (0, 0, 0)),
            pl.BlockSpec((2, outer, inner), lambda i: (0, 0, 0)),
        ],
        out_specs=pl.BlockSpec((groups, 2, block, length // groups), lambda i: (0, 0, i, 0)),
        out_shape=jax.ShapeDtypeStruct((groups, 2, step, length // groups), jnp.float32),
    )(lensed, handed, table, turn)


def lanes_inverse(back, source):
    groups, _, step, width = back.shape
    length = groups * width
    outer, inner, table, turn = lane_tables(length)
    block = min(step, 128)
    return pl.pallas_call(
        lanes_inverse_kernel,
        grid=(step // block,),
        in_specs=[
            pl.BlockSpec((groups, 2, block, width), lambda i: (0, 0, i, 0)),
            pl.BlockSpec((1, 2, block, length), lambda i: (0, 0, i, 0)),
            pl.BlockSpec((2, 3 * inner, 2 * inner), lambda i: (0, 0, 0)),
            pl.BlockSpec((2, outer, inner), lambda i: (0, 0, 0)),
        ],
        out_specs=[
            pl.BlockSpec((1, 2, block, length), lambda i: (0, 0, i, 0)),
            pl.BlockSpec((1, block, length), lambda i: (0, i, 0)),
        ],
        out_shape=[
            jax.ShapeDtypeStruct((1, 2, step, length), jnp.bfloat16),
            jax.ShapeDtypeStruct((1, step, length), jnp.float32),
        ],
    )(back, source, table, turn)


def signed_freq(index, length):
    signed = jnp.where(index < length // 2, index, index - length)
    return signed.astype(jnp.float32) * (2.0 * math.pi / length)


def permuted_freq(position, length):
    outer, inner = factor_pair(length)
    index = position // inner + outer * (position % inner)
    return signed_freq(index, length)


def propagator(freq_row, freq_col, base, scale):
    kz_square = (OMEGA * base) ** 2 - freq_row * freq_row - freq_col * freq_col
    root = jnp.sqrt(jnp.abs(kz_square))
    upward = kz_square >= 0.0
    real_part = jnp.where(upward, jnp.cos(root * DEPTH_STEP), jnp.exp(-root * DEPTH_STEP))
    imag_part = jnp.where(upward, -jnp.sin(root * DEPTH_STEP), jnp.zeros_like(root))
    return (real_part * scale, imag_part * scale)


def lens_rows(wave, handed, source, slow, refl, base):
    wave = wave.astype(jnp.float32)
    handed = handed.astype(jnp.float32)
    source = source.astype(jnp.float32)
    real_in = wave[0] + handed[0] + OMEGA * OMEGA * refl * source[0]
    imag_in = wave[1] + handed[1] + OMEGA * OMEGA * refl * source[1]
    angle = -OMEGA * (slow - base) * DEPTH_STEP
    cosine = jnp.cos(angle)
    sine = jnp.sin(angle)
    return (real_in * cosine - imag_in * sine, real_in * sine + imag_in * cosine)


def body(wavefield, boundary, source, slowness, reflectivity, ref_slowness):
    count = wavefield.shape[2]
    columns = wavefield.shape[3]
    eighth = count // 8
    if count % 8 == 0 and eighth % 8 == 0:
        bounds = [0, 4 * eighth, count]
    else:
        bounds = [0, count]
    groups = lax.axis_size("gx")
    device = lax.axis_index("gx")
    total_rows = count * groups
    width = columns // groups
    scale = 1.0 / (total_rows * columns)
    base = ref_slowness[0]
    pieces = []
    lensed = prelens(wavefield, source, slowness, reflectivity, base)
    for first, last in zip(bounds[:-1], bounds[1:]):
        handed = shifted(boundary[0, :, first:last], "slab", -1)
        field = lanes_forward(lensed, handed, first, last - first, groups)
        pieces.append(lax.all_to_all(field, "gx", split_axis=0, concat_axis=0, tiled=True))
    freq_row = permuted_freq(jnp.arange(total_rows, dtype=jnp.int32), total_rows)
    freq_col = permuted_freq(device * width + jnp.arange(width, dtype=jnp.int32), columns)
    factor = propagator(freq_row[:, None], freq_col[None, :], base, scale)
    spatial = rows_shift(pieces, jnp.stack(factor))
    back = lax.all_to_all(spatial, "gx", split_axis=0, concat_axis=0, tiled=True)
    return lanes_inverse(back, source)


def solution(mesh):
    return jax.shard_map(
        body,
        mesh=mesh,
        in_specs=(
            P("slab", None, "gx", None),
            P("slab", None, "gx", None),
            P("slab", None, "gx", None),
            P("slab", "gx", None),
            P("slab", "gx", None),
            P("slab"),
        ),
        out_specs=(P("slab", None, "gx", None), P("slab", "gx", None)),
        check_vma=False,
    )
```

```python
from functools import partial
import math

import jax
import ml_dtypes
import numpy as np
import jax.numpy as jnp
from jax import lax
from jax.sharding import PartitionSpec as P
from jax.experimental import pallas as pl
from jax.experimental.pallas import tpu as pltpu

OMEGA = 2.5
DEPTH_STEP = 1.0
precise = lax.Precision.HIGHEST


def shifted(block, axis, distance):
    devices = range(lax.axis_size(axis))
    route = [(i - distance, i) for i in devices if i - distance in devices]
    return lax.ppermute(block, axis, route)


def factor_pair(length):
    outer = math.gcd(length, 16)
    return (outer, length // outer)


def dft_table(length, orient):
    position = jnp.arange(length, dtype=jnp.int32)
    product = position[:, None] * position[None, :] % length
    angle = orient * 2.0 * math.pi * product.astype(jnp.float32) / length
    return (jnp.cos(angle), jnp.sin(angle))


def twiddle_table(first, second, length, orient):
    product = (
        jnp.arange(first, dtype=jnp.int32)[:, None]
        * jnp.arange(second, dtype=jnp.int32)[None, :]
        % length
    )
    angle = orient * 2.0 * math.pi * product.astype(jnp.float32) / length
    return (jnp.cos(angle), jnp.sin(angle))


def complex_einsum(form, table, field):
    mixing = partial(jnp.einsum, form, precision=precise)
    return (
        mixing(table[0], field[0]) - mixing(table[1], field[1]),
        mixing(table[0], field[1]) + mixing(table[1], field[0]),
    )


def times_complex(field, factor):
    return (
        field[0] * factor[0] - field[1] * factor[1],
        field[0] * factor[1] + field[1] * factor[0],
    )


def columns_forward(field):
    count, length = field[0].shape
    outer, inner = factor_pair(length)
    shaped = tuple((part.reshape(count, outer, inner) for part in field))
    section = complex_einsum("ka,rab->rkb", dft_table(outer, -1.0), shaped)
    section = times_complex(section, twiddle_table(outer, inner, length, -1.0))
    section = complex_einsum("mb,rkb->rkm", dft_table(inner, -1.0), section)
    return tuple((part.reshape(count, length) for part in section))


def columns_inverse(field):
    count, length = field[0].shape
    outer, inner = factor_pair(length)
    shaped = tuple((part.reshape(count, outer, inner) for part in field))
    section = complex_einsum("mb,rkm->rkb", dft_table(inner, 1.0), shaped)
    section = times_complex(section, twiddle_table(outer, inner, length, 1.0))
    section = complex_einsum("ka,rkb->rab", dft_table(outer, 1.0), section)
    return tuple((part.reshape(count, length) for part in section))


def rows_forward(field):
    length, count = field[0].shape
    outer, inner = factor_pair(length)
    shaped = tuple((part.reshape(outer, inner, count) for part in field))
    section = complex_einsum("ka,abc->kbc", dft_table(outer, -1.0), shaped)
    turned = twiddle_table(outer, inner, length, -1.0)
    section = times_complex(section, (turned[0][:, :, None], turned[1][:, :, None]))
    section = complex_einsum("mb,kbc->kmc", dft_table(inner, -1.0), section)
    return tuple((part.reshape(length, count) for part in section))


def rows_inverse(field):
    length, count = field[0].shape
    outer, inner = factor_pair(length)
    shaped = tuple((part.reshape(outer, inner, count) for part in field))
    section = complex_einsum("mb,kmc->kbc", dft_table(inner, 1.0), shaped)
    turned = twiddle_table(outer, inner, length, 1.0)
    section = times_complex(section, (turned[0][:, :, None], turned[1][:, :, None]))
    section = complex_einsum("ka,kbc->abc", dft_table(outer, 1.0), section)
    return tuple((part.reshape(length, count) for part in section))


def rotate(part, step, count):
    step %= count
    if step == 0:
        return part
    if 4 * step == count:
        return (-part[1], part[0])
    if 2 * step == count:
        return (-part[0], -part[1])
    if 4 * step == 3 * count:
        return (part[1], -part[0])
    cosine = math.cos(2.0 * math.pi * step / count)
    sine = math.sin(2.0 * math.pi * step / count)
    return (part[0] * cosine - part[1] * sine, part[0] * sine + part[1] * cosine)


def fft_slabs(parts, orient):
    count = len(parts)
    if count == 1:
        return list(parts)
    even = fft_slabs(parts[0::2], orient)
    odd = fft_slabs(parts[1::2], orient)
    half = count // 2
    out = [None] * count
    for k in range(half):
        turned = rotate(odd[k], orient * k, count)
        out[k] = (even[k][0] + turned[0], even[k][1] + turned[1])
        out[k + half] = (even[k][0] - turned[0], even[k][1] - turned[1])
    return out


def split_bf16(value):
    spread = value * 65537.0
    high = spread - (spread - value)
    return high.astype(jnp.bfloat16), (value - high).astype(jnp.bfloat16)


def split_table(table):
    table = np.asarray(table, np.float32)
    high = table.astype(ml_dtypes.bfloat16)
    low = (table - high.astype(np.float32)).astype(ml_dtypes.bfloat16)
    return high, low


def dft_numpy(length, orient):
    position = np.arange(length)
    angle = orient * 2.0 * np.pi * (position[:, None] * position[None, :] % length) / length
    return np.cos(angle), np.sin(angle)


def stacked_matmul(stacked, real, imag):
    size = real.shape[1]
    rows = stacked.shape[0] // 2
    high, low = split_bf16(jnp.concatenate([real, imag], axis=1))
    both = jnp.concatenate([high, low, high], axis=0)
    prod = jnp.dot(stacked, both, preferred_element_type=jnp.float32)
    return (
        prod[:rows, :size] - prod[rows:, size:],
        prod[:rows, size:] + prod[rows:, :size],
    )


def rows_kernel(*refs):
    x_refs = refs[:-4]
    p_ref, w_ref, tw_ref, o_ref = refs[-4:]
    outer = tw_ref.shape[1]
    inner = tw_ref.shape[2]
    count = sum(ref.shape[2] for ref in x_refs)

    def place(a):
        return (a * inner) // count, slice((a * inner) % count, (a * inner) % count + inner)

    sizes = [ref.shape[2] for ref in x_refs]
    starts = [sum(sizes[:i]) for i in range(len(sizes))]
    slabs = []
    for a in range(outer):
        origin = (a * inner) // count
        low = (a * inner) % count
        pieces = []
        for ref, start, size in zip(x_refs, starts, sizes):
            top = min(low + inner, start + size)
            bottom = max(low, start)
            if top > bottom:
                pieces.append((ref[origin, 0, bottom - start:top - start, :], ref[origin, 1, bottom - start:top - start, :]))
        if len(pieces) == 1:
            slabs.append(pieces[0])
        else:
            slabs.append((
                jnp.concatenate([p[0] for p in pieces], axis=0),
                jnp.concatenate([p[1] for p in pieces], axis=0),
            ))
    spec = fft_slabs(slabs, -1)
    forward = w_ref[0]
    backward = w_ref[1]
    outs = []
    for k in range(outer):
        zr, zi = spec[k]
        tr = tw_ref[0, k]
        ti = tw_ref[1, k]
        zr, zi = zr * tr - zi * ti, zr * ti + zi * tr
        yr, yi = stacked_matmul(forward, zr, zi)
        pr = p_ref[0, k * inner:(k + 1) * inner, :]
        pi = p_ref[1, k * inner:(k + 1) * inner, :]
        yr, yi = yr * pr - yi * pi, yr * pi + yi * pr
        sr, si = stacked_matmul(backward, yr, yi)
        outs.append((sr * tr + si * ti, si * tr - sr * ti))
    res = fft_slabs(outs, 1)
    for a in range(outer):
        origin, rows = place(a)
        o_ref[origin, 0, rows, :] = res[a][0]
        o_ref[origin, 1, rows, :] = res[a][1]


def rows_shift(turned, factor):
    groups, _, _, width = turned[0].shape
    count = sum(piece.shape[2] for piece in turned)
    length = groups * count
    outer, inner = factor_pair(length)
    block = min(width, 128)
    real, imag = dft_numpy(inner, -1.0)
    turn = twiddle_table(outer, inner, length, -1.0)
    turn = jnp.stack(turn)[..., None]
    parts = [split_table(np.concatenate([real, sign * imag], axis=0)) for sign in (1.0, -1.0)]
    table = jnp.asarray(np.stack([np.concatenate([hi, hi, lo], axis=1) for hi, lo in parts]))
    return pl.pallas_call(
        rows_kernel,
        grid=(width // block,),
        in_specs=[pl.BlockSpec((groups, 2, piece.shape[2], block), lambda j: (0, 0, 0, j)) for piece in turned] + [
            pl.BlockSpec((2, length, block), lambda j: (0, 0, j)),
            pl.BlockSpec((2, 2 * inner, 3 * inner), lambda j: (0, 0, 0)),
            pl.BlockSpec((2, outer, inner, 1), lambda j: (0, 0, 0, 0)),
        ],
        out_specs=pl.BlockSpec((groups, 2, count, block), lambda j: (0, 0, 0, j)),
        out_shape=jax.ShapeDtypeStruct((groups, 2, count, width), jnp.float32),
    )(*turned, factor, table, turn)


def prelens_kernel(base_ref, wave_ref, src_ref, slow_ref, refl_ref, o_ref):
    base = base_ref[0, 0]
    gain = OMEGA * OMEGA * refl_ref[0]
    real_in = wave_ref[0, 0].astype(jnp.float32) + gain * src_ref[0, 0].astype(jnp.float32)
    imag_in = wave_ref[0, 1].astype(jnp.float32) + gain * src_ref[0, 1].astype(jnp.float32)
    angle = -OMEGA * (slow_ref[0] - base) * DEPTH_STEP
    cosine = jnp.cos(angle)
    sine = jnp.sin(angle)
    o_ref[0] = real_in * cosine - imag_in * sine
    o_ref[1] = real_in * sine + imag_in * cosine
    o_ref[2] = cosine
    o_ref[3] = sine


def prelens(wavefield, source, slowness, reflectivity, base):
    _, _, count, length = wavefield.shape
    block = min(count, 128)
    quad = lambda i: (0, 0, i, 0)
    flat = lambda i: (0, i, 0)
    return pl.pallas_call(
        prelens_kernel,
        grid=(count // block,),
        in_specs=[
            pl.BlockSpec(memory_space=pltpu.SMEM),
            pl.BlockSpec((1, 2, block, length), quad),
            pl.BlockSpec((1, 2, block, length), quad),
            pl.BlockSpec((1, block, length), flat),
            pl.BlockSpec((1, block, length), flat),
        ],
        out_specs=pl.BlockSpec((4, block, length), flat),
        out_shape=jax.ShapeDtypeStruct((4, count, length), jnp.float32),
    )(base.reshape(1, 1), wavefield, source, slowness, reflectivity)


def lanes_forward_kernel(pre_ref, hand_ref, w_ref, tw_ref, o_ref):
    outer = tw_ref.shape[1]
    inner = tw_ref.shape[2]
    hand_real = hand_ref[0].astype(jnp.float32)
    hand_imag = hand_ref[1].astype(jnp.float32)
    cosine = pre_ref[2]
    sine = pre_ref[3]
    lensed_real = pre_ref[0] + (hand_real * cosine - hand_imag * sine)
    lensed_imag = pre_ref[1] + (hand_real * sine + hand_imag * cosine)
    slabs = [
        (lensed_real[:, a * inner:(a + 1) * inner], lensed_imag[:, a * inner:(a + 1) * inner])
        for a in range(outer)
    ]
    spec = fft_slabs(slabs, -1)
    both = w_ref[0]
    count = lensed_real.shape[0]
    for k in range(outer):
        zr, zi = spec[k]
        tr = tw_ref[0, k:k + 1, :]
        ti = tw_ref[1, k:k + 1, :]
        zr, zi = zr * tr - zi * ti, zr * ti + zi * tr
        high, low = split_bf16(jnp.concatenate([zr, zi], axis=0))
        prod = jnp.dot(jnp.concatenate([high, low, high], axis=1), both, preferred_element_type=jnp.float32)
        width = o_ref.shape[3]
        dest = (k * inner) // width
        lanes = slice((k * inner) % width, (k * inner) % width + inner)
        o_ref[dest, 0, :, lanes] = prod[:count, :inner] - prod[count:, inner:]
        o_ref[dest, 1, :, lanes] = prod[:count, inner:] + prod[count:, :inner]


def lanes_inverse_kernel(x_ref, src_ref, w_ref, tw_ref, ext_ref, img_ref):
    outer = tw_ref.shape[1]
    inner = tw_ref.shape[2]
    count = x_ref.shape[2]
    both = w_ref[1]
    outs = []
    for k in range(outer):
        width = x_ref.shape[3]
        origin = (k * inner) // width
        lanes = slice((k * inner) % width, (k * inner) % width + inner)
        yr = x_ref[origin, 0, :, lanes]
        yi = x_ref[origin, 1, :, lanes]
        high, low = split_bf16(jnp.concatenate([yr, yi], axis=0))
        prod = jnp.dot(jnp.concatenate([high, low, high], axis=1), both, preferred_element_type=jnp.float32)
        sr = prod[:count, :inner] - prod[count:, inner:]
        si = prod[:count, inner:] + prod[count:, :inner]
        tr = tw_ref[0, k:k + 1, :]
        ti = tw_ref[1, k:k + 1, :]
        outs.append((sr * tr + si * ti, si * tr - sr * ti))
    res = fft_slabs(outs, 1)
    for a in range(outer):
        out_real, out_imag = res[a]
        lanes = slice(a * inner, (a + 1) * inner)
        ext_ref[0, 0, :, lanes] = out_real.astype(ext_ref.dtype)
        ext_ref[0, 1, :, lanes] = out_imag.astype(ext_ref.dtype)
        img_ref[0, :, lanes] = (
            src_ref[0, 0, :, lanes].astype(jnp.float32) * out_real
            + src_ref[0, 1, :, lanes].astype(jnp.float32) * out_imag
        )


def lane_tables(length):
    outer, inner = factor_pair(length)
    real, imag = dft_numpy(inner, -1.0)
    parts = [split_table(np.concatenate([real, sign * imag], axis=1)) for sign in (1.0, -1.0)]
    table = jnp.asarray(np.stack([np.concatenate([hi, hi, lo], axis=0) for hi, lo in parts]))
    turn = jnp.stack(twiddle_table(outer, inner, length, -1.0))
    return outer, inner, table, turn


def lanes_forward(lensed, handed, first, step, groups):
    length = lensed.shape[2]
    outer, inner, table, turn = lane_tables(length)
    block = 64 if step % 64 == 0 and first % 64 == 0 else min(step, 32)
    offset = first // block
    return pl.pallas_call(
        lanes_forward_kernel,
        grid=(step // block,),
        in_specs=[
            pl.BlockSpec((4, block, length), lambda i: (0, offset + i, 0)),
            pl.BlockSpec((2, block, length), lambda i: (0, i, 0)),
            pl.BlockSpec((2, 3 * inner, 2 * inner), lambda i: (0, 0, 0)),
            pl.BlockSpec((2, outer, inner), lambda i: (0, 0, 0)),
        ],
        out_specs=pl.BlockSpec((groups, 2, block, length // groups), lambda i: (0, 0, i, 0)),
        out_shape=jax.ShapeDtypeStruct((groups, 2, step, length // groups), jnp.float32),
    )(lensed, handed, table, turn)


def lanes_inverse(back, source):
    groups, _, step, width = back.shape
    length = groups * width
    outer, inner, table, turn = lane_tables(length)
    block = min(step, 128)
    return pl.pallas_call(
        lanes_inverse_kernel,
        grid=(step // block,),
        in_specs=[
            pl.BlockSpec((groups, 2, block, width), lambda i: (0, 0, i, 0)),
            pl.BlockSpec((1, 2, block, length), lambda i: (0, 0, i, 0)),
            pl.BlockSpec((2, 3 * inner, 2 * inner), lambda i: (0, 0, 0)),
            pl.BlockSpec((2, outer, inner), lambda i: (0, 0, 0)),
        ],
        out_specs=[
            pl.BlockSpec((1, 2, block, length), lambda i: (0, 0, i, 0)),
            pl.BlockSpec((1, block, length), lambda i: (0, i, 0)),
        ],
        out_shape=[
            jax.ShapeDtypeStruct((1, 2, step, length), jnp.bfloat16),
            jax.ShapeDtypeStruct((1, step, length), jnp.float32),
        ],
    )(back, source, table, turn)


def signed_freq(index, length):
    signed = jnp.where(index < length // 2, index, index - length)
    return signed.astype(jnp.float32) * (2.0 * math.pi / length)


def permuted_freq(position, length):
    outer, inner = factor_pair(length)
    index = position // inner + outer * (position % inner)
    return signed_freq(index, length)


def propagator(freq_row, freq_col, base, scale):
    kz_square = (OMEGA * base) ** 2 - freq_row * freq_row - freq_col * freq_col
    root = jnp.sqrt(jnp.abs(kz_square))
    upward = kz_square >= 0.0
    real_part = jnp.where(upward, jnp.cos(root * DEPTH_STEP), jnp.exp(-root * DEPTH_STEP))
    imag_part = jnp.where(upward, -jnp.sin(root * DEPTH_STEP), jnp.zeros_like(root))
    return (real_part * scale, imag_part * scale)


def lens_rows(wave, handed, source, slow, refl, base):
    wave = wave.astype(jnp.float32)
    handed = handed.astype(jnp.float32)
    source = source.astype(jnp.float32)
    real_in = wave[0] + handed[0] + OMEGA * OMEGA * refl * source[0]
    imag_in = wave[1] + handed[1] + OMEGA * OMEGA * refl * source[1]
    angle = -OMEGA * (slow - base) * DEPTH_STEP
    cosine = jnp.cos(angle)
    sine = jnp.sin(angle)
    return (real_in * cosine - imag_in * sine, real_in * sine + imag_in * cosine)


def body(wavefield, boundary, source, slowness, reflectivity, ref_slowness):
    count = wavefield.shape[2]
    columns = wavefield.shape[3]
    eighth = count // 8
    if count % 8 == 0 and eighth % 8 == 0:
        bounds = [0, 4 * eighth, count]
    else:
        bounds = [0, count]
    groups = lax.axis_size("gx")
    device = lax.axis_index("gx")
    total_rows = count * groups
    width = columns // groups
    scale = 1.0 / (total_rows * columns)
    base = ref_slowness[0]
    pieces = []
    lensed = prelens(wavefield, source, slowness, reflectivity, base)
    for first, last in zip(bounds[:-1], bounds[1:]):
        handed = shifted(boundary[0, :, first:last], "slab", -1)
        field = lanes_forward(lensed, handed, first, last - first, groups)
        pieces.append(lax.all_to_all(field, "gx", split_axis=0, concat_axis=0, tiled=True))
    freq_row = permuted_freq(jnp.arange(total_rows, dtype=jnp.int32), total_rows)
    freq_col = permuted_freq(device * width + jnp.arange(width, dtype=jnp.int32), columns)
    factor = propagator(freq_row[:, None], freq_col[None, :], base, scale)
    spatial = rows_shift(pieces, jnp.stack(factor))
    back = lax.all_to_all(spatial, "gx", split_axis=0, concat_axis=0, tiled=True)
    return lanes_inverse(back, source)


def solution(mesh):
    return jax.shard_map(
        body,
        mesh=mesh,
        in_specs=(
            P("slab", None, "gx", None),
            P("slab", None, "gx", None),
            P("slab", None, "gx", None),
            P("slab", "gx", None),
            P("slab", "gx", None),
            P("slab"),
        ),
        out_specs=(P("slab", None, "gx", None), P("slab", "gx", None)),
        check_vma=False,
    )
```

```python
from functools import partial
import math

import jax
import ml_dtypes
import numpy as np
import jax.numpy as jnp
from jax import lax
from jax.sharding import PartitionSpec as P
from jax.experimental import pallas as pl
from jax.experimental.pallas import tpu as pltpu

OMEGA = 2.5
DEPTH_STEP = 1.0
precise = lax.Precision.HIGHEST


def shifted(block, axis, distance):
    devices = range(lax.axis_size(axis))
    route = [(i - distance, i) for i in devices if i - distance in devices]
    return lax.ppermute(block, axis, route)


def factor_pair(length):
    outer = math.gcd(length, 16)
    return (outer, length // outer)


def dft_table(length, orient):
    position = jnp.arange(length, dtype=jnp.int32)
    product = position[:, None] * position[None, :] % length
    angle = orient * 2.0 * math.pi * product.astype(jnp.float32) / length
    return (jnp.cos(angle), jnp.sin(angle))


def twiddle_table(first, second, length, orient):
    product = (
        jnp.arange(first, dtype=jnp.int32)[:, None]
        * jnp.arange(second, dtype=jnp.int32)[None, :]
        % length
    )
    angle = orient * 2.0 * math.pi * product.astype(jnp.float32) / length
    return (jnp.cos(angle), jnp.sin(angle))


def complex_einsum(form, table, field):
    mixing = partial(jnp.einsum, form, precision=precise)
    return (
        mixing(table[0], field[0]) - mixing(table[1], field[1]),
        mixing(table[0], field[1]) + mixing(table[1], field[0]),
    )


def times_complex(field, factor):
    return (
        field[0] * factor[0] - field[1] * factor[1],
        field[0] * factor[1] + field[1] * factor[0],
    )


def columns_forward(field):
    count, length = field[0].shape
    outer, inner = factor_pair(length)
    shaped = tuple((part.reshape(count, outer, inner) for part in field))
    section = complex_einsum("ka,rab->rkb", dft_table(outer, -1.0), shaped)
    section = times_complex(section, twiddle_table(outer, inner, length, -1.0))
    section = complex_einsum("mb,rkb->rkm", dft_table(inner, -1.0), section)
    return tuple((part.reshape(count, length) for part in section))


def columns_inverse(field):
    count, length = field[0].shape
    outer, inner = factor_pair(length)
    shaped = tuple((part.reshape(count, outer, inner) for part in field))
    section = complex_einsum("mb,rkm->rkb", dft_table(inner, 1.0), shaped)
    section = times_complex(section, twiddle_table(outer, inner, length, 1.0))
    section = complex_einsum("ka,rkb->rab", dft_table(outer, 1.0), section)
    return tuple((part.reshape(count, length) for part in section))


def rows_forward(field):
    length, count = field[0].shape
    outer, inner = factor_pair(length)
    shaped = tuple((part.reshape(outer, inner, count) for part in field))
    section = complex_einsum("ka,abc->kbc", dft_table(outer, -1.0), shaped)
    turned = twiddle_table(outer, inner, length, -1.0)
    section = times_complex(section, (turned[0][:, :, None], turned[1][:, :, None]))
    section = complex_einsum("mb,kbc->kmc", dft_table(inner, -1.0), section)
    return tuple((part.reshape(length, count) for part in section))


def rows_inverse(field):
    length, count = field[0].shape
    outer, inner = factor_pair(length)
    shaped = tuple((part.reshape(outer, inner, count) for part in field))
    section = complex_einsum("mb,kmc->kbc", dft_table(inner, 1.0), shaped)
    turned = twiddle_table(outer, inner, length, 1.0)
    section = times_complex(section, (turned[0][:, :, None], turned[1][:, :, None]))
    section = complex_einsum("ka,kbc->abc", dft_table(outer, 1.0), section)
    return tuple((part.reshape(length, count) for part in section))


def rotate(part, step, count):
    step %= count
    if step == 0:
        return part
    if 4 * step == count:
        return (-part[1], part[0])
    if 2 * step == count:
        return (-part[0], -part[1])
    if 4 * step == 3 * count:
        return (part[1], -part[0])
    cosine = math.cos(2.0 * math.pi * step / count)
    sine = math.sin(2.0 * math.pi * step / count)
    return (part[0] * cosine - part[1] * sine, part[0] * sine + part[1] * cosine)


def fft_slabs(parts, orient):
    count = len(parts)
    if count == 1:
        return list(parts)
    even = fft_slabs(parts[0::2], orient)
    odd = fft_slabs(parts[1::2], orient)
    half = count // 2
    out = [None] * count
    for k in range(half):
        turned = rotate(odd[k], orient * k, count)
        out[k] = (even[k][0] + turned[0], even[k][1] + turned[1])
        out[k + half] = (even[k][0] - turned[0], even[k][1] - turned[1])
    return out


def split_bf16(value):
    spread = value * 65537.0
    high = spread - (spread - value)
    return high.astype(jnp.bfloat16), (value - high).astype(jnp.bfloat16)


def split_table(table):
    table = np.asarray(table, np.float32)
    high = table.astype(ml_dtypes.bfloat16)
    low = (table - high.astype(np.float32)).astype(ml_dtypes.bfloat16)
    return high, low


def dft_numpy(length, orient):
    position = np.arange(length)
    angle = orient * 2.0 * np.pi * (position[:, None] * position[None, :] % length) / length
    return np.cos(angle), np.sin(angle)


def stacked_matmul(stacked, real, imag):
    size = real.shape[1]
    rows = stacked.shape[0] // 2
    high, low = split_bf16(jnp.concatenate([real, imag], axis=1))
    both = jnp.concatenate([high, low, high], axis=0)
    prod = jnp.dot(stacked, both, preferred_element_type=jnp.float32)
    return (
        prod[:rows, :size] - prod[rows:, size:],
        prod[:rows, size:] + prod[rows:, :size],
    )


def rows_kernel(*refs):
    x_refs = refs[:-4]
    p_ref, w_ref, tw_ref, o_ref = refs[-4:]
    outer = tw_ref.shape[1]
    inner = tw_ref.shape[2]
    count = sum(ref.shape[2] for ref in x_refs)

    def place(a):
        return (a * inner) // count, slice((a * inner) % count, (a * inner) % count + inner)

    sizes = [ref.shape[2] for ref in x_refs]
    starts = [sum(sizes[:i]) for i in range(len(sizes))]
    slabs = []
    for a in range(outer):
        origin = (a * inner) // count
        low = (a * inner) % count
        pieces = []
        for ref, start, size in zip(x_refs, starts, sizes):
            top = min(low + inner, start + size)
            bottom = max(low, start)
            if top > bottom:
                pieces.append((ref[origin, 0, bottom - start:top - start, :], ref[origin, 1, bottom - start:top - start, :]))
        if len(pieces) == 1:
            slabs.append(pieces[0])
        else:
            slabs.append((
                jnp.concatenate([p[0] for p in pieces], axis=0),
                jnp.concatenate([p[1] for p in pieces], axis=0),
            ))
    spec = fft_slabs(slabs, -1)
    forward = w_ref[0]
    backward = w_ref[1]
    outs = []
    for k in range(outer):
        zr, zi = spec[k]
        tr = tw_ref[0, k]
        ti = tw_ref[1, k]
        zr, zi = zr * tr - zi * ti, zr * ti + zi * tr
        yr, yi = stacked_matmul(forward, zr, zi)
        pr = p_ref[0, k * inner:(k + 1) * inner, :]
        pi = p_ref[1, k * inner:(k + 1) * inner, :]
        yr, yi = yr * pr - yi * pi, yr * pi + yi * pr
        sr, si = stacked_matmul(backward, yr, yi)
        outs.append((sr * tr + si * ti, si * tr - sr * ti))
    res = fft_slabs(outs, 1)
    for a in range(outer):
        origin, rows = place(a)
        o_ref[origin, 0, rows, :] = res[a][0]
        o_ref[origin, 1, rows, :] = res[a][1]


def rows_shift(turned, factor):
    groups, _, _, width = turned[0].shape
    count = sum(piece.shape[2] for piece in turned)
    length = groups * count
    outer, inner = factor_pair(length)
    block = min(width, 128)
    real, imag = dft_numpy(inner, -1.0)
    turn = twiddle_table(outer, inner, length, -1.0)
    turn = jnp.stack(turn)[..., None]
    parts = [split_table(np.concatenate([real, sign * imag], axis=0)) for sign in (1.0, -1.0)]
    table = jnp.asarray(np.stack([np.concatenate([hi, hi, lo], axis=1) for hi, lo in parts]))
    return pl.pallas_call(
        rows_kernel,
        grid=(width // block,),
        in_specs=[pl.BlockSpec((groups, 2, piece.shape[2], block), lambda j: (0, 0, 0, j)) for piece in turned] + [
            pl.BlockSpec((2, length, block), lambda j: (0, 0, j)),
            pl.BlockSpec((2, 2 * inner, 3 * inner), lambda j: (0, 0, 0)),
            pl.BlockSpec((2, outer, inner, 1), lambda j: (0, 0, 0, 0)),
        ],
        out_specs=pl.BlockSpec((groups, 2, count, block), lambda j: (0, 0, 0, j)),
        out_shape=jax.ShapeDtypeStruct((groups, 2, count, width), jnp.float32),
    )(*turned, factor, table, turn)


def prelens_kernel(base_ref, wave_ref, src_ref, slow_ref, refl_ref, o_ref):
    base = base_ref[0, 0]
    gain = OMEGA * OMEGA * refl_ref[0]
    real_in = wave_ref[0, 0].astype(jnp.float32) + gain * src_ref[0, 0].astype(jnp.float32)
    imag_in = wave_ref[0, 1].astype(jnp.float32) + gain * src_ref[0, 1].astype(jnp.float32)
    angle = -OMEGA * (slow_ref[0] - base) * DEPTH_STEP
    cosine = jnp.cos(angle)
    sine = jnp.sin(angle)
    o_ref[0] = real_in * cosine - imag_in * sine
    o_ref[1] = real_in * sine + imag_in * cosine
    o_ref[2] = cosine
    o_ref[3] = sine


def prelens(wavefield, source, slowness, reflectivity, base):
    _, _, count, length = wavefield.shape
    block = min(count, 256)
    quad = lambda i: (0, 0, i, 0)
    flat = lambda i: (0, i, 0)
    return pl.pallas_call(
        prelens_kernel,
        grid=(count // block,),
        in_specs=[
            pl.BlockSpec(memory_space=pltpu.SMEM),
            pl.BlockSpec((1, 2, block, length), quad),
            pl.BlockSpec((1, 2, block, length), quad),
            pl.BlockSpec((1, block, length), flat),
            pl.BlockSpec((1, block, length), flat),
        ],
        out_specs=pl.BlockSpec((4, block, length), flat),
        out_shape=jax.ShapeDtypeStruct((4, count, length), jnp.float32),
    )(base.reshape(1, 1), wavefield, source, slowness, reflectivity)


def lanes_forward_kernel(pre_ref, hand_ref, w_ref, tw_ref, o_ref):
    outer = tw_ref.shape[1]
    inner = tw_ref.shape[2]
    hand_real = hand_ref[0].astype(jnp.float32)
    hand_imag = hand_ref[1].astype(jnp.float32)
    cosine = pre_ref[2]
    sine = pre_ref[3]
    lensed_real = pre_ref[0] + (hand_real * cosine - hand_imag * sine)
    lensed_imag = pre_ref[1] + (hand_real * sine + hand_imag * cosine)
    slabs = [
        (lensed_real[:, a * inner:(a + 1) * inner], lensed_imag[:, a * inner:(a + 1) * inner])
        for a in range(outer)
    ]
    spec = fft_slabs(slabs, -1)
    both = w_ref[0]
    count = lensed_real.shape[0]
    for k in range(outer):
        zr, zi = spec[k]
        tr = tw_ref[0, k:k + 1, :]
        ti = tw_ref[1, k:k + 1, :]
        zr, zi = zr * tr - zi * ti, zr * ti + zi * tr
        high, low = split_bf16(jnp.concatenate([zr, zi], axis=0))
        prod = jnp.dot(jnp.concatenate([high, low, high], axis=1), both, preferred_element_type=jnp.float32)
        width = o_ref.shape[3]
        dest = (k * inner) // width
        lanes = slice((k * inner) % width, (k * inner) % width + inner)
        o_ref[dest, 0, :, lanes] = prod[:count, :inner] - prod[count:, inner:]
        o_ref[dest, 1, :, lanes] = prod[:count, inner:] + prod[count:, :inner]


def lanes_inverse_kernel(x_ref, src_ref, w_ref, tw_ref, ext_ref, img_ref):
    outer = tw_ref.shape[1]
    inner = tw_ref.shape[2]
    count = x_ref.shape[2]
    both = w_ref[1]
    outs = []
    for k in range(outer):
        width = x_ref.shape[3]
        origin = (k * inner) // width
        lanes = slice((k * inner) % width, (k * inner) % width + inner)
        yr = x_ref[origin, 0, :, lanes]
        yi = x_ref[origin, 1, :, lanes]
        high, low = split_bf16(jnp.concatenate([yr, yi], axis=0))
        prod = jnp.dot(jnp.concatenate([high, low, high], axis=1), both, preferred_element_type=jnp.float32)
        sr = prod[:count, :inner] - prod[count:, inner:]
        si = prod[:count, inner:] + prod[count:, :inner]
        tr = tw_ref[0, k:k + 1, :]
        ti = tw_ref[1, k:k + 1, :]
        outs.append((sr * tr + si * ti, si * tr - sr * ti))
    res = fft_slabs(outs, 1)
    for a in range(outer):
        out_real, out_imag = res[a]
        lanes = slice(a * inner, (a + 1) * inner)
        ext_ref[0, 0, :, lanes] = out_real.astype(ext_ref.dtype)
        ext_ref[0, 1, :, lanes] = out_imag.astype(ext_ref.dtype)
        img_ref[0, :, lanes] = (
            src_ref[0, 0, :, lanes].astype(jnp.float32) * out_real
            + src_ref[0, 1, :, lanes].astype(jnp.float32) * out_imag
        )


def lane_tables(length):
    outer, inner = factor_pair(length)
    real, imag = dft_numpy(inner, -1.0)
    parts = [split_table(np.concatenate([real, sign * imag], axis=1)) for sign in (1.0, -1.0)]
    table = jnp.asarray(np.stack([np.concatenate([hi, hi, lo], axis=0) for hi, lo in parts]))
    turn = jnp.stack(twiddle_table(outer, inner, length, -1.0))
    return outer, inner, table, turn


def lanes_forward(lensed, handed, first, step, groups):
    length = lensed.shape[2]
    outer, inner, table, turn = lane_tables(length)
    block = 64 if step % 64 == 0 and first % 64 == 0 else min(step, 32)
    offset = first // block
    return pl.pallas_call(
        lanes_forward_kernel,
        grid=(step // block,),
        in_specs=[
            pl.BlockSpec((4, block, length), lambda i: (0, offset + i, 0)),
            pl.BlockSpec((2, block, length), lambda i: (0, i, 0)),
            pl.BlockSpec((2, 3 * inner, 2 * inner), lambda i: (0, 0, 0)),
            pl.BlockSpec((2, outer, inner), lambda i: (0, 0, 0)),
        ],
        out_specs=pl.BlockSpec((groups, 2, block, length // groups), lambda i: (0, 0, i, 0)),
        out_shape=jax.ShapeDtypeStruct((groups, 2, step, length // groups), jnp.float32),
    )(lensed, handed, table, turn)


def lanes_inverse(back, source):
    groups, _, step, width = back.shape
    length = groups * width
    outer, inner, table, turn = lane_tables(length)
    block = min(step, 128)
    return pl.pallas_call(
        lanes_inverse_kernel,
        grid=(step // block,),
        in_specs=[
            pl.BlockSpec((groups, 2, block, width), lambda i: (0, 0, i, 0)),
            pl.BlockSpec((1, 2, block, length), lambda i: (0, 0, i, 0)),
            pl.BlockSpec((2, 3 * inner, 2 * inner), lambda i: (0, 0, 0)),
            pl.BlockSpec((2, outer, inner), lambda i: (0, 0, 0)),
        ],
        out_specs=[
            pl.BlockSpec((1, 2, block, length), lambda i: (0, 0, i, 0)),
            pl.BlockSpec((1, block, length), lambda i: (0, i, 0)),
        ],
        out_shape=[
            jax.ShapeDtypeStruct((1, 2, step, length), jnp.bfloat16),
            jax.ShapeDtypeStruct((1, step, length), jnp.float32),
        ],
    )(back, source, table, turn)


def signed_freq(index, length):
    signed = jnp.where(index < length // 2, index, index - length)
    return signed.astype(jnp.float32) * (2.0 * math.pi / length)


def permuted_freq(position, length):
    outer, inner = factor_pair(length)
    index = position // inner + outer * (position % inner)
    return signed_freq(index, length)


def propagator(freq_row, freq_col, base, scale):
    kz_square = (OMEGA * base) ** 2 - freq_row * freq_row - freq_col * freq_col
    root = jnp.sqrt(jnp.abs(kz_square))
    upward = kz_square >= 0.0
    real_part = jnp.where(upward, jnp.cos(root * DEPTH_STEP), jnp.exp(-root * DEPTH_STEP))
    imag_part = jnp.where(upward, -jnp.sin(root * DEPTH_STEP), jnp.zeros_like(root))
    return (real_part * scale, imag_part * scale)


def lens_rows(wave, handed, source, slow, refl, base):
    wave = wave.astype(jnp.float32)
    handed = handed.astype(jnp.float32)
    source = source.astype(jnp.float32)
    real_in = wave[0] + handed[0] + OMEGA * OMEGA * refl * source[0]
    imag_in = wave[1] + handed[1] + OMEGA * OMEGA * refl * source[1]
    angle = -OMEGA * (slow - base) * DEPTH_STEP
    cosine = jnp.cos(angle)
    sine = jnp.sin(angle)
    return (real_in * cosine - imag_in * sine, real_in * sine + imag_in * cosine)


def body(wavefield, boundary, source, slowness, reflectivity, ref_slowness):
    count = wavefield.shape[2]
    columns = wavefield.shape[3]
    eighth = count // 8
    if count % 8 == 0 and eighth % 8 == 0:
        bounds = [0, 4 * eighth, count]
    else:
        bounds = [0, count]
    groups = lax.axis_size("gx")
    device = lax.axis_index("gx")
    total_rows = count * groups
    width = columns // groups
    scale = 1.0 / (total_rows * columns)
    base = ref_slowness[0]
    pieces = []
    lensed = prelens(wavefield, source, slowness, reflectivity, base)
    for first, last in zip(bounds[:-1], bounds[1:]):
        handed = shifted(boundary[0, :, first:last], "slab", -1)
        field = lanes_forward(lensed, handed, first, last - first, groups)
        pieces.append(lax.all_to_all(field, "gx", split_axis=0, concat_axis=0, tiled=True))
    freq_row = permuted_freq(jnp.arange(total_rows, dtype=jnp.int32), total_rows)
    freq_col = permuted_freq(device * width + jnp.arange(width, dtype=jnp.int32), columns)
    factor = propagator(freq_row[:, None], freq_col[None, :], base, scale)
    spatial = rows_shift(pieces, jnp.stack(factor))
    back = lax.all_to_all(spatial, "gx", split_axis=0, concat_axis=0, tiled=True)
    return lanes_inverse(back, source)


def solution(mesh):
    return jax.shard_map(
        body,
        mesh=mesh,
        in_specs=(
            P("slab", None, "gx", None),
            P("slab", None, "gx", None),
            P("slab", None, "gx", None),
            P("slab", "gx", None),
            P("slab", "gx", None),
            P("slab"),
        ),
        out_specs=(P("slab", None, "gx", None), P("slab", "gx", None)),
        check_vma=False,
    )
```
